128 devices in a mesh: head: 4 (over y), tile: 32 (over x, z, core).
Axes of the slice: x: 4, y: 4, z: 4, core: 2. Of those that a mesh axis runs over, the one named last changes fastest.
Arguments:
- hidden: bfloat16 [32, 384, 1536], P(None, ('head', 'tile')), may hold values from -6 to 6
- latent: float32 [32, 384, 64], P(None, ('head', 'tile')), may hold values from -6 to 6
- cell_map: int32 [32, 384], P(None, ('head', 'tile')), may hold values from 0 to 383, each once within a row
- text_lengths: int32 [32], P('tile'), may hold values from 64 to 512, as said below
- block_modulation: float32 [32, 3, 1536], replicated, may hold values from -3 to 3
- head_modulation: float32 [32, 2, 1536], replicated, may hold values from -3 to 3
- step_sizes: float32 [32], replicated, may hold values from -0.5 to -0.1
- w_qkv: bfloat16 [1536, 4608], replicated, may hold values from -0.15625 to 0.15625
- self_q_gain: float32 [1536], replicated, may hold values from 0.5 to 2
- self_k_gain: float32 [1536], replicated, may hold values from 0.5 to 2
- w_out: bfloat16 [1536, 1536], replicated, may hold values from -0.15625 to 0.15625
- cross_gain: float32 [1536], replicated, may hold values from 0.1 to 1.9
- cross_wq: bfloat16 [1536, 1536], P(None, 'head'), may hold values from -0.15625 to 0.15625
- cross_q_gain: float32 [1536], P('head'), may hold values from 0.5 to 2
- text_keys: bfloat16 [32, 512, 1536], P('tile', None, 'head'), may hold values from -2.5 to 2.5
- text_values: bfloat16 [32, 512, 1536], P('tile', None, 'head'), may hold values from -4 to 4
- cross_wo: bfloat16 [1536, 1536], P('head'), may hold values from -0.15625 to 0.15625
- head_w: bfloat16 [1536, 64], replicated, may hold values from -0.15625 to 0.15625
Outputs:
- hidden_next: bfloat16 [32, 384, 1536], P(None, ('head', 'tile'))
- latent_next: float32 [32, 384, 64], P(None, ('head', 'tile'))
The draws below stay inside these ranges and needn't reach their ends.
Inputs may be any that keep to these rules, and one draw needn't show every extreme that they name: Each row cell_map[v] names every cell of video v once. Text positions from text_lengths[v] on are padding of video v.
All inputs are finite; a program needn't handle non-finite values.
Results may differ from the reference program's by a relative error of at most 0.007.
Values may be sent and summed in bfloat16 or wider, within the bound.
No kernel may reach another device: no remote copies, remote signals or barrier semaphores. Data moves between devices by JAX's collectives and lax.ppermute only.
A program may use at most 128 MiB of HBM per device.

```python
import math
import jax
import jax.numpy as jnp
from jax import lax

D = 1536
HEADS = 12
HEAD_DIM = 128
TEXT = 512
OUT_CH = 64
GRID_H = 24
GRID_W = 8
VIDEO_TOK = 384
VIDEOS = 32


def draw_text_lengths(key, part):
    lengths_drawn = jax.random.randint(jax.random.fold_in(key, 11), (VIDEOS,), TEXT // 8, TEXT + 1)
    chosen = jax.random.randint(jax.random.fold_in(key, 12), (), 0, VIDEOS)
    places = jnp.arange(VIDEOS)
    lengths_drawn = jnp.where(places == chosen, TEXT, lengths_drawn)
    lengths_drawn = jnp.where(places == (chosen + 1) % VIDEOS, TEXT // 8, lengths_drawn)
    return lengths_drawn.astype(jnp.int32)


def block_levels(stream_key, dims, cuts, smallest, largest):
    level = 1.0
    for axis_at, parts in cuts:
        steps = jax.random.uniform(jax.random.fold_in(jax.random.fold_in(stream_key, 6), axis_at), (parts,), jnp.float32, smallest / len(cuts), largest / len(cuts))
        level = level * jnp.repeat(jnp.exp(steps), dims[axis_at] // parts).reshape((-1,) + (1,) * (len(dims) - 1 - axis_at))
    return level


def noise(stream_key, extent, deviation, most, cuts=(), kind=jnp.bfloat16):
    result = deviation * jax.random.normal(stream_key, extent, jnp.float32)
    if cuts:
        result = result * block_levels(stream_key, extent, cuts, -0.22, 0.18)
    return jnp.clip(result, -most, most).astype(kind)


def setup_inputs(seed: int = 0) -> dict:
    key_list = jax.random.split(jax.random.key(seed), 19)
    return {
        "hidden": noise(key_list[0], (VIDEOS, VIDEO_TOK, D), 1.0, 6.0, ((1, 128),)),
        "latent": noise(key_list[1], (VIDEOS, VIDEO_TOK, OUT_CH), 1.0, 6.0, ((1, 128),), jnp.float32),
        "cell_map": jax.vmap(lambda own: jax.random.permutation(own, VIDEO_TOK))(jax.random.split(key_list[2], VIDEOS)).reshape((VIDEOS, VIDEO_TOK)).astype(jnp.int32),
        "text_lengths": draw_text_lengths(jax.random.fold_in(key_list[18], 71), 0),
        "block_modulation": noise(key_list[4], (VIDEOS, 3, D), 0.7, 3.0, (), jnp.float32),
        "head_modulation": noise(key_list[5], (VIDEOS, 2, D), 0.7, 3.0, (), jnp.float32),
        "step_sizes": jnp.clip(jax.random.uniform(key_list[6], (VIDEOS,), jnp.float32, -0.5, -0.1), -0.5, -0.1),
        "w_qkv": noise(key_list[7], (D, 3 * D), D ** -0.5, 0.15625),
        "self_q_gain": jnp.clip(jax.random.uniform(key_list[8], (D,), jnp.float32, 0.5, 2.0), 0.5, 2.0),
        "self_k_gain": jnp.clip(jax.random.uniform(key_list[9], (D,), jnp.float32, 0.5, 2.0), 0.5, 2.0),
        "w_out": noise(key_list[10], (D, D), D ** -0.5, 0.15625),
        "cross_gain": jnp.clip(1.0 + 0.18 * jax.random.normal(key_list[11], (D,), jnp.float32), 0.1, 1.9),
        "cross_wq": noise(key_list[12], (D, D), D ** -0.5, 0.15625, ((1, 4),)),
        "cross_q_gain": jnp.clip(0.5 + 1.5 * jax.random.uniform(key_list[13], (D,), jnp.float32) ** block_levels(key_list[13], (D,), ((0, 4),), -0.2, 0.2), 0.5, 2.0),
        "text_keys": noise(key_list[14], (VIDEOS, TEXT, D), 1.0, 2.5, ((0, 32), (2, 4))),
        "text_values": noise(key_list[15], (VIDEOS, TEXT, D), 1.0, 4.0, ((0, 32), (2, 4))),
        "cross_wo": noise(key_list[16], (D, D), D ** -0.5, 0.15625, ((0, 4),)),
        "head_w": noise(key_list[17], (D, OUT_CH), D ** -0.5, 0.15625),
    }


EPSILON = 1e-06

def rounded(inputs):
    return lax.optimization_barrier(inputs.astype(jnp.bfloat16))

def layer_norm(inputs):
    average = lax.optimization_barrier(jnp.mean(inputs, axis=-1, keepdims=True))
    centred = inputs - average
    variance = lax.optimization_barrier(jnp.mean(centred * centred, axis=-1, keepdims=True))
    return centred * lax.rsqrt(variance + EPSILON)

def head_norm(inputs, gain_table):
    mean_square = lax.optimization_barrier(jnp.mean(inputs * inputs, axis=-1, keepdims=True))
    return inputs * lax.rsqrt(mean_square + EPSILON) * gain_table

def frequencies(pair_count):
    return jnp.power(10000.0, -jnp.arange(pair_count, dtype=jnp.float32) / pair_count)

def rope_angles(cell_ids):
    sixth_part = HEAD_DIM // 6
    time_pairs = HEAD_DIM // 2 - 2 * sixth_part
    plane_cells = GRID_H * GRID_W
    frame_index = (cell_ids // plane_cells).astype(jnp.float32)
    row_index = (cell_ids // GRID_W % GRID_H).astype(jnp.float32)
    column = (cell_ids % GRID_W).astype(jnp.float32)
    return jnp.concatenate([frame_index[..., None] * frequencies(time_pairs), row_index[..., None] * frequencies(sixth_part), column[..., None] * frequencies(sixth_part)], axis=-1)

def rotate(inputs, angles):
    half_dim = inputs.shape[-1] // 2
    cosine = jnp.cos(angles)[..., None, :]
    sine_part = jnp.sin(angles)[..., None, :]
    lower_half = inputs[..., :half_dim]
    upper_half = inputs[..., half_dim:]
    return jnp.concatenate([lower_half * cosine - upper_half * sine_part, lower_half * sine_part + upper_half * cosine], axis=-1)

def attention(queries, keys_all, values_all, live_mask):
    factor = 1.0 / math.sqrt(HEAD_DIM)
    scores = jnp.einsum('qhd,khd->hqk', queries.astype(jnp.float32), keys_all.astype(jnp.float32)) * factor
    weights = jnp.exp(scores) * live_mask
    totals = lax.optimization_barrier(jnp.sum(weights, axis=-1))
    mixture = jnp.einsum('hqk,khd->qhd', rounded(weights).astype(jnp.float32), values_all.astype(jnp.float32))
    return mixture / jnp.transpose(totals)[:, :, None]

def reference(hidden, latent, cell_map, text_lengths, block_modulation, head_modulation, step_sizes, w_qkv, self_q_gain, self_k_gain, w_out, cross_gain, cross_wq, cross_q_gain, text_keys, text_values, cross_wo, head_w):

    def one_video(video_items):
        hidden_item, latent_item, cells_item, length_item, block_item, head_item, step_item, keys_item, values_item = video_items
        stream = hidden_item.astype(jnp.float32)
        block_in = rounded(layer_norm(stream) * (1.0 + block_item[1]) + block_item[0])
        projected = jnp.dot(block_in, w_qkv, preferred_element_type=jnp.float32).reshape(VIDEO_TOK, 3, HEADS, HEAD_DIM)
        angles = rope_angles(cells_item)
        self_queries = rounded(rotate(head_norm(projected[:, 0], self_q_gain.reshape(HEADS, HEAD_DIM)), angles))
        self_keys = rounded(rotate(head_norm(projected[:, 1], self_k_gain.reshape(HEADS, HEAD_DIM)), angles))
        self_values = rounded(projected[:, 2])
        every_key = jnp.ones((VIDEO_TOK,), jnp.float32)
        attended = rounded(attention(self_queries, self_keys, self_values, every_key)).reshape(VIDEO_TOK, D)
        self_update = jnp.dot(attended, w_out, preferred_element_type=jnp.float32)
        after_self = stream + block_item[2] * self_update
        cross_in = rounded(layer_norm(after_self) * cross_gain)
        cross_queries = jnp.dot(cross_in, cross_wq, preferred_element_type=jnp.float32).reshape(VIDEO_TOK, HEADS, HEAD_DIM)
        cross_queries = rounded(head_norm(cross_queries, cross_q_gain.reshape(HEADS, HEAD_DIM)))
        live_mask = (jnp.arange(TEXT) < length_item).astype(jnp.float32)
        cross_mixed = rounded(attention(cross_queries, keys_item.reshape(TEXT, HEADS, HEAD_DIM), values_item.reshape(TEXT, HEADS, HEAD_DIM), live_mask)).reshape(VIDEO_TOK, D)
        cross_out = rounded(jnp.dot(cross_mixed, cross_wo, preferred_element_type=jnp.float32))
        after_cross = after_self + cross_out.astype(jnp.float32)
        hidden_next = after_cross.astype(jnp.bfloat16)
        head_in = rounded(layer_norm(after_cross) * (1.0 + head_item[1]) + head_item[0])
        velocity = jnp.dot(head_in, head_w, preferred_element_type=jnp.float32)
        latent_next = latent_item + step_item * velocity
        return (hidden_next, latent_next)
    return lax.map(one_video, (hidden, latent, cell_map, text_lengths, block_modulation, head_modulation, step_sizes, text_keys, text_values))
```

```python
import math

import jax
import jax.numpy as jnp
from jax import lax
from jax.experimental import pallas as pl
from jax.experimental.pallas import tpu as pltpu
from jax.sharding import PartitionSpec as P

HEADS = 12
HEAD_DIM = 128
GRID_H = 24
GRID_W = 8


EPSILON = 1e-06


def layer_norm(inputs):
    average = jnp.mean(inputs, axis=-1, keepdims=True)
    centred = inputs - average
    variance = jnp.mean(centred * centred, axis=-1, keepdims=True)
    return centred * lax.rsqrt(variance + EPSILON)


def head_norm(inputs, gain_table):
    mean_square = jnp.mean(inputs * inputs, axis=-1, keepdims=True)
    return inputs * lax.rsqrt(mean_square + EPSILON) * gain_table


def frequencies(pair_count):
    return jnp.power(10000.0, -jnp.arange(pair_count, dtype=jnp.float32) / pair_count)


def rope_angles(cell_ids):
    sixth_part = HEAD_DIM // 6
    time_pairs = HEAD_DIM // 2 - 2 * sixth_part
    plane_cells = GRID_H * GRID_W
    frame_index = (cell_ids // plane_cells).astype(jnp.float32)
    row_index = (cell_ids // GRID_W % GRID_H).astype(jnp.float32)
    column = (cell_ids % GRID_W).astype(jnp.float32)
    return jnp.concatenate(
        [
            frame_index[..., None] * frequencies(time_pairs),
            row_index[..., None] * frequencies(sixth_part),
            column[..., None] * frequencies(sixth_part),
        ],
        axis=-1,
    )


def rotate(inputs, angles):
    half_dim = inputs.shape[-1] // 2
    cosine = jnp.cos(angles)[..., None, :]
    sine_part = jnp.sin(angles)[..., None, :]
    lower_half = inputs[..., :half_dim]
    upper_half = inputs[..., half_dim:]
    return jnp.concatenate(
        [
            lower_half * cosine - upper_half * sine_part,
            lower_half * sine_part + upper_half * cosine,
        ],
        axis=-1,
    )


def attend_self(queries, keys_own, values_own):
    factor = 1.0 / math.sqrt(queries.shape[-1])
    token_total = queries.shape[0]

    def one_block(block_queries):
        scores = (
            jnp.einsum("qhd,khd->hqk", block_queries, keys_own, preferred_element_type=jnp.float32)
            * factor
        )
        weights = jnp.exp(scores)
        totals = jnp.sum(weights, axis=-1)
        mixture = jnp.einsum(
            "hqk,khd->qhd",
            weights.astype(jnp.bfloat16),
            values_own,
            preferred_element_type=jnp.float32,
        )
        return (mixture / jnp.transpose(totals)[:, :, None]).astype(jnp.bfloat16)

    blocked = queries.reshape((token_total // token_total, token_total) + queries.shape[1:])
    return lax.map(one_block, blocked).reshape(queries.shape)


def attend_text(queries, keys_own, values_own, length):
    factor = 1.0 / math.sqrt(queries.shape[-1])
    live_mask = (jnp.arange(keys_own.shape[0]) < length).astype(jnp.float32)
    scores = (
        jnp.einsum("qhd,khd->hqk", queries, keys_own, preferred_element_type=jnp.float32) * factor
    )
    weights = jnp.exp(scores) * live_mask
    totals = jnp.sum(weights, axis=-1)
    mixture = jnp.einsum(
        "hqk,khd->qhd", weights.astype(jnp.bfloat16), values_own, preferred_element_type=jnp.float32
    )
    return (mixture / jnp.transpose(totals)[:, :, None]).astype(jnp.bfloat16)


def _matmul_kernel(x_ref, w_ref, o_ref):
    o_ref[...] = jnp.dot(x_ref[...], w_ref[...], preferred_element_type=jnp.float32)


def stream_matmul(rows, weight, column_block):
    row_count, inner = rows.shape
    columns = weight.shape[1]
    return pl.pallas_call(
        _matmul_kernel,
        grid=(columns // column_block,),
        in_specs=[
            pl.BlockSpec((row_count, inner), lambda j: (0, 0)),
            pl.BlockSpec((inner, column_block), lambda j: (0, j)),
        ],
        out_specs=pl.BlockSpec((row_count, column_block), lambda j: (0, j)),
        out_shape=jax.ShapeDtypeStruct((row_count, columns), jnp.float32),
        cost_estimate=pl.CostEstimate(
            flops=2 * row_count * inner * columns,
            bytes_accessed=2 * inner * columns + 2 * row_count * inner + 4 * row_count * columns,
            transcendentals=0,
        ),
    )(rows, weight)


def pack_projected(block_in, cell_map, w_qkv, self_q_gain, self_k_gain, head_count):
    videos, per_video, model_width = block_in.shape
    projected = stream_matmul(block_in.reshape(-1, model_width), w_qkv, 768)
    projected = projected.reshape(videos, per_video, 3, HEADS, HEAD_DIM)
    angles = rope_angles(cell_map)
    queries = rotate(
        head_norm(projected[:, :, 0], self_q_gain.reshape(HEADS, HEAD_DIM)), angles
    ).astype(jnp.bfloat16)
    keys_all = rotate(
        head_norm(projected[:, :, 1], self_k_gain.reshape(HEADS, HEAD_DIM)), angles
    ).astype(jnp.bfloat16)
    values_all = projected[:, :, 2].astype(jnp.bfloat16)
    packed = jnp.stack([queries, keys_all, values_all], axis=2)
    group_width = model_width // head_count
    packed = packed.reshape(videos, per_video, 3, head_count, group_width).transpose(3, 0, 1, 2, 4)
    return packed.reshape(head_count, videos, per_video, 3 * group_width)


def local(
    hidden,
    latent,
    cell_map,
    text_lengths,
    block_modulation,
    head_modulation,
    step_sizes,
    w_qkv,
    self_q_gain,
    self_k_gain,
    w_out,
    cross_gain,
    cross_wq,
    cross_q_gain,
    text_keys,
    text_values,
    cross_wo,
    head_w,
):
    head_count = lax.axis_size("head")
    tile_count = lax.axis_size("tile")
    videos, per_video, model_width = hidden.shape
    group_heads = HEADS // head_count
    group_width = group_heads * HEAD_DIM
    stream = hidden.astype(jnp.float32)
    block_shift = block_modulation[:, 0][:, None, :]
    block_scale = block_modulation[:, 1][:, None, :]
    block_gate = block_modulation[:, 2][:, None, :]
    block_in = (layer_norm(stream) * (1.0 + block_scale) + block_shift).astype(jnp.bfloat16)
    packed = pack_projected(block_in, cell_map, w_qkv, self_q_gain, self_k_gain, head_count)
    arrived = lax.all_to_all(
        packed.reshape(head_count * videos, per_video, 3 * group_width),
        ("head", "tile"),
        split_axis=0,
        concat_axis=0,
        tiled=True,
    )
    arrived = arrived.reshape(-1, 3, group_heads, HEAD_DIM)
    own_queries = arrived[:, 0]
    own_keys = arrived[:, 1]
    own_values = arrived[:, 2]
    own_mixture = attend_self(own_queries, own_keys, own_values)
    returned = lax.all_to_all(
        own_mixture.reshape(head_count * tile_count, per_video, group_width),
        ("head", "tile"),
        split_axis=0,
        concat_axis=0,
        tiled=True,
    )
    attended = (
        returned.reshape(head_count, videos, per_video, group_width)
        .transpose(1, 2, 0, 3)
        .reshape(videos * per_video, model_width)
    )
    self_update = jnp.dot(attended, w_out, preferred_element_type=jnp.float32).reshape(
        videos, per_video, model_width
    )
    after_self = stream + block_gate * self_update
    cross_in = (layer_norm(after_self) * cross_gain).astype(jnp.bfloat16)
    copies = jnp.broadcast_to(cross_in[None], (head_count,) + cross_in.shape).reshape(
        head_count * videos, per_video, model_width
    )
    owner_cross = lax.all_to_all(copies, ("head", "tile"), split_axis=0, concat_axis=0, tiled=True)
    owner_cross = owner_cross.reshape(-1, model_width)
    cross_queries = jnp.dot(owner_cross, cross_wq, preferred_element_type=jnp.float32).reshape(
        -1, group_heads, HEAD_DIM
    )
    cross_queries = head_norm(cross_queries, cross_q_gain.reshape(group_heads, HEAD_DIM)).astype(
        jnp.bfloat16
    )
    own_text_keys = text_keys[0].reshape(-1, group_heads, HEAD_DIM)
    own_text_values = text_values[0].reshape(-1, group_heads, HEAD_DIM)
    cross_mixture = attend_text(
        cross_queries, own_text_keys, own_text_values, text_lengths[0]
    ).reshape(-1, group_width)
    summed = lax.psum_scatter(
        jnp.dot(cross_mixture, cross_wo, preferred_element_type=jnp.float32).astype(jnp.bfloat16),
        "head",
        scatter_dimension=0,
        tiled=True,
    )
    cross_out = summed.reshape(tile_count, per_video, model_width)
    returned_cross = lax.all_to_all(cross_out, "tile", split_axis=0, concat_axis=0, tiled=True)
    after_cross = after_self + returned_cross.astype(jnp.float32)
    hidden_next = after_cross.astype(jnp.bfloat16)
    head_shift = head_modulation[:, 0][:, None, :]
    head_scale = head_modulation[:, 1][:, None, :]
    head_in = (layer_norm(after_cross) * (1.0 + head_scale) + head_shift).astype(jnp.bfloat16)
    velocity = jnp.dot(
        head_in.reshape(-1, model_width), head_w, preferred_element_type=jnp.float32
    ).reshape(videos, per_video, -1)
    latent_next = latent + step_sizes[:, None, None] * velocity
    return (hidden_next, latent_next)


def solution(mesh):
    return jax.shard_map(
        local,
        mesh=mesh,
        in_specs=(
            P(None, ("head", "tile"), None),
            P(None, ("head", "tile"), None),
            P(None, ("head", "tile")),
            P("tile"),
            P(),
            P(),
            P(),
            P(),
            P(),
            P(),
            P(),
            P(),
            P(None, "head"),
            P("head"),
            P("tile", None, "head"),
            P("tile", None, "head"),
            P("head", None),
            P(),
        ),
        out_specs=(P(None, ("head", "tile"), None), P(None, ("head", "tile"), None)),
        check_vma=False,
    )
```

```python
import math

import jax
import jax.numpy as jnp
from jax import lax
from jax.experimental import pallas as pl
from jax.experimental.pallas import tpu as pltpu
from jax.sharding import PartitionSpec as P

HEADS = 12
HEAD_DIM = 128
GRID_H = 24
GRID_W = 8


EPSILON = 1e-06


def layer_norm(inputs):
    average = jnp.mean(inputs, axis=-1, keepdims=True)
    centred = inputs - average
    variance = jnp.mean(centred * centred, axis=-1, keepdims=True)
    return centred * lax.rsqrt(variance + EPSILON)


def head_norm(inputs, gain_table):
    mean_square = jnp.mean(inputs * inputs, axis=-1, keepdims=True)
    return inputs * lax.rsqrt(mean_square + EPSILON) * gain_table


def frequencies(pair_count):
    return jnp.power(10000.0, -jnp.arange(pair_count, dtype=jnp.float32) / pair_count)


def rope_angles(cell_ids):
    sixth_part = HEAD_DIM // 6
    time_pairs = HEAD_DIM // 2 - 2 * sixth_part
    plane_cells = GRID_H * GRID_W
    frame_index = (cell_ids // plane_cells).astype(jnp.float32)
    row_index = (cell_ids // GRID_W % GRID_H).astype(jnp.float32)
    column = (cell_ids % GRID_W).astype(jnp.float32)
    return jnp.concatenate(
        [
            frame_index[..., None] * frequencies(time_pairs),
            row_index[..., None] * frequencies(sixth_part),
            column[..., None] * frequencies(sixth_part),
        ],
        axis=-1,
    )


def rotate(inputs, angles):
    half_dim = inputs.shape[-1] // 2
    cosine = jnp.cos(angles)[..., None, :]
    sine_part = jnp.sin(angles)[..., None, :]
    lower_half = inputs[..., :half_dim]
    upper_half = inputs[..., half_dim:]
    return jnp.concatenate(
        [
            lower_half * cosine - upper_half * sine_part,
            lower_half * sine_part + upper_half * cosine,
        ],
        axis=-1,
    )


def attend_self(queries, keys_own, values_own):
    factor = 1.0 / math.sqrt(queries.shape[-1])
    token_total = queries.shape[0]

    def one_block(block_queries):
        scores = (
            jnp.einsum("qhd,khd->hqk", block_queries, keys_own, preferred_element_type=jnp.float32)
            * factor
        )
        weights = jnp.exp(scores)
        totals = jnp.sum(weights, axis=-1)
        mixture = jnp.einsum(
            "hqk,khd->qhd",
            weights.astype(jnp.bfloat16),
            values_own,
            preferred_element_type=jnp.float32,
        )
        return (mixture / jnp.transpose(totals)[:, :, None]).astype(jnp.bfloat16)

    blocked = queries.reshape((token_total // token_total, token_total) + queries.shape[1:])
    return lax.map(one_block, blocked).reshape(queries.shape)


def attend_text(queries, keys_own, values_own, length):
    factor = 1.0 / math.sqrt(queries.shape[-1])
    live_mask = (jnp.arange(keys_own.shape[0]) < length).astype(jnp.float32)
    scores = (
        jnp.einsum("qhd,khd->hqk", queries, keys_own, preferred_element_type=jnp.float32) * factor
    )
    weights = jnp.exp(scores) * live_mask
    totals = jnp.sum(weights, axis=-1)
    mixture = jnp.einsum(
        "hqk,khd->qhd", weights.astype(jnp.bfloat16), values_own, preferred_element_type=jnp.float32
    )
    return (mixture / jnp.transpose(totals)[:, :, None]).astype(jnp.bfloat16)


def _qkv_kernel(x_ref, w_ref, cos_ref, sin_ref, gain_ref, o_ref):
    section = pl.program_id(1)
    projected = jnp.dot(x_ref[...], w_ref[...], preferred_element_type=jnp.float32)

    @pl.when(section == 2)
    def _():
        o_ref[0] = projected.astype(o_ref.dtype)

    @pl.when(section < 2)
    def _():
        gains = gain_ref[pl.ds(jnp.minimum(section, 1), 1), :]
        cosine = cos_ref[...]
        sine_signed = sin_ref[...]
        parts = []
        for head in range(projected.shape[1] // HEAD_DIM):
            lanes = slice(head * HEAD_DIM, (head + 1) * HEAD_DIM)
            piece = projected[:, lanes]
            mean_square = jnp.mean(piece * piece, axis=-1, keepdims=True)
            normed = piece * lax.rsqrt(mean_square + EPSILON) * gains[:, lanes]
            swapped = pltpu.roll(normed, HEAD_DIM // 2, 1)
            parts.append(normed * cosine + swapped * sine_signed)
        o_ref[0] = jnp.concatenate(parts, axis=-1).astype(o_ref.dtype)


def pack_projected(block_in, cell_map, w_qkv, self_q_gain, self_k_gain, head_count):
    videos, per_video, model_width = block_in.shape
    rows = block_in.reshape(-1, model_width)
    token_total = rows.shape[0]
    group_width = model_width // head_count
    angles = rope_angles(cell_map).reshape(token_total, HEAD_DIM // 2)
    cosine = jnp.cos(angles)
    sine = jnp.sin(angles)
    cos_full = jnp.concatenate([cosine, cosine], axis=-1)
    sin_signed = jnp.concatenate([-sine, sine], axis=-1)
    gains = jnp.stack([self_q_gain, self_k_gain])
    packed = pl.pallas_call(
        _qkv_kernel,
        grid=(head_count, 3),
        in_specs=[
            pl.BlockSpec((token_total, model_width), lambda g, s: (0, 0)),
            pl.BlockSpec((model_width, group_width), lambda g, s: (0, s * head_count + g)),
            pl.BlockSpec((token_total, HEAD_DIM), lambda g, s: (0, 0)),
            pl.BlockSpec((token_total, HEAD_DIM), lambda g, s: (0, 0)),
            pl.BlockSpec((2, group_width), lambda g, s: (0, g)),
        ],
        out_specs=pl.BlockSpec((1, token_total, group_width), lambda g, s: (g, 0, s)),
        out_shape=jax.ShapeDtypeStruct((head_count, token_total, 3 * group_width), jnp.bfloat16),
        cost_estimate=pl.CostEstimate(
            flops=2 * token_total * model_width * 3 * model_width,
            bytes_accessed=2 * model_width * 3 * model_width + 4 * token_total * 3 * model_width,
            transcendentals=0,
        ),
    )(rows, w_qkv, cos_full, sin_signed, gains)
    return packed.reshape(head_count, videos, per_video, 3 * group_width)


def local(
    hidden,
    latent,
    cell_map,
    text_lengths,
    block_modulation,
    head_modulation,
    step_sizes,
    w_qkv,
    self_q_gain,
    self_k_gain,
    w_out,
    cross_gain,
    cross_wq,
    cross_q_gain,
    text_keys,
    text_values,
    cross_wo,
    head_w,
):
    head_count = lax.axis_size("head")
    tile_count = lax.axis_size("tile")
    videos, per_video, model_width = hidden.shape
    group_heads = HEADS // head_count
    group_width = group_heads * HEAD_DIM
    stream = hidden.astype(jnp.float32)
    block_shift = block_modulation[:, 0][:, None, :]
    block_scale = block_modulation[:, 1][:, None, :]
    block_gate = block_modulation[:, 2][:, None, :]
    block_in = (layer_norm(stream) * (1.0 + block_scale) + block_shift).astype(jnp.bfloat16)
    packed = pack_projected(block_in, cell_map, w_qkv, self_q_gain, self_k_gain, head_count)
    arrived = lax.all_to_all(
        packed.reshape(head_count * videos, per_video, 3 * group_width),
        ("head", "tile"),
        split_axis=0,
        concat_axis=0,
        tiled=True,
    )
    arrived = arrived.reshape(-1, 3, group_heads, HEAD_DIM)
    own_queries = arrived[:, 0]
    own_keys = arrived[:, 1]
    own_values = arrived[:, 2]
    own_mixture = attend_self(own_queries, own_keys, own_values)
    returned = lax.all_to_all(
        own_mixture.reshape(head_count * tile_count, per_video, group_width),
        ("head", "tile"),
        split_axis=0,
        concat_axis=0,
        tiled=True,
    )
    attended = (
        returned.reshape(head_count, videos, per_video, group_width)
        .transpose(1, 2, 0, 3)
        .reshape(videos * per_video, model_width)
    )
    self_update = jnp.dot(attended, w_out, preferred_element_type=jnp.float32).reshape(
        videos, per_video, model_width
    )
    after_self = stream + block_gate * self_update
    cross_in = (layer_norm(after_self) * cross_gain).astype(jnp.bfloat16)
    copies = jnp.broadcast_to(cross_in[None], (head_count,) + cross_in.shape).reshape(
        head_count * videos, per_video, model_width
    )
    owner_cross = lax.all_to_all(copies, ("head", "tile"), split_axis=0, concat_axis=0, tiled=True)
    owner_cross = owner_cross.reshape(-1, model_width)
    cross_queries = jnp.dot(owner_cross, cross_wq, preferred_element_type=jnp.float32).reshape(
        -1, group_heads, HEAD_DIM
    )
    cross_queries = head_norm(cross_queries, cross_q_gain.reshape(group_heads, HEAD_DIM)).astype(
        jnp.bfloat16
    )
    own_text_keys = text_keys[0].reshape(-1, group_heads, HEAD_DIM)
    own_text_values = text_values[0].reshape(-1, group_heads, HEAD_DIM)
    cross_mixture = attend_text(
        cross_queries, own_text_keys, own_text_values, text_lengths[0]
    ).reshape(-1, group_width)
    summed = lax.psum_scatter(
        jnp.dot(cross_mixture, cross_wo, preferred_element_type=jnp.float32).astype(jnp.bfloat16),
        "head",
        scatter_dimension=0,
        tiled=True,
    )
    cross_out = summed.reshape(tile_count, per_video, model_width)
    returned_cross = lax.all_to_all(cross_out, "tile", split_axis=0, concat_axis=0, tiled=True)
    after_cross = after_self + returned_cross.astype(jnp.float32)
    hidden_next = after_cross.astype(jnp.bfloat16)
    head_shift = head_modulation[:, 0][:, None, :]
    head_scale = head_modulation[:, 1][:, None, :]
    head_in = (layer_norm(after_cross) * (1.0 + head_scale) + head_shift).astype(jnp.bfloat16)
    velocity = jnp.dot(
        head_in.reshape(-1, model_width), head_w, preferred_element_type=jnp.float32
    ).reshape(videos, per_video, -1)
    latent_next = latent + step_sizes[:, None, None] * velocity
    return (hidden_next, latent_next)


def solution(mesh):
    return jax.shard_map(
        local,
        mesh=mesh,
        in_specs=(
            P(None, ("head", "tile"), None),
            P(None, ("head", "tile"), None),
            P(None, ("head", "tile")),
            P("tile"),
            P(),
            P(),
            P(),
            P(),
            P(),
            P(),
            P(),
            P(),
            P(None, "head"),
            P("head"),
            P("tile", None, "head"),
            P("tile", None, "head"),
            P("head", None),
            P(),
        ),
        out_specs=(P(None, ("head", "tile"), None), P(None, ("head", "tile"), None)),
        check_vma=False,
    )
```

```python
import math

import jax
import jax.numpy as jnp
from jax import lax
from jax.experimental import pallas as pl
from jax.experimental.pallas import tpu as pltpu
from jax.sharding import PartitionSpec as P

HEADS = 12
HEAD_DIM = 128
GRID_H = 24
GRID_W = 8


EPSILON = 1e-06


def layer_norm(inputs):
    average = jnp.mean(inputs, axis=-1, keepdims=True)
    centred = inputs - average
    variance = jnp.mean(centred * centred, axis=-1, keepdims=True)
    return centred * lax.rsqrt(variance + EPSILON)


def head_norm(inputs, gain_table):
    mean_square = jnp.mean(inputs * inputs, axis=-1, keepdims=True)
    return inputs * lax.rsqrt(mean_square + EPSILON) * gain_table


def frequencies(pair_count):
    return jnp.power(10000.0, -jnp.arange(pair_count, dtype=jnp.float32) / pair_count)


def rope_angles(cell_ids):
    sixth_part = HEAD_DIM // 6
    time_pairs = HEAD_DIM // 2 - 2 * sixth_part
    plane_cells = GRID_H * GRID_W
    frame_index = (cell_ids // plane_cells).astype(jnp.float32)
    row_index = (cell_ids // GRID_W % GRID_H).astype(jnp.float32)
    column = (cell_ids % GRID_W).astype(jnp.float32)
    return jnp.concatenate(
        [
            frame_index[..., None] * frequencies(time_pairs),
            row_index[..., None] * frequencies(sixth_part),
            column[..., None] * frequencies(sixth_part),
        ],
        axis=-1,
    )


def rotate(inputs, angles):
    half_dim = inputs.shape[-1] // 2
    cosine = jnp.cos(angles)[..., None, :]
    sine_part = jnp.sin(angles)[..., None, :]
    lower_half = inputs[..., :half_dim]
    upper_half = inputs[..., half_dim:]
    return jnp.concatenate(
        [
            lower_half * cosine - upper_half * sine_part,
            lower_half * sine_part + upper_half * cosine,
        ],
        axis=-1,
    )


def attend_self(queries, keys_own, values_own):
    factor = 1.0 / math.sqrt(queries.shape[-1])
    token_total = queries.shape[0]

    def one_block(block_queries):
        scores = (
            jnp.einsum("qhd,khd->hqk", block_queries, keys_own, preferred_element_type=jnp.float32)
            * factor
        )
        weights = jnp.exp(scores)
        totals = jnp.sum(weights, axis=-1)
        mixture = jnp.einsum(
            "hqk,khd->qhd",
            weights.astype(jnp.bfloat16),
            values_own,
            preferred_element_type=jnp.float32,
        )
        return (mixture / jnp.transpose(totals)[:, :, None]).astype(jnp.bfloat16)

    blocked = queries.reshape((token_total // token_total, token_total) + queries.shape[1:])
    return lax.map(one_block, blocked).reshape(queries.shape)


def attend_text(queries, keys_own, values_own, length):
    factor = 1.0 / math.sqrt(queries.shape[-1])
    live_mask = (jnp.arange(keys_own.shape[0]) < length).astype(jnp.float32)
    scores = (
        jnp.einsum("qhd,khd->hqk", queries, keys_own, preferred_element_type=jnp.float32) * factor
    )
    weights = jnp.exp(scores) * live_mask
    totals = jnp.sum(weights, axis=-1)
    mixture = jnp.einsum(
        "hqk,khd->qhd", weights.astype(jnp.bfloat16), values_own, preferred_element_type=jnp.float32
    )
    return (mixture / jnp.transpose(totals)[:, :, None]).astype(jnp.bfloat16)


def _qkv_kernel(x_ref, w_ref, cos_ref, sin_ref, gain_ref, o_ref):
    section = pl.program_id(1)
    projected = jnp.dot(x_ref[...], w_ref[...], preferred_element_type=jnp.float32)

    @pl.when(section == 2)
    def _():
        o_ref[0] = projected.astype(o_ref.dtype)

    @pl.when(section < 2)
    def _():
        gains = gain_ref[pl.ds(jnp.minimum(section, 1), 1), :]
        cosine = cos_ref[...]
        sine_signed = sin_ref[...]
        parts = []
        for head in range(projected.shape[1] // HEAD_DIM):
            lanes = slice(head * HEAD_DIM, (head + 1) * HEAD_DIM)
            piece = projected[:, lanes]
            mean_square = jnp.mean(piece * piece, axis=-1, keepdims=True)
            normed = piece * lax.rsqrt(mean_square + EPSILON) * gains[:, lanes]
            swapped = pltpu.roll(normed, HEAD_DIM // 2, 1)
            parts.append(normed * cosine + swapped * sine_signed)
        o_ref[0] = jnp.concatenate(parts, axis=-1).astype(o_ref.dtype)


def pack_projected(block_in, cell_map, w_qkv, self_q_gain, self_k_gain, head_count):
    videos, per_video, model_width = block_in.shape
    rows = block_in.reshape(-1, model_width)
    token_total = rows.shape[0]
    group_width = model_width // head_count
    angles = rope_angles(cell_map).reshape(token_total, HEAD_DIM // 2)
    cosine = jnp.cos(angles)
    sine = jnp.sin(angles)
    cos_full = jnp.concatenate([cosine, cosine], axis=-1)
    sin_signed = jnp.concatenate([-sine, sine], axis=-1)
    gains = jnp.stack([self_q_gain, self_k_gain])
    packed = pl.pallas_call(
        _qkv_kernel,
        grid=(head_count, 3),
        in_specs=[
            pl.BlockSpec((token_total, model_width), lambda g, s: (0, 0)),
            pl.BlockSpec((model_width, group_width), lambda g, s: (0, s * head_count + g)),
            pl.BlockSpec((token_total, HEAD_DIM), lambda g, s: (0, 0)),
            pl.BlockSpec((token_total, HEAD_DIM), lambda g, s: (0, 0)),
            pl.BlockSpec((2, group_width), lambda g, s: (0, g)),
        ],
        out_specs=pl.BlockSpec((1, token_total, group_width), lambda g, s: (g, 0, s)),
        out_shape=jax.ShapeDtypeStruct((head_count, token_total, 3 * group_width), jnp.bfloat16),
        cost_estimate=pl.CostEstimate(
            flops=2 * token_total * model_width * 3 * model_width,
            bytes_accessed=2 * model_width * 3 * model_width + 4 * token_total * 3 * model_width,
            transcendentals=0,
        ),
    )(rows, w_qkv, cos_full, sin_signed, gains)
    return packed.reshape(head_count, videos, per_video, 3 * group_width)


def local(
    hidden,
    latent,
    cell_map,
    text_lengths,
    block_modulation,
    head_modulation,
    step_sizes,
    w_qkv,
    self_q_gain,
    self_k_gain,
    w_out,
    cross_gain,
    cross_wq,
    cross_q_gain,
    text_keys,
    text_values,
    cross_wo,
    head_w,
):
    head_count = lax.axis_size("head")
    tile_count = lax.axis_size("tile")
    videos, per_video, model_width = hidden.shape
    group_heads = HEADS // head_count
    group_width = group_heads * HEAD_DIM
    stream = hidden.astype(jnp.float32)
    block_shift = block_modulation[:, 0][:, None, :]
    block_scale = block_modulation[:, 1][:, None, :]
    block_gate = block_modulation[:, 2][:, None, :]
    block_in = (layer_norm(stream) * (1.0 + block_scale) + block_shift).astype(jnp.bfloat16)
    packed = pack_projected(block_in, cell_map, w_qkv, self_q_gain, self_k_gain, head_count)
    arrived = lax.all_to_all(
        packed.reshape(head_count * videos, per_video, 3 * group_width),
        ("head", "tile"),
        split_axis=0,
        concat_axis=0,
        tiled=True,
    )
    arrived = arrived.reshape(-1, 3, group_heads, HEAD_DIM)
    own_queries = arrived[:, 0]
    own_keys = arrived[:, 1]
    own_values = arrived[:, 2]
    own_mixture = attend_self(own_queries, own_keys, own_values)
    returned = lax.all_to_all(
        own_mixture.reshape(head_count * tile_count, per_video, group_width),
        ("head", "tile"),
        split_axis=0,
        concat_axis=0,
        tiled=True,
    )
    attended = (
        returned.reshape(head_count, videos, per_video, group_width)
        .transpose(1, 2, 0, 3)
        .reshape(videos * per_video, model_width)
    )
    self_update = jnp.dot(attended, w_out, preferred_element_type=jnp.float32).reshape(
        videos, per_video, model_width
    )
    after_self = stream + block_gate * self_update
    cross_in = (layer_norm(after_self) * cross_gain).astype(jnp.bfloat16)
    copies = jnp.broadcast_to(cross_in[None], (head_count,) + cross_in.shape).reshape(
        head_count * videos, per_video, model_width
    )
    owner_cross = lax.all_to_all(copies, ("head", "tile"), split_axis=0, concat_axis=0, tiled=True)
    owner_cross = owner_cross.reshape(-1, model_width)
    cross_queries = jnp.dot(owner_cross, cross_wq, preferred_element_type=jnp.float32).reshape(
        -1, group_heads, HEAD_DIM
    )
    cross_queries = head_norm(cross_queries, cross_q_gain.reshape(group_heads, HEAD_DIM)).astype(
        jnp.bfloat16
    )
    own_text_keys = text_keys[0].reshape(-1, group_heads, HEAD_DIM)
    own_text_values = text_values[0].reshape(-1, group_heads, HEAD_DIM)
    cross_mixture = attend_text(
        cross_queries, own_text_keys, own_text_values, text_lengths[0]
    ).reshape(-1, group_width)
    partial = jnp.dot(cross_mixture, cross_wo, preferred_element_type=jnp.float32).astype(
        jnp.bfloat16
    )
    returned_partials = lax.all_to_all(
        partial.reshape(head_count * tile_count, per_video, model_width),
        ("head", "tile"),
        split_axis=0,
        concat_axis=0,
        tiled=True,
    ).reshape(head_count, videos, per_video, model_width)
    returned_cross = jnp.sum(returned_partials.astype(jnp.float32), axis=0).astype(jnp.bfloat16)
    after_cross = after_self + returned_cross.astype(jnp.float32)
    hidden_next = after_cross.astype(jnp.bfloat16)
    head_shift = head_modulation[:, 0][:, None, :]
    head_scale = head_modulation[:, 1][:, None, :]
    head_in = (layer_norm(after_cross) * (1.0 + head_scale) + head_shift).astype(jnp.bfloat16)
    velocity = jnp.dot(
        head_in.reshape(-1, model_width), head_w, preferred_element_type=jnp.float32
    ).reshape(videos, per_video, -1)
    latent_next = latent + step_sizes[:, None, None] * velocity
    return (hidden_next, latent_next)


def solution(mesh):
    return jax.shard_map(
        local,
        mesh=mesh,
        in_specs=(
            P(None, ("head", "tile"), None),
            P(None, ("head", "tile"), None),
            P(None, ("head", "tile")),
            P("tile"),
            P(),
            P(),
            P(),
            P(),
            P(),
            P(),
            P(),
            P(),
            P(None, "head"),
            P("head"),
            P("tile", None, "head"),
            P("tile", None, "head"),
            P("head", None),
            P(),
        ),
        out_specs=(P(None, ("head", "tile"), None), P(None, ("head", "tile"), None)),
        check_vma=False,
    )
```

```python
import math

import jax
import jax.numpy as jnp
from jax import lax
from jax.experimental import pallas as pl
from jax.experimental.pallas import tpu as pltpu
from jax.sharding import PartitionSpec as P

HEADS = 12
HEAD_DIM = 128
GRID_H = 24
GRID_W = 8


EPSILON = 1e-06


def layer_norm(inputs):
    average = jnp.mean(inputs, axis=-1, keepdims=True)
    centred = inputs - average
    variance = jnp.mean(centred * centred, axis=-1, keepdims=True)
    return centred * lax.rsqrt(variance + EPSILON)


def head_norm(inputs, gain_table):
    mean_square = jnp.mean(inputs * inputs, axis=-1, keepdims=True)
    return inputs * lax.rsqrt(mean_square + EPSILON) * gain_table


def frequencies(pair_count):
    return jnp.power(10000.0, -jnp.arange(pair_count, dtype=jnp.float32) / pair_count)


def rope_angles(cell_ids):
    sixth_part = HEAD_DIM // 6
    time_pairs = HEAD_DIM // 2 - 2 * sixth_part
    plane_cells = GRID_H * GRID_W
    frame_index = (cell_ids // plane_cells).astype(jnp.float32)
    row_index = (cell_ids // GRID_W % GRID_H).astype(jnp.float32)
    column = (cell_ids % GRID_W).astype(jnp.float32)
    return jnp.concatenate(
        [
            frame_index[..., None] * frequencies(time_pairs),
            row_index[..., None] * frequencies(sixth_part),
            column[..., None] * frequencies(sixth_part),
        ],
        axis=-1,
    )


def rotate(inputs, angles):
    half_dim = inputs.shape[-1] // 2
    cosine = jnp.cos(angles)[..., None, :]
    sine_part = jnp.sin(angles)[..., None, :]
    lower_half = inputs[..., :half_dim]
    upper_half = inputs[..., half_dim:]
    return jnp.concatenate(
        [
            lower_half * cosine - upper_half * sine_part,
            lower_half * sine_part + upper_half * cosine,
        ],
        axis=-1,
    )


def attend_self(queries, keys_own, values_own):
    factor = 1.0 / math.sqrt(queries.shape[-1])
    token_total = queries.shape[0]

    def one_block(block_queries):
        scores = (
            jnp.einsum("qhd,khd->hqk", block_queries, keys_own, preferred_element_type=jnp.float32)
            * factor
        )
        weights = jnp.exp(scores)
        totals = jnp.sum(weights, axis=-1)
        mixture = jnp.einsum(
            "hqk,khd->qhd",
            weights.astype(jnp.bfloat16),
            values_own,
            preferred_element_type=jnp.float32,
        )
        return (mixture / jnp.transpose(totals)[:, :, None]).astype(jnp.bfloat16)

    blocked = queries.reshape((token_total // token_total, token_total) + queries.shape[1:])
    return lax.map(one_block, blocked).reshape(queries.shape)


def attend_text(queries, keys_own, values_own, length):
    factor = 1.0 / math.sqrt(queries.shape[-1])
    live_mask = (jnp.arange(keys_own.shape[0]) < length).astype(jnp.float32)
    scores = (
        jnp.einsum("qhd,khd->hqk", queries, keys_own, preferred_element_type=jnp.float32) * factor
    )
    weights = jnp.exp(scores) * live_mask
    totals = jnp.sum(weights, axis=-1)
    mixture = jnp.einsum(
        "hqk,khd->qhd", weights.astype(jnp.bfloat16), values_own, preferred_element_type=jnp.float32
    )
    return (mixture / jnp.transpose(totals)[:, :, None]).astype(jnp.bfloat16)


def _qkv_kernel(
    tokens_ref, shift_ref, scale_ref, wq_ref, wk_ref, wv_ref, cos_ref, sin_ref, gain_ref,
    o_ref, normed_ref,
):
    group = pl.program_id(0)
    videos = shift_ref.shape[0]
    per_video = tokens_ref.shape[0] // videos
    group_width = wq_ref.shape[1]

    @pl.when(group == 0)
    def _():
        shift = shift_ref[...]
        scale = 1.0 + scale_ref[...]
        for slot in range(per_video):
            rows = slice(slot * videos, (slot + 1) * videos)
            normed_ref[rows, :] = (layer_norm(tokens_ref[rows, :].astype(jnp.float32)) * scale + shift).astype(
                normed_ref.dtype
            )

    block_in = normed_ref[...]
    cosine = cos_ref[...]
    sine_signed = sin_ref[...]
    for section, w_ref in enumerate((wq_ref, wk_ref, wv_ref)):
        projected = jnp.dot(block_in, w_ref[...], preferred_element_type=jnp.float32)
        if section < 2:
            gains = gain_ref[section : section + 1, :]
            parts = []
            for head in range(group_width // HEAD_DIM):
                lanes = slice(head * HEAD_DIM, (head + 1) * HEAD_DIM)
                piece = projected[:, lanes]
                mean_square = jnp.mean(piece * piece, axis=-1, keepdims=True)
                normed = piece * lax.rsqrt(mean_square + EPSILON) * gains[:, lanes]
                swapped = pltpu.roll(normed, HEAD_DIM // 2, 1)
                parts.append(normed * cosine + swapped * sine_signed)
            projected = jnp.concatenate(parts, axis=-1)
        result = projected.astype(o_ref.dtype)
        for slot in range(per_video):
            column = (slot * 3 + section) * group_width
            o_ref[0, :, column : column + group_width] = result[slot * videos : (slot + 1) * videos, :]


def pack_projected(hidden, block_modulation, cell_map, w_qkv, self_q_gain, self_k_gain, head_count):
    videos, per_video, model_width = hidden.shape
    tokens = jnp.transpose(hidden, (1, 0, 2)).reshape(-1, model_width)
    token_total = tokens.shape[0]
    group_width = model_width // head_count
    angles = rope_angles(jnp.transpose(cell_map, (1, 0))).reshape(token_total, HEAD_DIM // 2)
    cosine = jnp.cos(angles)
    sine = jnp.sin(angles)
    cos_full = jnp.concatenate([cosine, cosine], axis=-1)
    sin_signed = jnp.concatenate([-sine, sine], axis=-1)
    gains = jnp.stack([self_q_gain, self_k_gain])
    whole = lambda g: (0, 0)
    packed = pl.pallas_call(
        _qkv_kernel,
        grid=(head_count,),
        in_specs=[
            pl.BlockSpec((token_total, model_width), whole),
            pl.BlockSpec((videos, model_width), whole),
            pl.BlockSpec((videos, model_width), whole),
            pl.BlockSpec((model_width, group_width), lambda g: (0, g)),
            pl.BlockSpec((model_width, group_width), lambda g: (0, head_count + g)),
            pl.BlockSpec((model_width, group_width), lambda g: (0, 2 * head_count + g)),
            pl.BlockSpec((token_total, HEAD_DIM), whole),
            pl.BlockSpec((token_total, HEAD_DIM), whole),
            pl.BlockSpec((2, group_width), lambda g: (0, g)),
        ],
        out_specs=pl.BlockSpec((1, videos, per_video * 3 * group_width), lambda g: (g, 0, 0)),
        out_shape=jax.ShapeDtypeStruct(
            (head_count, videos, per_video * 3 * group_width), jnp.bfloat16
        ),
        scratch_shapes=[pltpu.VMEM((token_total, model_width), jnp.bfloat16)],
        cost_estimate=pl.CostEstimate(
            flops=2 * token_total * model_width * 3 * model_width,
            bytes_accessed=2 * model_width * 3 * model_width + 8 * token_total * 3 * model_width,
            transcendentals=0,
        ),
    )(
        tokens, block_modulation[:, 0], block_modulation[:, 1], w_qkv, w_qkv, w_qkv,
        cos_full, sin_signed, gains,
    )
    return packed.reshape(head_count * videos, per_video * 3 * group_width)


def local(
    hidden,
    latent,
    cell_map,
    text_lengths,
    block_modulation,
    head_modulation,
    step_sizes,
    w_qkv,
    self_q_gain,
    self_k_gain,
    w_out,
    cross_gain,
    cross_wq,
    cross_q_gain,
    text_keys,
    text_values,
    cross_wo,
    head_w,
):
    head_count = lax.axis_size("head")
    tile_count = lax.axis_size("tile")
    videos, per_video, model_width = hidden.shape
    group_heads = HEADS // head_count
    group_width = group_heads * HEAD_DIM
    stream = hidden.astype(jnp.float32)
    block_gate = block_modulation[:, 2][:, None, :]
    packed = pack_projected(
        hidden, block_modulation, cell_map, w_qkv, self_q_gain, self_k_gain, head_count
    )
    arrived = lax.all_to_all(packed, ("head", "tile"), split_axis=0, concat_axis=0, tiled=True)
    arrived = arrived.reshape(-1, 3, group_heads, HEAD_DIM)
    own_queries = arrived[:, 0]
    own_keys = arrived[:, 1]
    own_values = arrived[:, 2]
    own_mixture = attend_self(own_queries, own_keys, own_values)
    returned = lax.all_to_all(
        own_mixture.reshape(head_count * tile_count, per_video, group_width),
        ("head", "tile"),
        split_axis=0,
        concat_axis=0,
        tiled=True,
    )
    attended = (
        returned.reshape(head_count, videos, per_video, group_width)
        .transpose(1, 2, 0, 3)
        .reshape(videos * per_video, model_width)
    )
    self_update = jnp.dot(attended, w_out, preferred_element_type=jnp.float32).reshape(
        videos, per_video, model_width
    )
    after_self = stream + block_gate * self_update
    cross_in = (layer_norm(after_self) * cross_gain).astype(jnp.bfloat16)
    copies = jnp.broadcast_to(cross_in[None], (head_count,) + cross_in.shape).reshape(
        head_count * videos, per_video, model_width
    )
    owner_cross = lax.all_to_all(copies, ("head", "tile"), split_axis=0, concat_axis=0, tiled=True)
    owner_cross = owner_cross.reshape(-1, model_width)
    cross_queries = jnp.dot(owner_cross, cross_wq, preferred_element_type=jnp.float32).reshape(
        -1, group_heads, HEAD_DIM
    )
    cross_queries = head_norm(cross_queries, cross_q_gain.reshape(group_heads, HEAD_DIM)).astype(
        jnp.bfloat16
    )
    own_text_keys = text_keys[0].reshape(-1, group_heads, HEAD_DIM)
    own_text_values = text_values[0].reshape(-1, group_heads, HEAD_DIM)
    cross_mixture = attend_text(
        cross_queries, own_text_keys, own_text_values, text_lengths[0]
    ).reshape(-1, group_width)
    partial = jnp.dot(cross_mixture, cross_wo, preferred_element_type=jnp.float32).astype(
        jnp.bfloat16
    )
    returned_partials = lax.all_to_all(
        partial.reshape(head_count * tile_count, per_video, model_width),
        ("head", "tile"),
        split_axis=0,
        concat_axis=0,
        tiled=True,
    ).reshape(head_count, videos, per_video, model_width)
    returned_cross = jnp.sum(returned_partials.astype(jnp.float32), axis=0).astype(jnp.bfloat16)
    after_cross = after_self + returned_cross.astype(jnp.float32)
    hidden_next = after_cross.astype(jnp.bfloat16)
    head_shift = head_modulation[:, 0][:, None, :]
    head_scale = head_modulation[:, 1][:, None, :]
    head_in = (layer_norm(after_cross) * (1.0 + head_scale) + head_shift).astype(jnp.bfloat16)
    velocity = jnp.dot(
        head_in.reshape(-1, model_width), head_w, preferred_element_type=jnp.float32
    ).reshape(videos, per_video, -1)
    latent_next = latent + step_sizes[:, None, None] * velocity
    return (hidden_next, latent_next)


def solution(mesh):
    return jax.shard_map(
        local,
        mesh=mesh,
        in_specs=(
            P(None, ("head", "tile"), None),
            P(None, ("head", "tile"), None),
            P(None, ("head", "tile")),
            P("tile"),
            P(),
            P(),
            P(),
            P(),
            P(),
            P(),
            P(),
            P(),
            P(None, "head"),
            P("head"),
            P("tile", None, "head"),
            P("tile", None, "head"),
            P("head", None),
            P(),
        ),
        out_specs=(P(None, ("head", "tile"), None), P(None, ("head", "tile"), None)),
        check_vma=False,
    )
```

```python
import math

import jax
import jax.numpy as jnp
from jax import lax
from jax.experimental import pallas as pl
from jax.experimental.pallas import tpu as pltpu
from jax.sharding import PartitionSpec as P

HEADS = 12
HEAD_DIM = 128
GRID_H = 24
GRID_W = 8


EPSILON = 1e-06


def layer_norm(inputs):
    average = jnp.mean(inputs, axis=-1, keepdims=True)
    centred = inputs - average
    variance = jnp.mean(centred * centred, axis=-1, keepdims=True)
    return centred * lax.rsqrt(variance + EPSILON)


def head_norm(inputs, gain_table):
    mean_square = jnp.mean(inputs * inputs, axis=-1, keepdims=True)
    return inputs * lax.rsqrt(mean_square + EPSILON) * gain_table


def frequencies(pair_count):
    return jnp.power(10000.0, -jnp.arange(pair_count, dtype=jnp.float32) / pair_count)


def rope_angles(cell_ids):
    sixth_part = HEAD_DIM // 6
    time_pairs = HEAD_DIM // 2 - 2 * sixth_part
    plane_cells = GRID_H * GRID_W
    frame_index = (cell_ids // plane_cells).astype(jnp.float32)
    row_index = (cell_ids // GRID_W % GRID_H).astype(jnp.float32)
    column = (cell_ids % GRID_W).astype(jnp.float32)
    return jnp.concatenate(
        [
            frame_index[..., None] * frequencies(time_pairs),
            row_index[..., None] * frequencies(sixth_part),
            column[..., None] * frequencies(sixth_part),
        ],
        axis=-1,
    )


def rotate(inputs, angles):
    half_dim = inputs.shape[-1] // 2
    cosine = jnp.cos(angles)[..., None, :]
    sine_part = jnp.sin(angles)[..., None, :]
    lower_half = inputs[..., :half_dim]
    upper_half = inputs[..., half_dim:]
    return jnp.concatenate(
        [
            lower_half * cosine - upper_half * sine_part,
            lower_half * sine_part + upper_half * cosine,
        ],
        axis=-1,
    )


def attend_self(queries, keys_own, values_own):
    factor = 1.0 / math.sqrt(queries.shape[-1])
    token_total = queries.shape[0]

    def one_block(block_queries):
        scores = (
            jnp.einsum("qhd,khd->hqk", block_queries, keys_own, preferred_element_type=jnp.float32)
            * factor
        )
        weights = jnp.exp(scores)
        totals = jnp.sum(weights, axis=-1)
        mixture = jnp.einsum(
            "hqk,khd->qhd",
            weights.astype(jnp.bfloat16),
            values_own,
            preferred_element_type=jnp.float32,
        )
        return (mixture / jnp.transpose(totals)[:, :, None]).astype(jnp.bfloat16)

    blocked = queries.reshape((token_total // token_total, token_total) + queries.shape[1:])
    return lax.map(one_block, blocked).reshape(queries.shape)


def attend_text(queries, keys_own, values_own, length):
    factor = 1.0 / math.sqrt(queries.shape[-1])
    live_mask = (jnp.arange(keys_own.shape[0]) < length).astype(jnp.float32)
    scores = (
        jnp.einsum("qhd,khd->hqk", queries, keys_own, preferred_element_type=jnp.float32) * factor
    )
    weights = jnp.exp(scores) * live_mask
    totals = jnp.sum(weights, axis=-1)
    mixture = jnp.einsum(
        "hqk,khd->qhd", weights.astype(jnp.bfloat16), values_own, preferred_element_type=jnp.float32
    )
    return (mixture / jnp.transpose(totals)[:, :, None]).astype(jnp.bfloat16)


def _qkv_kernel(x_ref, wq_ref, wk_ref, wv_ref, cos_ref, sin_ref, gain_ref, o_ref):
    block_in = x_ref[...]
    cosine = cos_ref[...]
    sine_signed = sin_ref[...]
    group_width = wq_ref.shape[1]
    for section, w_ref in enumerate((wq_ref, wk_ref, wv_ref)):
        projected = jnp.dot(block_in, w_ref[...], preferred_element_type=jnp.float32)
        if section < 2:
            gains = gain_ref[section : section + 1, :]
            parts = []
            for head in range(group_width // HEAD_DIM):
                lanes = slice(head * HEAD_DIM, (head + 1) * HEAD_DIM)
                piece = projected[:, lanes]
                mean_square = jnp.mean(piece * piece, axis=-1, keepdims=True)
                normed = piece * lax.rsqrt(mean_square + EPSILON) * gains[:, lanes]
                swapped = pltpu.roll(normed, HEAD_DIM // 2, 1)
                parts.append(normed * cosine + swapped * sine_signed)
            projected = jnp.concatenate(parts, axis=-1)
        o_ref[0, :, section * group_width : (section + 1) * group_width] = projected.astype(
            o_ref.dtype
        )


def pack_projected(block_in, cell_map, w_qkv, self_q_gain, self_k_gain, head_count):
    videos, per_video, model_width = block_in.shape
    rows = block_in.reshape(-1, model_width)
    token_total = rows.shape[0]
    group_width = model_width // head_count
    angles = rope_angles(cell_map).reshape(token_total, HEAD_DIM // 2)
    cosine = jnp.cos(angles)
    sine = jnp.sin(angles)
    cos_full = jnp.concatenate([cosine, cosine], axis=-1)
    sin_signed = jnp.concatenate([-sine, sine], axis=-1)
    gains = jnp.stack([self_q_gain, self_k_gain])
    whole = lambda g: (0, 0)
    packed = pl.pallas_call(
        _qkv_kernel,
        grid=(head_count,),
        in_specs=[
            pl.BlockSpec((token_total, model_width), whole),
            pl.BlockSpec((model_width, group_width), lambda g: (0, g)),
            pl.BlockSpec((model_width, group_width), lambda g: (0, head_count + g)),
            pl.BlockSpec((model_width, group_width), lambda g: (0, 2 * head_count + g)),
            pl.BlockSpec((token_total, HEAD_DIM), whole),
            pl.BlockSpec((token_total, HEAD_DIM), whole),
            pl.BlockSpec((2, group_width), lambda g: (0, g)),
        ],
        out_specs=pl.BlockSpec((1, token_total, 3 * group_width), lambda g: (g, 0, 0)),
        out_shape=jax.ShapeDtypeStruct((head_count, token_total, 3 * group_width), jnp.bfloat16),
        cost_estimate=pl.CostEstimate(
            flops=2 * token_total * model_width * 3 * model_width,
            bytes_accessed=2 * model_width * 3 * model_width + 4 * token_total * 3 * model_width,
            transcendentals=0,
        ),
    )(rows, w_qkv, w_qkv, w_qkv, cos_full, sin_signed, gains)
    return packed.reshape(head_count, videos, per_video, 3 * group_width)


def local(
    hidden,
    latent,
    cell_map,
    text_lengths,
    block_modulation,
    head_modulation,
    step_sizes,
    w_qkv,
    self_q_gain,
    self_k_gain,
    w_out,
    cross_gain,
    cross_wq,
    cross_q_gain,
    text_keys,
    text_values,
    cross_wo,
    head_w,
):
    head_count = lax.axis_size("head")
    tile_count = lax.axis_size("tile")
    videos, per_video, model_width = hidden.shape
    group_heads = HEADS // head_count
    group_width = group_heads * HEAD_DIM
    stream = hidden.astype(jnp.float32)
    block_shift = block_modulation[:, 0][:, None, :]
    block_scale = block_modulation[:, 1][:, None, :]
    block_gate = block_modulation[:, 2][:, None, :]
    block_in = (layer_norm(stream) * (1.0 + block_scale) + block_shift).astype(jnp.bfloat16)
    packed = pack_projected(block_in, cell_map, w_qkv, self_q_gain, self_k_gain, head_count)
    arrived = lax.all_to_all(
        packed.reshape(head_count * videos, per_video, 3 * group_width),
        ("head", "tile"),
        split_axis=0,
        concat_axis=0,
        tiled=True,
    )
    arrived = arrived.reshape(-1, 3, group_heads, HEAD_DIM)
    own_queries = arrived[:, 0]
    own_keys = arrived[:, 1]
    own_values = arrived[:, 2]
    own_mixture = attend_self(own_queries, own_keys, own_values)
    returned = lax.all_to_all(
        own_mixture.reshape(head_count * tile_count, per_video, group_width),
        ("head", "tile"),
        split_axis=0,
        concat_axis=0,
        tiled=True,
    )
    attended = (
        returned.reshape(head_count, videos, per_video, group_width)
        .transpose(1, 2, 0, 3)
        .reshape(videos * per_video, model_width)
    )
    self_update = jnp.dot(attended, w_out, preferred_element_type=jnp.float32).reshape(
        videos, per_video, model_width
    )
    after_self = stream + block_gate * self_update
    cross_in = (layer_norm(after_self) * cross_gain).astype(jnp.bfloat16)
    copies = jnp.broadcast_to(cross_in[None], (head_count,) + cross_in.shape).reshape(
        head_count * videos, per_video, model_width
    )
    owner_cross = lax.all_to_all(copies, ("head", "tile"), split_axis=0, concat_axis=0, tiled=True)
    owner_cross = owner_cross.reshape(-1, model_width)
    cross_queries = jnp.dot(owner_cross, cross_wq, preferred_element_type=jnp.float32).reshape(
        -1, group_heads, HEAD_DIM
    )
    cross_queries = head_norm(cross_queries, cross_q_gain.reshape(group_heads, HEAD_DIM)).astype(
        jnp.bfloat16
    )
    own_text_keys = text_keys[0].reshape(-1, group_heads, HEAD_DIM)
    own_text_values = text_values[0].reshape(-1, group_heads, HEAD_DIM)
    cross_mixture = attend_text(
        cross_queries, own_text_keys, own_text_values, text_lengths[0]
    ).reshape(-1, group_width)
    partial = jnp.dot(cross_mixture, cross_wo, preferred_element_type=jnp.float32).astype(
        jnp.bfloat16
    )
    returned_partials = lax.all_to_all(
        partial.reshape(head_count * tile_count, per_video, model_width),
        ("head", "tile"),
        split_axis=0,
        concat_axis=0,
        tiled=True,
    ).reshape(head_count, videos, per_video, model_width)
    returned_cross = jnp.sum(returned_partials.astype(jnp.float32), axis=0).astype(jnp.bfloat16)
    after_cross = after_self + returned_cross.astype(jnp.float32)
    hidden_next = after_cross.astype(jnp.bfloat16)
    head_shift = head_modulation[:, 0][:, None, :]
    head_scale = head_modulation[:, 1][:, None, :]
    head_in = (layer_norm(after_cross) * (1.0 + head_scale) + head_shift).astype(jnp.bfloat16)
    velocity = jnp.dot(
        head_in.reshape(-1, model_width), head_w, preferred_element_type=jnp.float32
    ).reshape(videos, per_video, -1)
    latent_next = latent + step_sizes[:, None, None] * velocity
    return (hidden_next, latent_next)


def solution(mesh):
    return jax.shard_map(
        local,
        mesh=mesh,
        in_specs=(
            P(None, ("head", "tile"), None),
            P(None, ("head", "tile"), None),
            P(None, ("head", "tile")),
            P("tile"),
            P(),
            P(),
            P(),
            P(),
            P(),
            P(),
            P(),
            P(),
            P(None, "head"),
            P("head"),
            P("tile", None, "head"),
            P("tile", None, "head"),
            P("head", None),
            P(),
        ),
        out_specs=(P(None, ("head", "tile"), None), P(None, ("head", "tile"), None)),
        check_vma=False,
    )
```

```python
import math

import jax
import jax.numpy as jnp
from jax import lax
from jax.experimental import pallas as pl
from jax.experimental.pallas import tpu as pltpu
from jax.sharding import PartitionSpec as P

HEADS = 12
HEAD_DIM = 128
GRID_H = 24
GRID_W = 8


EPSILON = 1e-06


def layer_norm(inputs):
    average = jnp.mean(inputs, axis=-1, keepdims=True)
    centred = inputs - average
    variance = jnp.mean(centred * centred, axis=-1, keepdims=True)
    return centred * lax.rsqrt(variance + EPSILON)


def head_norm(inputs, gain_table):
    mean_square = jnp.mean(inputs * inputs, axis=-1, keepdims=True)
    return inputs * lax.rsqrt(mean_square + EPSILON) * gain_table


def frequencies(pair_count):
    return jnp.power(10000.0, -jnp.arange(pair_count, dtype=jnp.float32) / pair_count)


def rope_angles(cell_ids):
    sixth_part = HEAD_DIM // 6
    time_pairs = HEAD_DIM // 2 - 2 * sixth_part
    plane_cells = GRID_H * GRID_W
    frame_index = (cell_ids // plane_cells).astype(jnp.float32)
    row_index = (cell_ids // GRID_W % GRID_H).astype(jnp.float32)
    column = (cell_ids % GRID_W).astype(jnp.float32)
    return jnp.concatenate(
        [
            frame_index[..., None] * frequencies(time_pairs),
            row_index[..., None] * frequencies(sixth_part),
            column[..., None] * frequencies(sixth_part),
        ],
        axis=-1,
    )


def rotate(inputs, angles):
    half_dim = inputs.shape[-1] // 2
    cosine = jnp.cos(angles)[..., None, :]
    sine_part = jnp.sin(angles)[..., None, :]
    lower_half = inputs[..., :half_dim]
    upper_half = inputs[..., half_dim:]
    return jnp.concatenate(
        [
            lower_half * cosine - upper_half * sine_part,
            lower_half * sine_part + upper_half * cosine,
        ],
        axis=-1,
    )


def _self_attention_kernel(x_ref, o_ref):
    group_width = o_ref.shape[1]
    factor = 1.0 / math.sqrt(HEAD_DIM)
    for head in range(group_width // HEAD_DIM):
        lanes = slice(head * HEAD_DIM, (head + 1) * HEAD_DIM)
        queries = x_ref[:, head * HEAD_DIM : (head + 1) * HEAD_DIM]
        keys = x_ref[:, group_width + head * HEAD_DIM : group_width + (head + 1) * HEAD_DIM]
        values = x_ref[:, 2 * group_width + head * HEAD_DIM : 2 * group_width + (head + 1) * HEAD_DIM]
        scores = (
            lax.dot_general(
                queries, keys, (((1,), (1,)), ((), ())), preferred_element_type=jnp.float32
            )
            * factor
        )
        weights = jnp.exp(scores)
        totals = jnp.sum(weights, axis=-1, keepdims=True)
        mixture = jnp.dot(
            weights.astype(jnp.bfloat16), values, preferred_element_type=jnp.float32
        )
        o_ref[:, lanes] = (mixture / totals).astype(o_ref.dtype)


def attend_self(arrived, group_width):
    token_total = arrived.shape[0]
    return pl.pallas_call(
        _self_attention_kernel,
        out_shape=jax.ShapeDtypeStruct((token_total, group_width), jnp.bfloat16),
        cost_estimate=pl.CostEstimate(
            flops=4 * token_total * token_total * group_width,
            bytes_accessed=2 * token_total * 4 * group_width,
            transcendentals=token_total * token_total * (group_width // HEAD_DIM),
        ),
    )(arrived)


def attend_text(queries, keys_own, values_own, length):
    factor = 1.0 / math.sqrt(queries.shape[-1])
    live_mask = (jnp.arange(keys_own.shape[0]) < length).astype(jnp.float32)
    scores = (
        jnp.einsum("qhd,khd->hqk", queries, keys_own, preferred_element_type=jnp.float32) * factor
    )
    weights = jnp.exp(scores) * live_mask
    totals = jnp.sum(weights, axis=-1)
    mixture = jnp.einsum(
        "hqk,khd->qhd", weights.astype(jnp.bfloat16), values_own, preferred_element_type=jnp.float32
    )
    return (mixture / jnp.transpose(totals)[:, :, None]).astype(jnp.bfloat16)


def _qkv_kernel(x_ref, wq_ref, wk_ref, wv_ref, cos_ref, sin_ref, gain_ref, o_ref):
    block_in = x_ref[...]
    cosine = cos_ref[...]
    sine_signed = sin_ref[...]
    group_width = wq_ref.shape[1]
    for section, w_ref in enumerate((wq_ref, wk_ref, wv_ref)):
        projected = jnp.dot(block_in, w_ref[...], preferred_element_type=jnp.float32)
        if section < 2:
            gains = gain_ref[section : section + 1, :]
            parts = []
            for head in range(group_width // HEAD_DIM):
                lanes = slice(head * HEAD_DIM, (head + 1) * HEAD_DIM)
                piece = projected[:, lanes]
                mean_square = jnp.mean(piece * piece, axis=-1, keepdims=True)
                normed = piece * lax.rsqrt(mean_square + EPSILON) * gains[:, lanes]
                swapped = pltpu.roll(normed, HEAD_DIM // 2, 1)
                parts.append(normed * cosine + swapped * sine_signed)
            projected = jnp.concatenate(parts, axis=-1)
        o_ref[0, :, section * group_width : (section + 1) * group_width] = projected.astype(
            o_ref.dtype
        )


def pack_projected(block_in, cell_map, w_qkv, self_q_gain, self_k_gain, head_count):
    videos, per_video, model_width = block_in.shape
    rows = block_in.reshape(-1, model_width)
    token_total = rows.shape[0]
    group_width = model_width // head_count
    angles = rope_angles(cell_map).reshape(token_total, HEAD_DIM // 2)
    cosine = jnp.cos(angles)
    sine = jnp.sin(angles)
    cos_full = jnp.concatenate([cosine, cosine], axis=-1)
    sin_signed = jnp.concatenate([-sine, sine], axis=-1)
    gains = jnp.stack([self_q_gain, self_k_gain])
    whole = lambda g: (0, 0)
    packed = pl.pallas_call(
        _qkv_kernel,
        grid=(head_count,),
        in_specs=[
            pl.BlockSpec((token_total, model_width), whole),
            pl.BlockSpec((model_width, group_width), lambda g: (0, g)),
            pl.BlockSpec((model_width, group_width), lambda g: (0, head_count + g)),
            pl.BlockSpec((model_width, group_width), lambda g: (0, 2 * head_count + g)),
            pl.BlockSpec((token_total, HEAD_DIM), whole),
            pl.BlockSpec((token_total, HEAD_DIM), whole),
            pl.BlockSpec((2, group_width), lambda g: (0, g)),
        ],
        out_specs=pl.BlockSpec((1, token_total, 3 * group_width), lambda g: (g, 0, 0)),
        out_shape=jax.ShapeDtypeStruct((head_count, token_total, 3 * group_width), jnp.bfloat16),
        cost_estimate=pl.CostEstimate(
            flops=2 * token_total * model_width * 3 * model_width,
            bytes_accessed=2 * model_width * 3 * model_width + 4 * token_total * 3 * model_width,
            transcendentals=0,
        ),
    )(rows, w_qkv, w_qkv, w_qkv, cos_full, sin_signed, gains)
    return packed.reshape(head_count, videos, per_video, 3 * group_width)


def local(
    hidden,
    latent,
    cell_map,
    text_lengths,
    block_modulation,
    head_modulation,
    step_sizes,
    w_qkv,
    self_q_gain,
    self_k_gain,
    w_out,
    cross_gain,
    cross_wq,
    cross_q_gain,
    text_keys,
    text_values,
    cross_wo,
    head_w,
):
    head_count = lax.axis_size("head")
    tile_count = lax.axis_size("tile")
    videos, per_video, model_width = hidden.shape
    group_heads = HEADS // head_count
    group_width = group_heads * HEAD_DIM
    stream = hidden.astype(jnp.float32)
    block_shift = block_modulation[:, 0][:, None, :]
    block_scale = block_modulation[:, 1][:, None, :]
    block_gate = block_modulation[:, 2][:, None, :]
    block_in = (layer_norm(stream) * (1.0 + block_scale) + block_shift).astype(jnp.bfloat16)
    packed = pack_projected(block_in, cell_map, w_qkv, self_q_gain, self_k_gain, head_count)
    arrived = lax.all_to_all(
        packed.reshape(head_count * videos, per_video, 3 * group_width),
        ("head", "tile"),
        split_axis=0,
        concat_axis=0,
        tiled=True,
    )
    own_mixture = attend_self(arrived.reshape(-1, 3 * group_width), group_width)
    returned = lax.all_to_all(
        own_mixture.reshape(head_count * tile_count, per_video, group_width),
        ("head", "tile"),
        split_axis=0,
        concat_axis=0,
        tiled=True,
    )
    attended = (
        returned.reshape(head_count, videos, per_video, group_width)
        .transpose(1, 2, 0, 3)
        .reshape(videos * per_video, model_width)
    )
    self_update = jnp.dot(attended, w_out, preferred_element_type=jnp.float32).reshape(
        videos, per_video, model_width
    )
    after_self = stream + block_gate * self_update
    cross_in = (layer_norm(after_self) * cross_gain).astype(jnp.bfloat16)
    copies = jnp.broadcast_to(cross_in[None], (head_count,) + cross_in.shape).reshape(
        head_count * videos, per_video, model_width
    )
    owner_cross = lax.all_to_all(copies, ("head", "tile"), split_axis=0, concat_axis=0, tiled=True)
    owner_cross = owner_cross.reshape(-1, model_width)
    cross_queries = jnp.dot(owner_cross, cross_wq, preferred_element_type=jnp.float32).reshape(
        -1, group_heads, HEAD_DIM
    )
    cross_queries = head_norm(cross_queries, cross_q_gain.reshape(group_heads, HEAD_DIM)).astype(
        jnp.bfloat16
    )
    own_text_keys = text_keys[0].reshape(-1, group_heads, HEAD_DIM)
    own_text_values = text_values[0].reshape(-1, group_heads, HEAD_DIM)
    cross_mixture = attend_text(
        cross_queries, own_text_keys, own_text_values, text_lengths[0]
    ).reshape(-1, group_width)
    partial = jnp.dot(cross_mixture, cross_wo, preferred_element_type=jnp.float32).astype(
        jnp.bfloat16
    )
    returned_partials = lax.all_to_all(
        partial.reshape(head_count * tile_count, per_video, model_width),
        ("head", "tile"),
        split_axis=0,
        concat_axis=0,
        tiled=True,
    ).reshape(head_count, videos, per_video, model_width)
    returned_cross = jnp.sum(returned_partials.astype(jnp.float32), axis=0).astype(jnp.bfloat16)
    after_cross = after_self + returned_cross.astype(jnp.float32)
    hidden_next = after_cross.astype(jnp.bfloat16)
    head_shift = head_modulation[:, 0][:, None, :]
    head_scale = head_modulation[:, 1][:, None, :]
    head_in = (layer_norm(after_cross) * (1.0 + head_scale) + head_shift).astype(jnp.bfloat16)
    velocity = jnp.dot(
        head_in.reshape(-1, model_width), head_w, preferred_element_type=jnp.float32
    ).reshape(videos, per_video, -1)
    latent_next = latent + step_sizes[:, None, None] * velocity
    return (hidden_next, latent_next)


def solution(mesh):
    return jax.shard_map(
        local,
        mesh=mesh,
        in_specs=(
            P(None, ("head", "tile"), None),
            P(None, ("head", "tile"), None),
            P(None, ("head", "tile")),
            P("tile"),
            P(),
            P(),
            P(),
            P(),
            P(),
            P(),
            P(),
            P(),
            P(None, "head"),
            P("head"),
            P("tile", None, "head"),
            P("tile", None, "head"),
            P("head", None),
            P(),
        ),
        out_specs=(P(None, ("head", "tile"), None), P(None, ("head", "tile"), None)),
        check_vma=False,
    )
```

```python
import math

import jax
import jax.numpy as jnp
from jax import lax
from jax.experimental import pallas as pl
from jax.experimental.pallas import tpu as pltpu
from jax.sharding import PartitionSpec as P

HEADS = 12
HEAD_DIM = 128
GRID_H = 24
GRID_W = 8


EPSILON = 1e-06


def layer_norm(inputs):
    average = jnp.mean(inputs, axis=-1, keepdims=True)
    centred = inputs - average
    variance = jnp.mean(centred * centred, axis=-1, keepdims=True)
    return centred * lax.rsqrt(variance + EPSILON)


def head_norm(inputs, gain_table):
    mean_square = jnp.mean(inputs * inputs, axis=-1, keepdims=True)
    return inputs * lax.rsqrt(mean_square + EPSILON) * gain_table


def frequencies(pair_count):
    return jnp.power(10000.0, -jnp.arange(pair_count, dtype=jnp.float32) / pair_count)


def rope_angles(cell_ids):
    sixth_part = HEAD_DIM // 6
    time_pairs = HEAD_DIM // 2 - 2 * sixth_part
    plane_cells = GRID_H * GRID_W
    frame_index = (cell_ids // plane_cells).astype(jnp.float32)
    row_index = (cell_ids // GRID_W % GRID_H).astype(jnp.float32)
    column = (cell_ids % GRID_W).astype(jnp.float32)
    return jnp.concatenate(
        [
            frame_index[..., None] * frequencies(time_pairs),
            row_index[..., None] * frequencies(sixth_part),
            column[..., None] * frequencies(sixth_part),
        ],
        axis=-1,
    )


def rotate(inputs, angles):
    half_dim = inputs.shape[-1] // 2
    cosine = jnp.cos(angles)[..., None, :]
    sine_part = jnp.sin(angles)[..., None, :]
    lower_half = inputs[..., :half_dim]
    upper_half = inputs[..., half_dim:]
    return jnp.concatenate(
        [
            lower_half * cosine - upper_half * sine_part,
            lower_half * sine_part + upper_half * cosine,
        ],
        axis=-1,
    )


def _self_attention_kernel(x_ref, o_ref):
    group_width = o_ref.shape[1]
    factor = 1.0 / math.sqrt(HEAD_DIM)
    for head in range(group_width // HEAD_DIM):
        lanes = slice(head * HEAD_DIM, (head + 1) * HEAD_DIM)
        queries = x_ref[:, head * HEAD_DIM : (head + 1) * HEAD_DIM]
        keys = x_ref[:, group_width + head * HEAD_DIM : group_width + (head + 1) * HEAD_DIM]
        values = x_ref[:, 2 * group_width + head * HEAD_DIM : 2 * group_width + (head + 1) * HEAD_DIM]
        scores = (
            lax.dot_general(
                queries, keys, (((1,), (1,)), ((), ())), preferred_element_type=jnp.float32
            )
            * factor
        )
        weights = jnp.exp(scores)
        totals = jnp.sum(weights, axis=-1, keepdims=True)
        mixture = jnp.dot(
            weights.astype(jnp.bfloat16), values, preferred_element_type=jnp.float32
        )
        o_ref[:, lanes] = (mixture / totals).astype(o_ref.dtype)


def attend_self(arrived, group_width):
    token_total = arrived.shape[0]
    return pl.pallas_call(
        _self_attention_kernel,
        out_shape=jax.ShapeDtypeStruct((token_total, group_width), jnp.bfloat16),
        cost_estimate=pl.CostEstimate(
            flops=4 * token_total * token_total * group_width,
            bytes_accessed=2 * token_total * 4 * group_width,
            transcendentals=token_total * token_total * (group_width // HEAD_DIM),
        ),
    )(arrived)


def _cross_kernel(length_ref, x_ref, wq_ref, gain_ref, keys_ref, values_ref, wo_ref, o_ref, mixed_ref):
    factor = 1.0 / math.sqrt(HEAD_DIM)
    group_width = wq_ref.shape[1]
    text = keys_ref.shape[0]
    projected = jnp.dot(x_ref[...], wq_ref[...], preferred_element_type=jnp.float32)
    gains = gain_ref[...]
    live = (lax.broadcasted_iota(jnp.int32, (1, text), 1) < length_ref[0]).astype(jnp.float32)
    for head in range(group_width // HEAD_DIM):
        lanes = slice(head * HEAD_DIM, (head + 1) * HEAD_DIM)
        piece = projected[:, lanes]
        mean_square = jnp.mean(piece * piece, axis=-1, keepdims=True)
        queries = (piece * lax.rsqrt(mean_square + EPSILON) * gains[:, lanes]).astype(jnp.bfloat16)
        scores = (
            lax.dot_general(
                queries, keys_ref[:, lanes], (((1,), (1,)), ((), ())),
                preferred_element_type=jnp.float32,
            )
            * factor
        )
        weights = jnp.exp(scores) * live
        totals = jnp.sum(weights, axis=-1, keepdims=True)
        mixture = jnp.dot(
            weights.astype(jnp.bfloat16), values_ref[:, lanes], preferred_element_type=jnp.float32
        )
        mixed_ref[:, lanes] = (mixture / totals).astype(mixed_ref.dtype)
    o_ref[...] = jnp.dot(mixed_ref[...], wo_ref[...], preferred_element_type=jnp.float32).astype(
        o_ref.dtype
    )


def cross_partial(owner_cross, cross_wq, cross_q_gain, keys_own, values_own, length, cross_wo):
    token_total, model_width = owner_cross.shape
    group_width = cross_wq.shape[1]
    text = keys_own.shape[0]
    vmem = pl.BlockSpec(memory_space=pltpu.VMEM)
    return pl.pallas_call(
        _cross_kernel,
        in_specs=[pl.BlockSpec(memory_space=pltpu.SMEM)] + [vmem] * 6,
        out_specs=vmem,
        out_shape=jax.ShapeDtypeStruct((token_total, model_width), jnp.bfloat16),
        scratch_shapes=[pltpu.VMEM((token_total, group_width), jnp.bfloat16)],
        cost_estimate=pl.CostEstimate(
            flops=4 * token_total * model_width * group_width + 4 * token_total * text * group_width,
            bytes_accessed=4 * model_width * group_width + 4 * text * group_width
            + 4 * token_total * model_width,
            transcendentals=token_total * text * (group_width // HEAD_DIM),
        ),
    )(length, owner_cross, cross_wq, cross_q_gain.reshape(1, group_width), keys_own, values_own, cross_wo)


def _qkv_kernel(x_ref, wq_ref, wk_ref, wv_ref, cos_ref, sin_ref, gain_ref, o_ref):
    block_in = x_ref[...]
    cosine = cos_ref[...]
    sine_signed = sin_ref[...]
    group_width = wq_ref.shape[1]
    for section, w_ref in enumerate((wq_ref, wk_ref, wv_ref)):
        projected = jnp.dot(block_in, w_ref[...], preferred_element_type=jnp.float32)
        if section < 2:
            gains = gain_ref[section : section + 1, :]
            parts = []
            for head in range(group_width // HEAD_DIM):
                lanes = slice(head * HEAD_DIM, (head + 1) * HEAD_DIM)
                piece = projected[:, lanes]
                mean_square = jnp.mean(piece * piece, axis=-1, keepdims=True)
                normed = piece * lax.rsqrt(mean_square + EPSILON) * gains[:, lanes]
                swapped = pltpu.roll(normed, HEAD_DIM // 2, 1)
                parts.append(normed * cosine + swapped * sine_signed)
            projected = jnp.concatenate(parts, axis=-1)
        o_ref[0, :, section * group_width : (section + 1) * group_width] = projected.astype(
            o_ref.dtype
        )


def pack_projected(block_in, cell_map, w_qkv, self_q_gain, self_k_gain, head_count):
    videos, per_video, model_width = block_in.shape
    rows = block_in.reshape(-1, model_width)
    token_total = rows.shape[0]
    group_width = model_width // head_count
    angles = rope_angles(cell_map).reshape(token_total, HEAD_DIM // 2)
    cosine = jnp.cos(angles)
    sine = jnp.sin(angles)
    cos_full = jnp.concatenate([cosine, cosine], axis=-1)
    sin_signed = jnp.concatenate([-sine, sine], axis=-1)
    gains = jnp.stack([self_q_gain, self_k_gain])
    whole = lambda g: (0, 0)
    packed = pl.pallas_call(
        _qkv_kernel,
        grid=(head_count,),
        in_specs=[
            pl.BlockSpec((token_total, model_width), whole),
            pl.BlockSpec((model_width, group_width), lambda g: (0, g)),
            pl.BlockSpec((model_width, group_width), lambda g: (0, head_count + g)),
            pl.BlockSpec((model_width, group_width), lambda g: (0, 2 * head_count + g)),
            pl.BlockSpec((token_total, HEAD_DIM), whole),
            pl.BlockSpec((token_total, HEAD_DIM), whole),
            pl.BlockSpec((2, group_width), lambda g: (0, g)),
        ],
        out_specs=pl.BlockSpec((1, token_total, 3 * group_width), lambda g: (g, 0, 0)),
        out_shape=jax.ShapeDtypeStruct((head_count, token_total, 3 * group_width), jnp.bfloat16),
        cost_estimate=pl.CostEstimate(
            flops=2 * token_total * model_width * 3 * model_width,
            bytes_accessed=2 * model_width * 3 * model_width + 4 * token_total * 3 * model_width,
            transcendentals=0,
        ),
    )(rows, w_qkv, w_qkv, w_qkv, cos_full, sin_signed, gains)
    return packed.reshape(head_count, videos, per_video, 3 * group_width)


def local(
    hidden,
    latent,
    cell_map,
    text_lengths,
    block_modulation,
    head_modulation,
    step_sizes,
    w_qkv,
    self_q_gain,
    self_k_gain,
    w_out,
    cross_gain,
    cross_wq,
    cross_q_gain,
    text_keys,
    text_values,
    cross_wo,
    head_w,
):
    head_count = lax.axis_size("head")
    tile_count = lax.axis_size("tile")
    videos, per_video, model_width = hidden.shape
    group_heads = HEADS // head_count
    group_width = group_heads * HEAD_DIM
    stream = hidden.astype(jnp.float32)
    block_shift = block_modulation[:, 0][:, None, :]
    block_scale = block_modulation[:, 1][:, None, :]
    block_gate = block_modulation[:, 2][:, None, :]
    block_in = (layer_norm(stream) * (1.0 + block_scale) + block_shift).astype(jnp.bfloat16)
    packed = pack_projected(block_in, cell_map, w_qkv, self_q_gain, self_k_gain, head_count)
    arrived = lax.all_to_all(
        packed.reshape(head_count * videos, per_video, 3 * group_width),
        ("head", "tile"),
        split_axis=0,
        concat_axis=0,
        tiled=True,
    )
    own_mixture = attend_self(arrived.reshape(-1, 3 * group_width), group_width)
    returned = lax.all_to_all(
        own_mixture.reshape(head_count * tile_count, per_video, group_width),
        ("head", "tile"),
        split_axis=0,
        concat_axis=0,
        tiled=True,
    )
    attended = (
        returned.reshape(head_count, videos, per_video, group_width)
        .transpose(1, 2, 0, 3)
        .reshape(videos * per_video, model_width)
    )
    self_update = jnp.dot(attended, w_out, preferred_element_type=jnp.float32).reshape(
        videos, per_video, model_width
    )
    after_self = stream + block_gate * self_update
    cross_in = (layer_norm(after_self) * cross_gain).astype(jnp.bfloat16)
    copies = jnp.broadcast_to(cross_in[None], (head_count,) + cross_in.shape).reshape(
        head_count * videos, per_video, model_width
    )
    owner_cross = lax.all_to_all(copies, ("head", "tile"), split_axis=0, concat_axis=0, tiled=True)
    owner_cross = owner_cross.reshape(-1, model_width)
    partial = cross_partial(
        owner_cross, cross_wq, cross_q_gain, text_keys[0], text_values[0], text_lengths, cross_wo
    )
    returned_partials = lax.all_to_all(
        partial.reshape(head_count * tile_count, per_video, model_width),
        ("head", "tile"),
        split_axis=0,
        concat_axis=0,
        tiled=True,
    ).reshape(head_count, videos, per_video, model_width)
    returned_cross = jnp.sum(returned_partials.astype(jnp.float32), axis=0).astype(jnp.bfloat16)
    after_cross = after_self + returned_cross.astype(jnp.float32)
    hidden_next = after_cross.astype(jnp.bfloat16)
    head_shift = head_modulation[:, 0][:, None, :]
    head_scale = head_modulation[:, 1][:, None, :]
    head_in = (layer_norm(after_cross) * (1.0 + head_scale) + head_shift).astype(jnp.bfloat16)
    velocity = jnp.dot(
        head_in.reshape(-1, model_width), head_w, preferred_element_type=jnp.float32
    ).reshape(videos, per_video, -1)
    latent_next = latent + step_sizes[:, None, None] * velocity
    return (hidden_next, latent_next)


def solution(mesh):
    return jax.shard_map(
        local,
        mesh=mesh,
        in_specs=(
            P(None, ("head", "tile"), None),
            P(None, ("head", "tile"), None),
            P(None, ("head", "tile")),
            P("tile"),
            P(),
            P(),
            P(),
            P(),
            P(),
            P(),
            P(),
            P(),
            P(None, "head"),
            P("head"),
            P("tile", None, "head"),
            P("tile", None, "head"),
            P("head", None),
            P(),
        ),
        out_specs=(P(None, ("head", "tile"), None), P(None, ("head", "tile"), None)),
        check_vma=False,
    )
```

```python
import math

import jax
import jax.numpy as jnp
from jax import lax
from jax.experimental import pallas as pl
from jax.experimental.pallas import tpu as pltpu
from jax.sharding import PartitionSpec as P

HEADS = 12
HEAD_DIM = 128
GRID_H = 24
GRID_W = 8


EPSILON = 1e-06


def layer_norm(inputs):
    average = jnp.mean(inputs, axis=-1, keepdims=True)
    centred = inputs - average
    variance = jnp.mean(centred * centred, axis=-1, keepdims=True)
    return centred * lax.rsqrt(variance + EPSILON)


def head_norm(inputs, gain_table):
    mean_square = jnp.mean(inputs * inputs, axis=-1, keepdims=True)
    return inputs * lax.rsqrt(mean_square + EPSILON) * gain_table


def frequencies(pair_count):
    return jnp.power(10000.0, -jnp.arange(pair_count, dtype=jnp.float32) / pair_count)


def rope_angles(cell_ids):
    sixth_part = HEAD_DIM // 6
    time_pairs = HEAD_DIM // 2 - 2 * sixth_part
    plane_cells = GRID_H * GRID_W
    frame_index = (cell_ids // plane_cells).astype(jnp.float32)
    row_index = (cell_ids // GRID_W % GRID_H).astype(jnp.float32)
    column = (cell_ids % GRID_W).astype(jnp.float32)
    return jnp.concatenate(
        [
            frame_index[..., None] * frequencies(time_pairs),
            row_index[..., None] * frequencies(sixth_part),
            column[..., None] * frequencies(sixth_part),
        ],
        axis=-1,
    )


def rotate(inputs, angles):
    half_dim = inputs.shape[-1] // 2
    cosine = jnp.cos(angles)[..., None, :]
    sine_part = jnp.sin(angles)[..., None, :]
    lower_half = inputs[..., :half_dim]
    upper_half = inputs[..., half_dim:]
    return jnp.concatenate(
        [
            lower_half * cosine - upper_half * sine_part,
            lower_half * sine_part + upper_half * cosine,
        ],
        axis=-1,
    )


def _self_attention_kernel(x_ref, o_ref):
    group_width = o_ref.shape[1]
    factor = 1.0 / math.sqrt(HEAD_DIM)
    for head in range(group_width // HEAD_DIM):
        lanes = slice(head * HEAD_DIM, (head + 1) * HEAD_DIM)
        queries = x_ref[:, head * HEAD_DIM : (head + 1) * HEAD_DIM]
        keys = x_ref[:, group_width + head * HEAD_DIM : group_width + (head + 1) * HEAD_DIM]
        values = x_ref[:, 2 * group_width + head * HEAD_DIM : 2 * group_width + (head + 1) * HEAD_DIM]
        scores = (
            lax.dot_general(
                queries, keys, (((1,), (1,)), ((), ())), preferred_element_type=jnp.float32
            )
            * factor
        )
        weights = jnp.exp(scores)
        totals = jnp.sum(weights, axis=-1, keepdims=True)
        mixture = jnp.dot(
            weights.astype(jnp.bfloat16), values, preferred_element_type=jnp.float32
        )
        o_ref[:, lanes] = (mixture / totals).astype(o_ref.dtype)


def attend_self(arrived, group_width):
    token_total = arrived.shape[0]
    return pl.pallas_call(
        _self_attention_kernel,
        out_shape=jax.ShapeDtypeStruct((token_total, group_width), jnp.bfloat16),
        cost_estimate=pl.CostEstimate(
            flops=4 * token_total * token_total * group_width,
            bytes_accessed=2 * token_total * 4 * group_width,
            transcendentals=token_total * token_total * (group_width // HEAD_DIM),
        ),
    )(arrived)


def _cross_kernel(length_ref, q_ref, keys_ref, values_ref, wo_ref, o_ref, mixed_ref):
    factor = 1.0 / math.sqrt(HEAD_DIM)
    group_width = q_ref.shape[1]
    text = keys_ref.shape[0]
    live = (lax.broadcasted_iota(jnp.int32, (1, text), 1) < length_ref[0]).astype(jnp.float32)
    for head in range(group_width // HEAD_DIM):
        lanes = slice(head * HEAD_DIM, (head + 1) * HEAD_DIM)
        scores = (
            lax.dot_general(
                q_ref[:, lanes], keys_ref[:, lanes], (((1,), (1,)), ((), ())),
                preferred_element_type=jnp.float32,
            )
            * factor
        )
        weights = jnp.exp(scores) * live
        totals = jnp.sum(weights, axis=-1, keepdims=True)
        mixture = jnp.dot(
            weights.astype(jnp.bfloat16), values_ref[:, lanes], preferred_element_type=jnp.float32
        )
        mixed_ref[:, lanes] = (mixture / totals).astype(mixed_ref.dtype)
    o_ref[...] = jnp.dot(mixed_ref[...], wo_ref[...], preferred_element_type=jnp.float32).astype(
        o_ref.dtype
    )


def cross_partial(queries, keys_own, values_own, length, cross_wo):
    token_total, group_width = queries.shape
    model_width = cross_wo.shape[1]
    text = keys_own.shape[0]
    vmem = pl.BlockSpec(memory_space=pltpu.VMEM)
    return pl.pallas_call(
        _cross_kernel,
        in_specs=[pl.BlockSpec(memory_space=pltpu.SMEM)] + [vmem] * 4,
        out_specs=vmem,
        out_shape=jax.ShapeDtypeStruct((token_total, model_width), jnp.bfloat16),
        scratch_shapes=[pltpu.VMEM((token_total, group_width), jnp.bfloat16)],
        cost_estimate=pl.CostEstimate(
            flops=2 * token_total * model_width * group_width + 4 * token_total * text * group_width,
            bytes_accessed=2 * model_width * group_width + 4 * text * group_width
            + 2 * token_total * (model_width + group_width),
            transcendentals=token_total * text * (group_width // HEAD_DIM),
        ),
    )(length, queries, keys_own, values_own, cross_wo)


def gather_over_head(shard, head_count):
    pieces = [shard]
    for shift in range(1, head_count):
        pieces.append(
            lax.ppermute(shard, "head", [(i, (i + shift) % head_count) for i in range(head_count)])
        )
    return pieces


def _qkv_kernel(x_ref, wq_ref, wk_ref, wv_ref, cos_ref, sin_ref, gain_ref, o_ref):
    block_in = x_ref[...]
    cosine = cos_ref[...]
    sine_signed = sin_ref[...]
    group_width = wq_ref.shape[1]
    for section, w_ref in enumerate((wq_ref, wk_ref, wv_ref)):
        projected = jnp.dot(block_in, w_ref[...], preferred_element_type=jnp.float32)
        if section < 2:
            gains = gain_ref[section : section + 1, :]
            parts = []
            for head in range(group_width // HEAD_DIM):
                lanes = slice(head * HEAD_DIM, (head + 1) * HEAD_DIM)
                piece = projected[:, lanes]
                mean_square = jnp.mean(piece * piece, axis=-1, keepdims=True)
                normed = piece * lax.rsqrt(mean_square + EPSILON) * gains[:, lanes]
                swapped = pltpu.roll(normed, HEAD_DIM // 2, 1)
                parts.append(normed * cosine + swapped * sine_signed)
            projected = jnp.concatenate(parts, axis=-1)
        o_ref[0, :, section * group_width : (section + 1) * group_width] = projected.astype(
            o_ref.dtype
        )


def pack_projected(block_in, cell_map, w_qkv, self_q_gain, self_k_gain, head_count):
    videos, per_video, model_width = block_in.shape
    rows = block_in.reshape(-1, model_width)
    token_total = rows.shape[0]
    group_width = model_width // head_count
    angles = rope_angles(cell_map).reshape(token_total, HEAD_DIM // 2)
    cosine = jnp.cos(angles)
    sine = jnp.sin(angles)
    cos_full = jnp.concatenate([cosine, cosine], axis=-1)
    sin_signed = jnp.concatenate([-sine, sine], axis=-1)
    gains = jnp.stack([self_q_gain, self_k_gain])
    whole = lambda g: (0, 0)
    packed = pl.pallas_call(
        _qkv_kernel,
        grid=(head_count,),
        in_specs=[
            pl.BlockSpec((token_total, model_width), whole),
            pl.BlockSpec((model_width, group_width), lambda g: (0, g)),
            pl.BlockSpec((model_width, group_width), lambda g: (0, head_count + g)),
            pl.BlockSpec((model_width, group_width), lambda g: (0, 2 * head_count + g)),
            pl.BlockSpec((token_total, HEAD_DIM), whole),
            pl.BlockSpec((token_total, HEAD_DIM), whole),
            pl.BlockSpec((2, group_width), lambda g: (0, g)),
        ],
        out_specs=pl.BlockSpec((1, token_total, 3 * group_width), lambda g: (g, 0, 0)),
        out_shape=jax.ShapeDtypeStruct((head_count, token_total, 3 * group_width), jnp.bfloat16),
        cost_estimate=pl.CostEstimate(
            flops=2 * token_total * model_width * 3 * model_width,
            bytes_accessed=2 * model_width * 3 * model_width + 4 * token_total * 3 * model_width,
            transcendentals=0,
        ),
    )(rows, w_qkv, w_qkv, w_qkv, cos_full, sin_signed, gains)
    return packed.reshape(head_count, videos, per_video, 3 * group_width)


def local(
    hidden,
    latent,
    cell_map,
    text_lengths,
    block_modulation,
    head_modulation,
    step_sizes,
    w_qkv,
    self_q_gain,
    self_k_gain,
    w_out,
    cross_gain,
    cross_wq,
    cross_q_gain,
    text_keys,
    text_values,
    cross_wo,
    head_w,
):
    head_count = lax.axis_size("head")
    tile_count = lax.axis_size("tile")
    videos, per_video, model_width = hidden.shape
    group_heads = HEADS // head_count
    group_width = group_heads * HEAD_DIM
    weight_pieces = gather_over_head(cross_wq, head_count)
    gain_pieces = gather_over_head(cross_q_gain, head_count)
    stream = hidden.astype(jnp.float32)
    block_shift = block_modulation[:, 0][:, None, :]
    block_scale = block_modulation[:, 1][:, None, :]
    block_gate = block_modulation[:, 2][:, None, :]
    block_in = (layer_norm(stream) * (1.0 + block_scale) + block_shift).astype(jnp.bfloat16)
    packed = pack_projected(block_in, cell_map, w_qkv, self_q_gain, self_k_gain, head_count)
    arrived = lax.all_to_all(
        packed.reshape(head_count * videos, per_video, 3 * group_width),
        ("head", "tile"),
        split_axis=0,
        concat_axis=0,
        tiled=True,
    )
    own_mixture = attend_self(arrived.reshape(-1, 3 * group_width), group_width)
    returned = lax.all_to_all(
        own_mixture.reshape(head_count * tile_count, per_video, group_width),
        ("head", "tile"),
        split_axis=0,
        concat_axis=0,
        tiled=True,
    )
    attended = (
        returned.reshape(head_count, videos, per_video, group_width)
        .transpose(1, 2, 0, 3)
        .reshape(videos * per_video, model_width)
    )
    self_update = jnp.dot(attended, w_out, preferred_element_type=jnp.float32).reshape(
        videos, per_video, model_width
    )
    after_self = stream + block_gate * self_update
    cross_in = (layer_norm(after_self) * cross_gain).astype(jnp.bfloat16)
    token_rows = cross_in.reshape(-1, model_width)
    query_blocks = []
    for weight_piece, gain_piece in zip(weight_pieces, gain_pieces):
        block = jnp.dot(token_rows, weight_piece, preferred_element_type=jnp.float32)
        block = head_norm(block.reshape(-1, group_heads, HEAD_DIM), gain_piece.reshape(group_heads, HEAD_DIM))
        query_blocks.append(block.astype(jnp.bfloat16).reshape(videos, per_video, group_width))
    by_shift = jnp.stack([query_blocks[(-g) % head_count] for g in range(head_count)])
    head_index = lax.axis_index("head")
    by_group = jnp.roll(by_shift, head_index, axis=0)
    owner_queries = lax.all_to_all(
        by_group.reshape(head_count * videos, per_video, group_width),
        ("head", "tile"),
        split_axis=0,
        concat_axis=0,
        tiled=True,
    ).reshape(-1, group_width)
    partial = cross_partial(owner_queries, text_keys[0], text_values[0], text_lengths, cross_wo)
    returned_partials = lax.all_to_all(
        partial.reshape(head_count * tile_count, per_video, model_width),
        ("head", "tile"),
        split_axis=0,
        concat_axis=0,
        tiled=True,
    ).reshape(head_count, videos, per_video, model_width)
    returned_cross = jnp.sum(returned_partials.astype(jnp.float32), axis=0).astype(jnp.bfloat16)
    after_cross = after_self + returned_cross.astype(jnp.float32)
    hidden_next = after_cross.astype(jnp.bfloat16)
    head_shift = head_modulation[:, 0][:, None, :]
    head_scale = head_modulation[:, 1][:, None, :]
    head_in = (layer_norm(after_cross) * (1.0 + head_scale) + head_shift).astype(jnp.bfloat16)
    velocity = jnp.dot(
        head_in.reshape(-1, model_width), head_w, preferred_element_type=jnp.float32
    ).reshape(videos, per_video, -1)
    latent_next = latent + step_sizes[:, None, None] * velocity
    return (hidden_next, latent_next)


def solution(mesh):
    return jax.shard_map(
        local,
        mesh=mesh,
        in_specs=(
            P(None, ("head", "tile"), None),
            P(None, ("head", "tile"), None),
            P(None, ("head", "tile")),
            P("tile"),
            P(),
            P(),
            P(),
            P(),
            P(),
            P(),
            P(),
            P(),
            P(None, "head"),
            P("head"),
            P("tile", None, "head"),
            P("tile", None, "head"),
            P("head", None),
            P(),
        ),
        out_specs=(P(None, ("head", "tile"), None), P(None, ("head", "tile"), None)),
        check_vma=False,
    )
```

```python
import math

import jax
import jax.numpy as jnp
from jax import lax
from jax.experimental import pallas as pl
from jax.experimental.pallas import tpu as pltpu
from jax.sharding import PartitionSpec as P

HEADS = 12
HEAD_DIM = 128
GRID_H = 24
GRID_W = 8


EPSILON = 1e-06


def layer_norm(inputs):
    average = jnp.mean(inputs, axis=-1, keepdims=True)
    centred = inputs - average
    variance = jnp.mean(centred * centred, axis=-1, keepdims=True)
    return centred * lax.rsqrt(variance + EPSILON)


def head_norm(inputs, gain_table):
    mean_square = jnp.mean(inputs * inputs, axis=-1, keepdims=True)
    return inputs * lax.rsqrt(mean_square + EPSILON) * gain_table


def frequencies(pair_count):
    return jnp.power(10000.0, -jnp.arange(pair_count, dtype=jnp.float32) / pair_count)


def rope_angles(cell_ids):
    sixth_part = HEAD_DIM // 6
    time_pairs = HEAD_DIM // 2 - 2 * sixth_part
    plane_cells = GRID_H * GRID_W
    frame_index = (cell_ids // plane_cells).astype(jnp.float32)
    row_index = (cell_ids // GRID_W % GRID_H).astype(jnp.float32)
    column = (cell_ids % GRID_W).astype(jnp.float32)
    return jnp.concatenate(
        [
            frame_index[..., None] * frequencies(time_pairs),
            row_index[..., None] * frequencies(sixth_part),
            column[..., None] * frequencies(sixth_part),
        ],
        axis=-1,
    )


def rotate(inputs, angles):
    half_dim = inputs.shape[-1] // 2
    cosine = jnp.cos(angles)[..., None, :]
    sine_part = jnp.sin(angles)[..., None, :]
    lower_half = inputs[..., :half_dim]
    upper_half = inputs[..., half_dim:]
    return jnp.concatenate(
        [
            lower_half * cosine - upper_half * sine_part,
            lower_half * sine_part + upper_half * cosine,
        ],
        axis=-1,
    )


def _self_attention_kernel(x_ref, o_ref):
    group_width = o_ref.shape[1]
    factor = 1.0 / math.sqrt(HEAD_DIM)
    for head in range(group_width // HEAD_DIM):
        lanes = slice(head * HEAD_DIM, (head + 1) * HEAD_DIM)
        queries = x_ref[:, head * HEAD_DIM : (head + 1) * HEAD_DIM]
        keys = x_ref[:, group_width + head * HEAD_DIM : group_width + (head + 1) * HEAD_DIM]
        values = x_ref[:, 2 * group_width + head * HEAD_DIM : 2 * group_width + (head + 1) * HEAD_DIM]
        scores = (
            lax.dot_general(
                queries, keys, (((1,), (1,)), ((), ())), preferred_element_type=jnp.float32
            )
            * factor
        )
        weights = jnp.exp(scores)
        totals = jnp.sum(weights, axis=-1, keepdims=True)
        mixture = jnp.dot(
            weights.astype(jnp.bfloat16), values, preferred_element_type=jnp.float32
        )
        o_ref[:, lanes] = (mixture / totals).astype(o_ref.dtype)


def attend_self(arrived, group_width):
    token_total = arrived.shape[0]
    return pl.pallas_call(
        _self_attention_kernel,
        out_shape=jax.ShapeDtypeStruct((token_total, group_width), jnp.bfloat16),
        cost_estimate=pl.CostEstimate(
            flops=4 * token_total * token_total * group_width,
            bytes_accessed=2 * token_total * 4 * group_width,
            transcendentals=token_total * token_total * (group_width // HEAD_DIM),
        ),
    )(arrived)


def _cross_kernel(length_ref, x_ref, wq_ref, gain_ref, keys_ref, values_ref, wo_ref, o_ref, mixed_ref):
    factor = 1.0 / math.sqrt(HEAD_DIM)
    group_width = wq_ref.shape[1]
    text = keys_ref.shape[0]
    projected = jnp.dot(x_ref[...], wq_ref[...], preferred_element_type=jnp.float32)
    gains = gain_ref[...]
    live = (lax.broadcasted_iota(jnp.int32, (1, text), 1) < length_ref[0]).astype(jnp.float32)
    for head in range(group_width // HEAD_DIM):
        lanes = slice(head * HEAD_DIM, (head + 1) * HEAD_DIM)
        piece = projected[:, lanes]
        mean_square = jnp.mean(piece * piece, axis=-1, keepdims=True)
        queries = (piece * lax.rsqrt(mean_square + EPSILON) * gains[:, lanes]).astype(jnp.bfloat16)
        scores = (
            lax.dot_general(
                queries, keys_ref[:, lanes], (((1,), (1,)), ((), ())),
                preferred_element_type=jnp.float32,
            )
            * factor
        )
        weights = jnp.exp(scores) * live
        totals = jnp.sum(weights, axis=-1, keepdims=True)
        mixture = jnp.dot(
            weights.astype(jnp.bfloat16), values_ref[:, lanes], preferred_element_type=jnp.float32
        )
        mixed_ref[:, lanes] = (mixture / totals).astype(mixed_ref.dtype)
    o_ref[...] = jnp.dot(mixed_ref[...], wo_ref[...], preferred_element_type=jnp.float32).astype(
        o_ref.dtype
    )


def cross_partial(owner_cross, cross_wq, cross_q_gain, keys_own, values_own, length, cross_wo):
    token_total, model_width = owner_cross.shape
    group_width = cross_wq.shape[1]
    text = keys_own.shape[0]
    vmem = pl.BlockSpec(memory_space=pltpu.VMEM)
    return pl.pallas_call(
        _cross_kernel,
        in_specs=[pl.BlockSpec(memory_space=pltpu.SMEM)] + [vmem] * 6,
        out_specs=vmem,
        out_shape=jax.ShapeDtypeStruct((token_total, model_width), jnp.bfloat16),
        scratch_shapes=[pltpu.VMEM((token_total, group_width), jnp.bfloat16)],
        cost_estimate=pl.CostEstimate(
            flops=4 * token_total * model_width * group_width + 4 * token_total * text * group_width,
            bytes_accessed=4 * model_width * group_width + 4 * text * group_width
            + 4 * token_total * model_width,
            transcendentals=token_total * text * (group_width // HEAD_DIM),
        ),
    )(length, owner_cross, cross_wq, cross_q_gain.reshape(1, group_width), keys_own, values_own, cross_wo)


def _qkv_kernel(
    hidden_ref, modulation_ref, wq_ref, wk_ref, wv_ref, cos_ref, sin_ref, gain_ref, o_ref, normed_ref
):
    group = pl.program_id(0)
    videos, per_video, _ = hidden_ref.shape

    @pl.when(group == 0)
    def _():
        shift = modulation_ref[:, 0, :]
        scale = 1.0 + modulation_ref[:, 1, :]
        for slot in range(per_video):
            stream = hidden_ref[:, slot, :].astype(jnp.float32)
            normed_ref[slot * videos : (slot + 1) * videos, :] = (
                layer_norm(stream) * scale + shift
            ).astype(normed_ref.dtype)

    block_in = normed_ref[...]
    cosine = cos_ref[...]
    sine_signed = sin_ref[...]
    group_width = wq_ref.shape[1]
    for section, w_ref in enumerate((wq_ref, wk_ref, wv_ref)):
        projected = jnp.dot(block_in, w_ref[...], preferred_element_type=jnp.float32)
        if section < 2:
            gains = gain_ref[section : section + 1, :]
            parts = []
            for head in range(group_width // HEAD_DIM):
                lanes = slice(head * HEAD_DIM, (head + 1) * HEAD_DIM)
                piece = projected[:, lanes]
                mean_square = jnp.mean(piece * piece, axis=-1, keepdims=True)
                normed = piece * lax.rsqrt(mean_square + EPSILON) * gains[:, lanes]
                swapped = pltpu.roll(normed, HEAD_DIM // 2, 1)
                parts.append(normed * cosine + swapped * sine_signed)
            projected = jnp.concatenate(parts, axis=-1)
        o_ref[0, :, section * group_width : (section + 1) * group_width] = projected.astype(
            o_ref.dtype
        )


def pack_projected(hidden, block_modulation, cell_map, w_qkv, self_q_gain, self_k_gain, head_count):
    videos, per_video, model_width = hidden.shape
    token_total = videos * per_video
    group_width = model_width // head_count
    angles = rope_angles(jnp.transpose(cell_map, (1, 0))).reshape(token_total, HEAD_DIM // 2)
    cosine = jnp.cos(angles)
    sine = jnp.sin(angles)
    cos_full = jnp.concatenate([cosine, cosine], axis=-1)
    sin_signed = jnp.concatenate([-sine, sine], axis=-1)
    gains = jnp.stack([self_q_gain, self_k_gain])
    whole2 = lambda g: (0, 0)
    whole3 = lambda g: (0, 0, 0)
    packed = pl.pallas_call(
        _qkv_kernel,
        grid=(head_count,),
        in_specs=[
            pl.BlockSpec(hidden.shape, whole3),
            pl.BlockSpec(block_modulation.shape, whole3),
            pl.BlockSpec((model_width, group_width), lambda g: (0, g)),
            pl.BlockSpec((model_width, group_width), lambda g: (0, head_count + g)),
            pl.BlockSpec((model_width, group_width), lambda g: (0, 2 * head_count + g)),
            pl.BlockSpec((token_total, HEAD_DIM), whole2),
            pl.BlockSpec((token_total, HEAD_DIM), whole2),
            pl.BlockSpec((2, group_width), lambda g: (0, g)),
        ],
        out_specs=pl.BlockSpec((1, token_total, 3 * group_width), lambda g: (g, 0, 0)),
        out_shape=jax.ShapeDtypeStruct((head_count, token_total, 3 * group_width), jnp.bfloat16),
        scratch_shapes=[pltpu.VMEM((token_total, model_width), jnp.bfloat16)],
        cost_estimate=pl.CostEstimate(
            flops=2 * token_total * model_width * 3 * model_width,
            bytes_accessed=2 * model_width * 3 * model_width + 4 * token_total * 3 * model_width,
            transcendentals=0,
        ),
    )(hidden, block_modulation, w_qkv, w_qkv, w_qkv, cos_full, sin_signed, gains)
    packed = packed.reshape(head_count, per_video, videos, 3 * group_width)
    return jnp.transpose(packed, (0, 2, 1, 3))


def local(
    hidden,
    latent,
    cell_map,
    text_lengths,
    block_modulation,
    head_modulation,
    step_sizes,
    w_qkv,
    self_q_gain,
    self_k_gain,
    w_out,
    cross_gain,
    cross_wq,
    cross_q_gain,
    text_keys,
    text_values,
    cross_wo,
    head_w,
):
    head_count = lax.axis_size("head")
    tile_count = lax.axis_size("tile")
    videos, per_video, model_width = hidden.shape
    group_heads = HEADS // head_count
    group_width = group_heads * HEAD_DIM
    stream = hidden.astype(jnp.float32)
    block_gate = block_modulation[:, 2][:, None, :]
    packed = pack_projected(
        hidden, block_modulation, cell_map, w_qkv, self_q_gain, self_k_gain, head_count
    )
    arrived = lax.all_to_all(
        packed.reshape(head_count * videos, per_video, 3 * group_width),
        ("head", "tile"),
        split_axis=0,
        concat_axis=0,
        tiled=True,
    )
    own_mixture = attend_self(arrived.reshape(-1, 3 * group_width), group_width)
    returned = lax.all_to_all(
        own_mixture.reshape(head_count * tile_count, per_video, group_width),
        ("head", "tile"),
        split_axis=0,
        concat_axis=0,
        tiled=True,
    )
    attended = (
        returned.reshape(head_count, videos, per_video, group_width)
        .transpose(1, 2, 0, 3)
        .reshape(videos * per_video, model_width)
    )
    self_update = jnp.dot(attended, w_out, preferred_element_type=jnp.float32).reshape(
        videos, per_video, model_width
    )
    after_self = stream + block_gate * self_update
    cross_in = (layer_norm(after_self) * cross_gain).astype(jnp.bfloat16)
    copies = jnp.broadcast_to(cross_in[None], (head_count,) + cross_in.shape).reshape(
        head_count * videos, per_video, model_width
    )
    owner_cross = lax.all_to_all(copies, ("head", "tile"), split_axis=0, concat_axis=0, tiled=True)
    owner_cross = owner_cross.reshape(-1, model_width)
    partial = cross_partial(
        owner_cross, cross_wq, cross_q_gain, text_keys[0], text_values[0], text_lengths, cross_wo
    )
    returned_partials = lax.all_to_all(
        partial.reshape(head_count * tile_count, per_video, model_width),
        ("head", "tile"),
        split_axis=0,
        concat_axis=0,
        tiled=True,
    ).reshape(head_count, videos, per_video, model_width)
    returned_cross = jnp.sum(returned_partials.astype(jnp.float32), axis=0).astype(jnp.bfloat16)
    after_cross = after_self + returned_cross.astype(jnp.float32)
    hidden_next = after_cross.astype(jnp.bfloat16)
    head_shift = head_modulation[:, 0][:, None, :]
    head_scale = head_modulation[:, 1][:, None, :]
    head_in = (layer_norm(after_cross) * (1.0 + head_scale) + head_shift).astype(jnp.bfloat16)
    velocity = jnp.dot(
        head_in.reshape(-1, model_width), head_w, preferred_element_type=jnp.float32
    ).reshape(videos, per_video, -1)
    latent_next = latent + step_sizes[:, None, None] * velocity
    return (hidden_next, latent_next)


def solution(mesh):
    return jax.shard_map(
        local,
        mesh=mesh,
        in_specs=(
            P(None, ("head", "tile"), None),
            P(None, ("head", "tile"), None),
            P(None, ("head", "tile")),
            P("tile"),
            P(),
            P(),
            P(),
            P(),
            P(),
            P(),
            P(),
            P(),
            P(None, "head"),
            P("head"),
            P("tile", None, "head"),
            P("tile", None, "head"),
            P("head", None),
            P(),
        ),
        out_specs=(P(None, ("head", "tile"), None), P(None, ("head", "tile"), None)),
        check_vma=False,
    )
```

```python
import math

import jax
import jax.numpy as jnp
from jax import lax
from jax.experimental import pallas as pl
from jax.experimental.pallas import tpu as pltpu
from jax.sharding import PartitionSpec as P

HEADS = 12
HEAD_DIM = 128
GRID_H = 24
GRID_W = 8


EPSILON = 1e-06


def layer_norm(inputs):
    average = jnp.mean(inputs, axis=-1, keepdims=True)
    centred = inputs - average
    variance = jnp.mean(centred * centred, axis=-1, keepdims=True)
    return centred * lax.rsqrt(variance + EPSILON)


def head_norm(inputs, gain_table):
    mean_square = jnp.mean(inputs * inputs, axis=-1, keepdims=True)
    return inputs * lax.rsqrt(mean_square + EPSILON) * gain_table


def frequencies(pair_count):
    return jnp.power(10000.0, -jnp.arange(pair_count, dtype=jnp.float32) / pair_count)


def rope_angles(cell_ids):
    sixth_part = HEAD_DIM // 6
    time_pairs = HEAD_DIM // 2 - 2 * sixth_part
    plane_cells = GRID_H * GRID_W
    frame_index = (cell_ids // plane_cells).astype(jnp.float32)
    row_index = (cell_ids // GRID_W % GRID_H).astype(jnp.float32)
    column = (cell_ids % GRID_W).astype(jnp.float32)
    return jnp.concatenate(
        [
            frame_index[..., None] * frequencies(time_pairs),
            row_index[..., None] * frequencies(sixth_part),
            column[..., None] * frequencies(sixth_part),
        ],
        axis=-1,
    )


def rotate(inputs, angles):
    half_dim = inputs.shape[-1] // 2
    cosine = jnp.cos(angles)[..., None, :]
    sine_part = jnp.sin(angles)[..., None, :]
    lower_half = inputs[..., :half_dim]
    upper_half = inputs[..., half_dim:]
    return jnp.concatenate(
        [
            lower_half * cosine - upper_half * sine_part,
            lower_half * sine_part + upper_half * cosine,
        ],
        axis=-1,
    )


def _self_attention_kernel(x_ref, o_ref):
    group_width = o_ref.shape[1]
    factor = 1.0 / math.sqrt(HEAD_DIM)
    for head in range(group_width // HEAD_DIM):
        lanes = slice(head * HEAD_DIM, (head + 1) * HEAD_DIM)
        queries = x_ref[:, head * HEAD_DIM : (head + 1) * HEAD_DIM]
        keys = x_ref[:, group_width + head * HEAD_DIM : group_width + (head + 1) * HEAD_DIM]
        values = x_ref[:, 2 * group_width + head * HEAD_DIM : 2 * group_width + (head + 1) * HEAD_DIM]
        scores = (
            lax.dot_general(
                queries, keys, (((1,), (1,)), ((), ())), preferred_element_type=jnp.float32
            )
            * factor
        )
        weights = jnp.exp(scores)
        totals = jnp.sum(weights, axis=-1, keepdims=True)
        mixture = jnp.dot(
            weights.astype(jnp.bfloat16), values, preferred_element_type=jnp.float32
        )
        o_ref[:, lanes] = (mixture / totals).astype(o_ref.dtype)


def attend_self(arrived, group_width):
    token_total = arrived.shape[0]
    return pl.pallas_call(
        _self_attention_kernel,
        out_shape=jax.ShapeDtypeStruct((token_total, group_width), jnp.bfloat16),
        cost_estimate=pl.CostEstimate(
            flops=4 * token_total * token_total * group_width,
            bytes_accessed=2 * token_total * 4 * group_width,
            transcendentals=token_total * token_total * (group_width // HEAD_DIM),
        ),
    )(arrived)


def _cross_kernel(length_ref, x_ref, wq_ref, gain_ref, keys_ref, values_ref, wo_ref, o_ref, total_ref):
    head = pl.program_id(0)
    factor = 1.0 / math.sqrt(HEAD_DIM)
    text = keys_ref.shape[0]
    piece = jnp.dot(x_ref[...], wq_ref[...], preferred_element_type=jnp.float32)
    mean_square = jnp.mean(piece * piece, axis=-1, keepdims=True)
    queries = (piece * lax.rsqrt(mean_square + EPSILON) * gain_ref[...]).astype(jnp.bfloat16)
    live = (lax.broadcasted_iota(jnp.int32, (1, text), 1) < length_ref[0]).astype(jnp.float32)
    scores = (
        lax.dot_general(
            queries, keys_ref[...], (((1,), (1,)), ((), ())), preferred_element_type=jnp.float32
        )
        * factor
    )
    weights = jnp.exp(scores) * live
    totals = jnp.sum(weights, axis=-1, keepdims=True)
    mixture = jnp.dot(weights.astype(jnp.bfloat16), values_ref[...], preferred_element_type=jnp.float32)
    mixed = (mixture / totals).astype(jnp.bfloat16)
    contribution = jnp.dot(mixed, wo_ref[...], preferred_element_type=jnp.float32)

    @pl.when(head == 0)
    def _():
        total_ref[...] = contribution

    @pl.when(head > 0)
    def _():
        total_ref[...] += contribution

    @pl.when(head == pl.num_programs(0) - 1)
    def _():
        o_ref[...] = total_ref[...].astype(o_ref.dtype)


def cross_partial(owner_cross, cross_wq, cross_q_gain, keys_own, values_own, length, cross_wo):
    token_total, model_width = owner_cross.shape
    group_width = cross_wq.shape[1]
    text = keys_own.shape[0]
    return pl.pallas_call(
        _cross_kernel,
        grid=(group_width // HEAD_DIM,),
        in_specs=[
            pl.BlockSpec(memory_space=pltpu.SMEM),
            pl.BlockSpec((token_total, model_width), lambda h: (0, 0)),
            pl.BlockSpec((model_width, HEAD_DIM), lambda h: (0, h)),
            pl.BlockSpec((1, HEAD_DIM), lambda h: (0, h)),
            pl.BlockSpec((text, HEAD_DIM), lambda h: (0, h)),
            pl.BlockSpec((text, HEAD_DIM), lambda h: (0, h)),
            pl.BlockSpec((HEAD_DIM, model_width), lambda h: (h, 0)),
        ],
        out_specs=pl.BlockSpec((token_total, model_width), lambda h: (0, 0)),
        out_shape=jax.ShapeDtypeStruct((token_total, model_width), jnp.bfloat16),
        scratch_shapes=[pltpu.VMEM((token_total, model_width), jnp.float32)],
        cost_estimate=pl.CostEstimate(
            flops=4 * token_total * model_width * group_width + 4 * token_total * text * group_width,
            bytes_accessed=4 * model_width * group_width + 4 * text * group_width
            + 4 * token_total * model_width,
            transcendentals=token_total * text * (group_width // HEAD_DIM),
        ),
    )(length, owner_cross, cross_wq, cross_q_gain.reshape(1, group_width), keys_own, values_own, cross_wo)


def _qkv_kernel(x_ref, wq_ref, wk_ref, wv_ref, cos_ref, sin_ref, gain_ref, o_ref):
    block_in = x_ref[...]
    cosine = cos_ref[...]
    sine_signed = sin_ref[...]
    group_width = wq_ref.shape[1]
    for section, w_ref in enumerate((wq_ref, wk_ref, wv_ref)):
        projected = jnp.dot(block_in, w_ref[...], preferred_element_type=jnp.float32)
        if section < 2:
            gains = gain_ref[section : section + 1, :]
            parts = []
            for head in range(group_width // HEAD_DIM):
                lanes = slice(head * HEAD_DIM, (head + 1) * HEAD_DIM)
                piece = projected[:, lanes]
                mean_square = jnp.mean(piece * piece, axis=-1, keepdims=True)
                normed = piece * lax.rsqrt(mean_square + EPSILON) * gains[:, lanes]
                swapped = pltpu.roll(normed, HEAD_DIM // 2, 1)
                parts.append(normed * cosine + swapped * sine_signed)
            projected = jnp.concatenate(parts, axis=-1)
        o_ref[0, :, section * group_width : (section + 1) * group_width] = projected.astype(
            o_ref.dtype
        )


def pack_projected(block_in, cell_map, w_qkv, self_q_gain, self_k_gain, head_count):
    videos, per_video, model_width = block_in.shape
    rows = block_in.reshape(-1, model_width)
    token_total = rows.shape[0]
    group_width = model_width // head_count
    angles = rope_angles(cell_map).reshape(token_total, HEAD_DIM // 2)
    cosine = jnp.cos(angles)
    sine = jnp.sin(angles)
    cos_full = jnp.concatenate([cosine, cosine], axis=-1)
    sin_signed = jnp.concatenate([-sine, sine], axis=-1)
    gains = jnp.stack([self_q_gain, self_k_gain])
    whole = lambda g: (0, 0)
    packed = pl.pallas_call(
        _qkv_kernel,
        grid=(head_count,),
        in_specs=[
            pl.BlockSpec((token_total, model_width), whole),
            pl.BlockSpec((model_width, group_width), lambda g: (0, g)),
            pl.BlockSpec((model_width, group_width), lambda g: (0, head_count + g)),
            pl.BlockSpec((model_width, group_width), lambda g: (0, 2 * head_count + g)),
            pl.BlockSpec((token_total, HEAD_DIM), whole),
            pl.BlockSpec((token_total, HEAD_DIM), whole),
            pl.BlockSpec((2, group_width), lambda g: (0, g)),
        ],
        out_specs=pl.BlockSpec((1, token_total, 3 * group_width), lambda g: (g, 0, 0)),
        out_shape=jax.ShapeDtypeStruct((head_count, token_total, 3 * group_width), jnp.bfloat16),
        cost_estimate=pl.CostEstimate(
            flops=2 * token_total * model_width * 3 * model_width,
            bytes_accessed=2 * model_width * 3 * model_width + 4 * token_total * 3 * model_width,
            transcendentals=0,
        ),
    )(rows, w_qkv, w_qkv, w_qkv, cos_full, sin_signed, gains)
    return packed.reshape(head_count, videos, per_video, 3 * group_width)


def local(
    hidden,
    latent,
    cell_map,
    text_lengths,
    block_modulation,
    head_modulation,
    step_sizes,
    w_qkv,
    self_q_gain,
    self_k_gain,
    w_out,
    cross_gain,
    cross_wq,
    cross_q_gain,
    text_keys,
    text_values,
    cross_wo,
    head_w,
):
    head_count = lax.axis_size("head")
    tile_count = lax.axis_size("tile")
    videos, per_video, model_width = hidden.shape
    group_heads = HEADS // head_count
    group_width = group_heads * HEAD_DIM
    stream = hidden.astype(jnp.float32)
    block_shift = block_modulation[:, 0][:, None, :]
    block_scale = block_modulation[:, 1][:, None, :]
    block_gate = block_modulation[:, 2][:, None, :]
    block_in = (layer_norm(stream) * (1.0 + block_scale) + block_shift).astype(jnp.bfloat16)
    packed = pack_projected(block_in, cell_map, w_qkv, self_q_gain, self_k_gain, head_count)
    arrived = lax.all_to_all(
        packed.reshape(head_count * videos, per_video, 3 * group_width),
        ("head", "tile"),
        split_axis=0,
        concat_axis=0,
        tiled=True,
    )
    own_mixture = attend_self(arrived.reshape(-1, 3 * group_width), group_width)
    returned = lax.all_to_all(
        own_mixture.reshape(head_count * tile_count, per_video, group_width),
        ("head", "tile"),
        split_axis=0,
        concat_axis=0,
        tiled=True,
    )
    attended = (
        returned.reshape(head_count, videos, per_video, group_width)
        .transpose(1, 2, 0, 3)
        .reshape(videos * per_video, model_width)
    )
    self_update = jnp.dot(attended, w_out, preferred_element_type=jnp.float32).reshape(
        videos, per_video, model_width
    )
    after_self = stream + block_gate * self_update
    cross_in = (layer_norm(after_self) * cross_gain).astype(jnp.bfloat16)
    copies = jnp.broadcast_to(cross_in[None], (head_count,) + cross_in.shape).reshape(
        head_count * videos, per_video, model_width
    )
    owner_cross = lax.all_to_all(copies, ("head", "tile"), split_axis=0, concat_axis=0, tiled=True)
    owner_cross = owner_cross.reshape(-1, model_width)
    partial = cross_partial(
        owner_cross, cross_wq, cross_q_gain, text_keys[0], text_values[0], text_lengths, cross_wo
    )
    returned_partials = lax.all_to_all(
        partial.reshape(head_count * tile_count, per_video, model_width),
        ("head", "tile"),
        split_axis=0,
        concat_axis=0,
        tiled=True,
    ).reshape(head_count, videos, per_video, model_width)
    returned_cross = jnp.sum(returned_partials.astype(jnp.float32), axis=0).astype(jnp.bfloat16)
    after_cross = after_self + returned_cross.astype(jnp.float32)
    hidden_next = after_cross.astype(jnp.bfloat16)
    head_shift = head_modulation[:, 0][:, None, :]
    head_scale = head_modulation[:, 1][:, None, :]
    head_in = (layer_norm(after_cross) * (1.0 + head_scale) + head_shift).astype(jnp.bfloat16)
    velocity = jnp.dot(
        head_in.reshape(-1, model_width), head_w, preferred_element_type=jnp.float32
    ).reshape(videos, per_video, -1)
    latent_next = latent + step_sizes[:, None, None] * velocity
    return (hidden_next, latent_next)


def solution(mesh):
    return jax.shard_map(
        local,
        mesh=mesh,
        in_specs=(
            P(None, ("head", "tile"), None),
            P(None, ("head", "tile"), None),
            P(None, ("head", "tile")),
            P("tile"),
            P(),
            P(),
            P(),
            P(),
            P(),
            P(),
            P(),
            P(),
            P(None, "head"),
            P("head"),
            P("tile", None, "head"),
            P("tile", None, "head"),
            P("head", None),
            P(),
        ),
        out_specs=(P(None, ("head", "tile"), None), P(None, ("head", "tile"), None)),
        check_vma=False,
    )
```

```python
import math

import jax
import jax.numpy as jnp
from jax import lax
from jax.experimental import pallas as pl
from jax.experimental.pallas import tpu as pltpu
from jax.sharding import PartitionSpec as P

HEADS = 12
HEAD_DIM = 128
GRID_H = 24
GRID_W = 8


EPSILON = 1e-06


def layer_norm(inputs):
    average = jnp.mean(inputs, axis=-1, keepdims=True)
    centred = inputs - average
    variance = jnp.mean(centred * centred, axis=-1, keepdims=True)
    return centred * lax.rsqrt(variance + EPSILON)


def head_norm(inputs, gain_table):
    mean_square = jnp.mean(inputs * inputs, axis=-1, keepdims=True)
    return inputs * lax.rsqrt(mean_square + EPSILON) * gain_table


def frequencies(pair_count):
    return jnp.power(10000.0, -jnp.arange(pair_count, dtype=jnp.float32) / pair_count)


def rope_angles(cell_ids):
    sixth_part = HEAD_DIM // 6
    time_pairs = HEAD_DIM // 2 - 2 * sixth_part
    plane_cells = GRID_H * GRID_W
    frame_index = (cell_ids // plane_cells).astype(jnp.float32)
    row_index = (cell_ids // GRID_W % GRID_H).astype(jnp.float32)
    column = (cell_ids % GRID_W).astype(jnp.float32)
    return jnp.concatenate(
        [
            frame_index[..., None] * frequencies(time_pairs),
            row_index[..., None] * frequencies(sixth_part),
            column[..., None] * frequencies(sixth_part),
        ],
        axis=-1,
    )


def rotate(inputs, angles):
    half_dim = inputs.shape[-1] // 2
    cosine = jnp.cos(angles)[..., None, :]
    sine_part = jnp.sin(angles)[..., None, :]
    lower_half = inputs[..., :half_dim]
    upper_half = inputs[..., half_dim:]
    return jnp.concatenate(
        [
            lower_half * cosine - upper_half * sine_part,
            lower_half * sine_part + upper_half * cosine,
        ],
        axis=-1,
    )


def _self_attention_kernel(x_ref, o_ref):
    group_width = o_ref.shape[1]
    factor = 1.0 / math.sqrt(HEAD_DIM)
    for head in range(group_width // HEAD_DIM):
        lanes = slice(head * HEAD_DIM, (head + 1) * HEAD_DIM)
        queries = x_ref[:, head * HEAD_DIM : (head + 1) * HEAD_DIM]
        keys = x_ref[:, group_width + head * HEAD_DIM : group_width + (head + 1) * HEAD_DIM]
        values = x_ref[:, 2 * group_width + head * HEAD_DIM : 2 * group_width + (head + 1) * HEAD_DIM]
        scores = (
            lax.dot_general(
                queries, keys, (((1,), (1,)), ((), ())), preferred_element_type=jnp.float32
            )
            * factor
        )
        weights = jnp.exp(scores)
        totals = jnp.sum(weights, axis=-1, keepdims=True)
        mixture = jnp.dot(
            weights.astype(jnp.bfloat16), values, preferred_element_type=jnp.float32
        )
        o_ref[:, lanes] = (mixture / totals).astype(o_ref.dtype)


def attend_self(arrived, group_width):
    token_total = arrived.shape[0]
    return pl.pallas_call(
        _self_attention_kernel,
        out_shape=jax.ShapeDtypeStruct((token_total, group_width), jnp.bfloat16),
        cost_estimate=pl.CostEstimate(
            flops=4 * token_total * token_total * group_width,
            bytes_accessed=2 * token_total * 4 * group_width,
            transcendentals=token_total * token_total * (group_width // HEAD_DIM),
        ),
    )(arrived)


def _cross_kernel(length_ref, x_ref, wq_ref, gain_ref, keys_ref, values_ref, wo_ref, o_ref, mixed_ref):
    factor = 1.0 / math.sqrt(HEAD_DIM)
    group_width = wq_ref.shape[1]
    text = keys_ref.shape[0]
    projected = jnp.dot(x_ref[...], wq_ref[...], preferred_element_type=jnp.float32)
    gains = gain_ref[...]
    live = (lax.broadcasted_iota(jnp.int32, (1, text), 1) < length_ref[0]).astype(jnp.float32)
    for head in range(group_width // HEAD_DIM):
        lanes = slice(head * HEAD_DIM, (head + 1) * HEAD_DIM)
        piece = projected[:, lanes]
        mean_square = jnp.mean(piece * piece, axis=-1, keepdims=True)
        queries = (piece * lax.rsqrt(mean_square + EPSILON) * gains[:, lanes]).astype(jnp.bfloat16)
        scores = (
            lax.dot_general(
                queries, keys_ref[:, lanes], (((1,), (1,)), ((), ())),
                preferred_element_type=jnp.float32,
            )
            * factor
        )
        weights = jnp.exp(scores) * live
        totals = jnp.sum(weights, axis=-1, keepdims=True)
        mixture = jnp.dot(
            weights.astype(jnp.bfloat16), values_ref[:, lanes], preferred_element_type=jnp.float32
        )
        mixed_ref[:, lanes] = (mixture / totals).astype(mixed_ref.dtype)
    o_ref[...] = jnp.dot(mixed_ref[...], wo_ref[...], preferred_element_type=jnp.float32).astype(
        o_ref.dtype
    )


def cross_partial(owner_cross, cross_wq, cross_q_gain, keys_own, values_own, length, cross_wo):
    token_total, model_width = owner_cross.shape
    group_width = cross_wq.shape[1]
    text = keys_own.shape[0]
    vmem = pl.BlockSpec(memory_space=pltpu.VMEM)
    return pl.pallas_call(
        _cross_kernel,
        in_specs=[pl.BlockSpec(memory_space=pltpu.SMEM)] + [vmem] * 6,
        out_specs=vmem,
        out_shape=jax.ShapeDtypeStruct((token_total, model_width), jnp.bfloat16),
        scratch_shapes=[pltpu.VMEM((token_total, group_width), jnp.bfloat16)],
        cost_estimate=pl.CostEstimate(
            flops=4 * token_total * model_width * group_width + 4 * token_total * text * group_width,
            bytes_accessed=4 * model_width * group_width + 4 * text * group_width
            + 4 * token_total * model_width,
            transcendentals=token_total * text * (group_width // HEAD_DIM),
        ),
    )(length, owner_cross, cross_wq, cross_q_gain.reshape(1, group_width), keys_own, values_own, cross_wo)


def _qkv_kernel(
    hidden_ref, shift_ref, scale_ref, wq_ref, wk_ref, wv_ref, cos_ref, sin_ref, gain_ref, o_ref,
    normed_ref,
):
    group = pl.program_id(0)
    videos, per_video, _ = hidden_ref.shape

    @pl.when(group == 0)
    def _():
        shift = shift_ref[...]
        scale = 1.0 + scale_ref[...]
        for slot in range(per_video):
            stream = hidden_ref[:, slot, :].astype(jnp.float32)
            normed_ref[slot * videos : (slot + 1) * videos, :] = (
                layer_norm(stream) * scale + shift
            ).astype(normed_ref.dtype)

    block_in = normed_ref[...]
    cosine = cos_ref[...]
    sine_signed = sin_ref[...]
    group_width = wq_ref.shape[1]
    for section, w_ref in enumerate((wq_ref, wk_ref, wv_ref)):
        projected = jnp.dot(block_in, w_ref[...], preferred_element_type=jnp.float32)
        if section < 2:
            gains = gain_ref[section : section + 1, :]
            parts = []
            for head in range(group_width // HEAD_DIM):
                lanes = slice(head * HEAD_DIM, (head + 1) * HEAD_DIM)
                piece = projected[:, lanes]
                mean_square = jnp.mean(piece * piece, axis=-1, keepdims=True)
                normed = piece * lax.rsqrt(mean_square + EPSILON) * gains[:, lanes]
                swapped = pltpu.roll(normed, HEAD_DIM // 2, 1)
                parts.append(normed * cosine + swapped * sine_signed)
            projected = jnp.concatenate(parts, axis=-1)
        o_ref[0, :, section * group_width : (section + 1) * group_width] = projected.astype(
            o_ref.dtype
        )


def pack_projected(hidden, block_modulation, cell_map, w_qkv, self_q_gain, self_k_gain, head_count):
    videos, per_video, model_width = hidden.shape
    token_total = videos * per_video
    group_width = model_width // head_count
    angles = rope_angles(jnp.transpose(cell_map, (1, 0))).reshape(token_total, HEAD_DIM // 2)
    cosine = jnp.cos(angles)
    sine = jnp.sin(angles)
    cos_full = jnp.concatenate([cosine, cosine], axis=-1)
    sin_signed = jnp.concatenate([-sine, sine], axis=-1)
    gains = jnp.stack([self_q_gain, self_k_gain])
    whole2 = lambda g: (0, 0)
    whole3 = lambda g: (0, 0, 0)
    packed = pl.pallas_call(
        _qkv_kernel,
        grid=(head_count,),
        in_specs=[
            pl.BlockSpec(hidden.shape, whole3),
            pl.BlockSpec((videos, model_width), whole2),
            pl.BlockSpec((videos, model_width), whole2),
            pl.BlockSpec((model_width, group_width), lambda g: (0, g)),
            pl.BlockSpec((model_width, group_width), lambda g: (0, head_count + g)),
            pl.BlockSpec((model_width, group_width), lambda g: (0, 2 * head_count + g)),
            pl.BlockSpec((token_total, HEAD_DIM), whole2),
            pl.BlockSpec((token_total, HEAD_DIM), whole2),
            pl.BlockSpec((2, group_width), lambda g: (0, g)),
        ],
        out_specs=pl.BlockSpec((1, token_total, 3 * group_width), lambda g: (g, 0, 0)),
        out_shape=jax.ShapeDtypeStruct((head_count, token_total, 3 * group_width), jnp.bfloat16),
        scratch_shapes=[pltpu.VMEM((token_total, model_width), jnp.bfloat16)],
        cost_estimate=pl.CostEstimate(
            flops=2 * token_total * model_width * 3 * model_width,
            bytes_accessed=2 * model_width * 3 * model_width + 4 * token_total * 3 * model_width,
            transcendentals=0,
        ),
    )(
        hidden, block_modulation[:, 0], block_modulation[:, 1], w_qkv, w_qkv, w_qkv,
        cos_full, sin_signed, gains,
    )
    packed = packed.reshape(head_count, per_video, videos, 3 * group_width)
    return jnp.transpose(packed, (0, 2, 1, 3))


def local(
    hidden,
    latent,
    cell_map,
    text_lengths,
    block_modulation,
    head_modulation,
    step_sizes,
    w_qkv,
    self_q_gain,
    self_k_gain,
    w_out,
    cross_gain,
    cross_wq,
    cross_q_gain,
    text_keys,
    text_values,
    cross_wo,
    head_w,
):
    head_count = lax.axis_size("head")
    tile_count = lax.axis_size("tile")
    videos, per_video, model_width = hidden.shape
    group_heads = HEADS // head_count
    group_width = group_heads * HEAD_DIM
    stream = hidden.astype(jnp.float32)
    block_gate = block_modulation[:, 2][:, None, :]
    packed = pack_projected(
        hidden, block_modulation, cell_map, w_qkv, self_q_gain, self_k_gain, head_count
    )
    arrived = lax.all_to_all(
        packed.reshape(head_count * videos, per_video, 3 * group_width),
        ("head", "tile"),
        split_axis=0,
        concat_axis=0,
        tiled=True,
    )
    own_mixture = attend_self(arrived.reshape(-1, 3 * group_width), group_width)
    returned = lax.all_to_all(
        own_mixture.reshape(head_count * tile_count, per_video, group_width),
        ("head", "tile"),
        split_axis=0,
        concat_axis=0,
        tiled=True,
    )
    attended = (
        returned.reshape(head_count, videos, per_video, group_width)
        .transpose(1, 2, 0, 3)
        .reshape(videos * per_video, model_width)
    )
    self_update = jnp.dot(attended, w_out, preferred_element_type=jnp.float32).reshape(
        videos, per_video, model_width
    )
    after_self = stream + block_gate * self_update
    cross_in = (layer_norm(after_self) * cross_gain).astype(jnp.bfloat16)
    copies = jnp.broadcast_to(cross_in[None], (head_count,) + cross_in.shape).reshape(
        head_count * videos, per_video, model_width
    )
    owner_cross = lax.all_to_all(copies, ("head", "tile"), split_axis=0, concat_axis=0, tiled=True)
    owner_cross = owner_cross.reshape(-1, model_width)
    partial = cross_partial(
        owner_cross, cross_wq, cross_q_gain, text_keys[0], text_values[0], text_lengths, cross_wo
    )
    returned_partials = lax.all_to_all(
        partial.reshape(head_count * tile_count, per_video, model_width),
        ("head", "tile"),
        split_axis=0,
        concat_axis=0,
        tiled=True,
    ).reshape(head_count, videos, per_video, model_width)
    returned_cross = jnp.sum(returned_partials.astype(jnp.float32), axis=0).astype(jnp.bfloat16)
    after_cross = after_self + returned_cross.astype(jnp.float32)
    hidden_next = after_cross.astype(jnp.bfloat16)
    head_shift = head_modulation[:, 0][:, None, :]
    head_scale = head_modulation[:, 1][:, None, :]
    head_in = (layer_norm(after_cross) * (1.0 + head_scale) + head_shift).astype(jnp.bfloat16)
    velocity = jnp.dot(
        head_in.reshape(-1, model_width), head_w, preferred_element_type=jnp.float32
    ).reshape(videos, per_video, -1)
    latent_next = latent + step_sizes[:, None, None] * velocity
    return (hidden_next, latent_next)


def solution(mesh):
    return jax.shard_map(
        local,
        mesh=mesh,
        in_specs=(
            P(None, ("head", "tile"), None),
            P(None, ("head", "tile"), None),
            P(None, ("head", "tile")),
            P("tile"),
            P(),
            P(),
            P(),
            P(),
            P(),
            P(),
            P(),
            P(),
            P(None, "head"),
            P("head"),
            P("tile", None, "head"),
            P("tile", None, "head"),
            P("head", None),
            P(),
        ),
        out_specs=(P(None, ("head", "tile"), None), P(None, ("head", "tile"), None)),
        check_vma=False,
    )
```

```python
import math

import jax
import jax.numpy as jnp
from jax import lax
from jax.experimental import pallas as pl
from jax.experimental.pallas import tpu as pltpu
from jax.sharding import PartitionSpec as P

HEADS = 12
HEAD_DIM = 128
GRID_H = 24
GRID_W = 8


EPSILON = 1e-06


def layer_norm(inputs):
    average = jnp.mean(inputs, axis=-1, keepdims=True)
    centred = inputs - average
    variance = jnp.mean(centred * centred, axis=-1, keepdims=True)
    return centred * lax.rsqrt(variance + EPSILON)


def head_norm(inputs, gain_table):
    mean_square = jnp.mean(inputs * inputs, axis=-1, keepdims=True)
    return inputs * lax.rsqrt(mean_square + EPSILON) * gain_table


def frequencies(pair_count):
    return jnp.power(10000.0, -jnp.arange(pair_count, dtype=jnp.float32) / pair_count)


def rope_angles(cell_ids):
    sixth_part = HEAD_DIM // 6
    time_pairs = HEAD_DIM // 2 - 2 * sixth_part
    plane_cells = GRID_H * GRID_W
    frame_index = (cell_ids // plane_cells).astype(jnp.float32)
    row_index = (cell_ids // GRID_W % GRID_H).astype(jnp.float32)
    column = (cell_ids % GRID_W).astype(jnp.float32)
    return jnp.concatenate(
        [
            frame_index[..., None] * frequencies(time_pairs),
            row_index[..., None] * frequencies(sixth_part),
            column[..., None] * frequencies(sixth_part),
        ],
        axis=-1,
    )


def rotate(inputs, angles):
    half_dim = inputs.shape[-1] // 2
    cosine = jnp.cos(angles)[..., None, :]
    sine_part = jnp.sin(angles)[..., None, :]
    lower_half = inputs[..., :half_dim]
    upper_half = inputs[..., half_dim:]
    return jnp.concatenate(
        [
            lower_half * cosine - upper_half * sine_part,
            lower_half * sine_part + upper_half * cosine,
        ],
        axis=-1,
    )


def _self_attention_kernel(x_ref, o_ref):
    group_width = o_ref.shape[1]
    factor = 1.0 / math.sqrt(HEAD_DIM)
    for head in range(group_width // HEAD_DIM):
        lanes = slice(head * HEAD_DIM, (head + 1) * HEAD_DIM)
        queries = x_ref[:, head * HEAD_DIM : (head + 1) * HEAD_DIM]
        keys = x_ref[:, group_width + head * HEAD_DIM : group_width + (head + 1) * HEAD_DIM]
        values = x_ref[:, 2 * group_width + head * HEAD_DIM : 2 * group_width + (head + 1) * HEAD_DIM]
        scores = (
            lax.dot_general(
                queries, keys, (((1,), (1,)), ((), ())), preferred_element_type=jnp.float32
            )
            * factor
        )
        weights = jnp.exp(scores)
        totals = jnp.sum(weights, axis=-1, keepdims=True)
        mixture = jnp.dot(
            weights.astype(jnp.bfloat16), values, preferred_element_type=jnp.float32
        )
        o_ref[:, lanes] = (mixture / totals).astype(o_ref.dtype)


def attend_self(arrived, group_width):
    token_total = arrived.shape[0]
    return pl.pallas_call(
        _self_attention_kernel,
        out_shape=jax.ShapeDtypeStruct((token_total, group_width), jnp.bfloat16),
        cost_estimate=pl.CostEstimate(
            flops=4 * token_total * token_total * group_width,
            bytes_accessed=2 * token_total * 4 * group_width,
            transcendentals=token_total * token_total * (group_width // HEAD_DIM),
        ),
    )(arrived)


def _cross_kernel(length_ref, x_ref, wq_ref, gain_ref, keys_ref, values_ref, wo_ref, o_ref, mixed_ref):
    factor = 1.0 / math.sqrt(HEAD_DIM)
    group_width = wq_ref.shape[1]
    text = keys_ref.shape[0]
    projected = jnp.dot(x_ref[...], wq_ref[...], preferred_element_type=jnp.float32)
    gains = gain_ref[...]
    live = (lax.broadcasted_iota(jnp.int32, (1, text), 1) < length_ref[0]).astype(jnp.float32)
    for head in range(group_width // HEAD_DIM):
        lanes = slice(head * HEAD_DIM, (head + 1) * HEAD_DIM)
        piece = projected[:, lanes]
        mean_square = jnp.mean(piece * piece, axis=-1, keepdims=True)
        queries = (piece * lax.rsqrt(mean_square + EPSILON) * gains[:, lanes]).astype(jnp.bfloat16)
        scores = (
            lax.dot_general(
                queries, keys_ref[:, lanes], (((1,), (1,)), ((), ())),
                preferred_element_type=jnp.float32,
            )
            * factor
        )
        weights = jnp.exp(scores) * live
        totals = jnp.sum(weights, axis=-1, keepdims=True)
        mixture = jnp.dot(
            weights.astype(jnp.bfloat16), values_ref[:, lanes], preferred_element_type=jnp.float32
        )
        mixed_ref[:, lanes] = (mixture / totals).astype(mixed_ref.dtype)
    o_ref[...] = jnp.dot(mixed_ref[...], wo_ref[...], preferred_element_type=jnp.float32).astype(
        o_ref.dtype
    )


def cross_partial(owner_cross, cross_wq, cross_q_gain, keys_own, values_own, length, cross_wo):
    token_total, model_width = owner_cross.shape
    group_width = cross_wq.shape[1]
    text = keys_own.shape[0]
    vmem = pl.BlockSpec(memory_space=pltpu.VMEM)
    return pl.pallas_call(
        _cross_kernel,
        in_specs=[pl.BlockSpec(memory_space=pltpu.SMEM)] + [vmem] * 6,
        out_specs=vmem,
        out_shape=jax.ShapeDtypeStruct((token_total, model_width), jnp.bfloat16),
        scratch_shapes=[pltpu.VMEM((token_total, group_width), jnp.bfloat16)],
        cost_estimate=pl.CostEstimate(
            flops=4 * token_total * model_width * group_width + 4 * token_total * text * group_width,
            bytes_accessed=4 * model_width * group_width + 4 * text * group_width
            + 4 * token_total * model_width,
            transcendentals=token_total * text * (group_width // HEAD_DIM),
        ),
    )(length, owner_cross, cross_wq, cross_q_gain.reshape(1, group_width), keys_own, values_own, cross_wo)


def _qkv_kernel(x_ref, wq_ref, wk_ref, wv_ref, cos_ref, sin_ref, gain_ref, o_ref):
    block_in = x_ref[...]
    cosine = cos_ref[...]
    sine_signed = sin_ref[...]
    group_width = wq_ref.shape[1]
    for section, w_ref in enumerate((wq_ref, wk_ref, wv_ref)):
        projected = jnp.dot(block_in, w_ref[...], preferred_element_type=jnp.float32)
        if section < 2:
            gains = gain_ref[section : section + 1, :]
            parts = []
            for head in range(group_width // HEAD_DIM):
                lanes = slice(head * HEAD_DIM, (head + 1) * HEAD_DIM)
                piece = projected[:, lanes]
                mean_square = jnp.mean(piece * piece, axis=-1, keepdims=True)
                normed = piece * lax.rsqrt(mean_square + EPSILON) * gains[:, lanes]
                swapped = pltpu.roll(normed, HEAD_DIM // 2, 1)
                parts.append(normed * cosine + swapped * sine_signed)
            projected = jnp.concatenate(parts, axis=-1)
        o_ref[0, :, section * group_width : (section + 1) * group_width] = projected.astype(
            o_ref.dtype
        )


def pack_projected(block_in, cell_map, w_qkv, self_q_gain, self_k_gain, head_count):
    videos, per_video, model_width = block_in.shape
    rows = block_in.reshape(-1, model_width)
    token_total = rows.shape[0]
    group_width = model_width // head_count
    angles = rope_angles(cell_map).reshape(token_total, HEAD_DIM // 2)
    cosine = jnp.cos(angles)
    sine = jnp.sin(angles)
    cos_full = jnp.concatenate([cosine, cosine], axis=-1)
    sin_signed = jnp.concatenate([-sine, sine], axis=-1)
    gains = jnp.stack([self_q_gain, self_k_gain])
    whole = lambda g: (0, 0)
    packed = pl.pallas_call(
        _qkv_kernel,
        grid=(head_count,),
        in_specs=[
            pl.BlockSpec((token_total, model_width), whole),
            pl.BlockSpec((model_width, group_width), lambda g: (0, g)),
            pl.BlockSpec((model_width, group_width), lambda g: (0, head_count + g)),
            pl.BlockSpec((model_width, group_width), lambda g: (0, 2 * head_count + g)),
            pl.BlockSpec((token_total, HEAD_DIM), whole),
            pl.BlockSpec((token_total, HEAD_DIM), whole),
            pl.BlockSpec((2, group_width), lambda g: (0, g)),
        ],
        out_specs=pl.BlockSpec((1, token_total, 3 * group_width), lambda g: (g, 0, 0)),
        out_shape=jax.ShapeDtypeStruct((head_count, token_total, 3 * group_width), jnp.bfloat16),
        cost_estimate=pl.CostEstimate(
            flops=2 * token_total * model_width * 3 * model_width,
            bytes_accessed=2 * model_width * 3 * model_width + 4 * token_total * 3 * model_width,
            transcendentals=0,
        ),
    )(rows, w_qkv, w_qkv, w_qkv, cos_full, sin_signed, gains)
    return packed.reshape(head_count, videos, per_video, 3 * group_width)


def local(
    hidden,
    latent,
    cell_map,
    text_lengths,
    block_modulation,
    head_modulation,
    step_sizes,
    w_qkv,
    self_q_gain,
    self_k_gain,
    w_out,
    cross_gain,
    cross_wq,
    cross_q_gain,
    text_keys,
    text_values,
    cross_wo,
    head_w,
):
    head_count = lax.axis_size("head")
    tile_count = lax.axis_size("tile")
    videos, per_video, model_width = hidden.shape
    group_heads = HEADS // head_count
    group_width = group_heads * HEAD_DIM
    stream = hidden.astype(jnp.float32)
    block_shift = block_modulation[:, 0][:, None, :]
    block_scale = block_modulation[:, 1][:, None, :]
    block_gate = block_modulation[:, 2][:, None, :]
    block_in = (layer_norm(stream) * (1.0 + block_scale) + block_shift).astype(jnp.bfloat16)
    packed = pack_projected(block_in, cell_map, w_qkv, self_q_gain, self_k_gain, head_count)
    arrived = lax.all_to_all(
        packed.reshape(head_count * videos, per_video, 3 * group_width),
        ("head", "tile"),
        split_axis=0,
        concat_axis=0,
        tiled=True,
    )
    own_mixture = attend_self(arrived.reshape(-1, 3 * group_width), group_width)
    returned = lax.all_to_all(
        own_mixture.reshape(head_count * tile_count, per_video, group_width),
        ("head", "tile"),
        split_axis=0,
        concat_axis=0,
        tiled=True,
    )
    attended = (
        returned.reshape(head_count, videos, per_video, group_width)
        .transpose(1, 2, 0, 3)
        .reshape(videos * per_video, model_width)
    )
    self_update = jnp.dot(attended, w_out, preferred_element_type=jnp.float32).reshape(
        videos, per_video, model_width
    )
    after_self = stream + block_gate * self_update
    cross_in = (layer_norm(after_self) * cross_gain).astype(jnp.bfloat16)
    copies = jnp.broadcast_to(cross_in[None], (head_count,) + cross_in.shape).reshape(
        head_count * videos, 2, per_video * model_width // 2
    )
    owner_cross = lax.all_to_all(copies, ("head", "tile"), split_axis=0, concat_axis=0, tiled=True)
    owner_cross = owner_cross.reshape(-1, model_width)
    partial = cross_partial(
        owner_cross, cross_wq, cross_q_gain, text_keys[0], text_values[0], text_lengths, cross_wo
    )
    returned_partials = lax.all_to_all(
        partial.reshape(head_count * tile_count, 2, per_video * model_width // 2),
        ("head", "tile"),
        split_axis=0,
        concat_axis=0,
        tiled=True,
    ).reshape(head_count, videos, per_video, model_width)
    returned_cross = jnp.sum(returned_partials.astype(jnp.float32), axis=0).astype(jnp.bfloat16)
    after_cross = after_self + returned_cross.astype(jnp.float32)
    hidden_next = after_cross.astype(jnp.bfloat16)
    head_shift = head_modulation[:, 0][:, None, :]
    head_scale = head_modulation[:, 1][:, None, :]
    head_in = (layer_norm(after_cross) * (1.0 + head_scale) + head_shift).astype(jnp.bfloat16)
    velocity = jnp.dot(
        head_in.reshape(-1, model_width), head_w, preferred_element_type=jnp.float32
    ).reshape(videos, per_video, -1)
    latent_next = latent + step_sizes[:, None, None] * velocity
    return (hidden_next, latent_next)


def solution(mesh):
    return jax.shard_map(
        local,
        mesh=mesh,
        in_specs=(
            P(None, ("head", "tile"), None),
            P(None, ("head", "tile"), None),
            P(None, ("head", "tile")),
            P("tile"),
            P(),
            P(),
            P(),
            P(),
            P(),
            P(),
            P(),
            P(),
            P(None, "head"),
            P("head"),
            P("tile", None, "head"),
            P("tile", None, "head"),
            P("head", None),
            P(),
        ),
        out_specs=(P(None, ("head", "tile"), None), P(None, ("head", "tile"), None)),
        check_vma=False,
    )
```

```python
import math

import jax
import jax.numpy as jnp
from jax import lax
from jax.experimental import pallas as pl
from jax.experimental.pallas import tpu as pltpu
from jax.sharding import PartitionSpec as P

HEADS = 12
HEAD_DIM = 128
GRID_H = 24
GRID_W = 8


EPSILON = 1e-06


def layer_norm(inputs):
    average = jnp.mean(inputs, axis=-1, keepdims=True)
    centred = inputs - average
    variance = jnp.mean(centred * centred, axis=-1, keepdims=True)
    return centred * lax.rsqrt(variance + EPSILON)


def head_norm(inputs, gain_table):
    mean_square = jnp.mean(inputs * inputs, axis=-1, keepdims=True)
    return inputs * lax.rsqrt(mean_square + EPSILON) * gain_table


def frequencies(pair_count):
    return jnp.power(10000.0, -jnp.arange(pair_count, dtype=jnp.float32) / pair_count)


def rope_angles(cell_ids):
    sixth_part = HEAD_DIM // 6
    time_pairs = HEAD_DIM // 2 - 2 * sixth_part
    plane_cells = GRID_H * GRID_W
    frame_index = (cell_ids // plane_cells).astype(jnp.float32)
    row_index = (cell_ids // GRID_W % GRID_H).astype(jnp.float32)
    column = (cell_ids % GRID_W).astype(jnp.float32)
    return jnp.concatenate(
        [
            frame_index[..., None] * frequencies(time_pairs),
            row_index[..., None] * frequencies(sixth_part),
            column[..., None] * frequencies(sixth_part),
        ],
        axis=-1,
    )


def rotate(inputs, angles):
    half_dim = inputs.shape[-1] // 2
    cosine = jnp.cos(angles)[..., None, :]
    sine_part = jnp.sin(angles)[..., None, :]
    lower_half = inputs[..., :half_dim]
    upper_half = inputs[..., half_dim:]
    return jnp.concatenate(
        [
            lower_half * cosine - upper_half * sine_part,
            lower_half * sine_part + upper_half * cosine,
        ],
        axis=-1,
    )


def _self_attention_kernel(x_ref, o_ref):
    group_width = o_ref.shape[1]
    factor = 1.0 / math.sqrt(HEAD_DIM)
    for head in range(group_width // HEAD_DIM):
        lanes = slice(head * HEAD_DIM, (head + 1) * HEAD_DIM)
        queries = x_ref[:, head * HEAD_DIM : (head + 1) * HEAD_DIM]
        keys = x_ref[:, group_width + head * HEAD_DIM : group_width + (head + 1) * HEAD_DIM]
        values = x_ref[:, 2 * group_width + head * HEAD_DIM : 2 * group_width + (head + 1) * HEAD_DIM]
        scores = (
            lax.dot_general(
                queries, keys, (((1,), (1,)), ((), ())), preferred_element_type=jnp.float32
            )
            * factor
        )
        weights = jnp.exp(scores)
        totals = jnp.sum(weights, axis=-1, keepdims=True)
        mixture = jnp.dot(
            weights.astype(jnp.bfloat16), values, preferred_element_type=jnp.float32
        )
        o_ref[:, lanes] = (mixture / totals).astype(o_ref.dtype)


def attend_self(arrived, group_width):
    token_total = arrived.shape[0]
    return pl.pallas_call(
        _self_attention_kernel,
        out_shape=jax.ShapeDtypeStruct((token_total, group_width), jnp.bfloat16),
        cost_estimate=pl.CostEstimate(
            flops=4 * token_total * token_total * group_width,
            bytes_accessed=2 * token_total * 4 * group_width,
            transcendentals=token_total * token_total * (group_width // HEAD_DIM),
        ),
    )(arrived)


def _cross_kernel(length_ref, x_ref, wq_ref, gain_ref, keys_ref, values_ref, wo_ref, o_ref, mixed_ref):
    factor = 1.0 / math.sqrt(HEAD_DIM)
    group_width = wq_ref.shape[1]
    text = keys_ref.shape[0]
    projected = jnp.dot(x_ref[...], wq_ref[...], preferred_element_type=jnp.float32)
    gains = gain_ref[...]
    live = (lax.broadcasted_iota(jnp.int32, (1, text), 1) < length_ref[0]).astype(jnp.float32)
    for head in range(group_width // HEAD_DIM):
        lanes = slice(head * HEAD_DIM, (head + 1) * HEAD_DIM)
        piece = projected[:, lanes]
        mean_square = jnp.mean(piece * piece, axis=-1, keepdims=True)
        queries = (piece * lax.rsqrt(mean_square + EPSILON) * gains[:, lanes]).astype(jnp.bfloat16)
        scores = (
            lax.dot_general(
                queries, keys_ref[:, lanes], (((1,), (1,)), ((), ())),
                preferred_element_type=jnp.float32,
            )
            * factor
        )
        weights = jnp.exp(scores) * live
        totals = jnp.sum(weights, axis=-1, keepdims=True)
        mixture = jnp.dot(
            weights.astype(jnp.bfloat16), values_ref[:, lanes], preferred_element_type=jnp.float32
        )
        mixed_ref[:, lanes] = (mixture / totals).astype(mixed_ref.dtype)
    o_ref[...] = jnp.dot(mixed_ref[...], wo_ref[...], preferred_element_type=jnp.float32).astype(
        o_ref.dtype
    )


def cross_partial(owner_cross, cross_wq, cross_q_gain, keys_own, values_own, length, cross_wo):
    token_total, model_width = owner_cross.shape
    group_width = cross_wq.shape[1]
    text = keys_own.shape[0]
    vmem = pl.BlockSpec(memory_space=pltpu.VMEM)
    return pl.pallas_call(
        _cross_kernel,
        in_specs=[pl.BlockSpec(memory_space=pltpu.SMEM)] + [vmem] * 6,
        out_specs=vmem,
        out_shape=jax.ShapeDtypeStruct((token_total, model_width), jnp.bfloat16),
        scratch_shapes=[pltpu.VMEM((token_total, group_width), jnp.bfloat16)],
        cost_estimate=pl.CostEstimate(
            flops=4 * token_total * model_width * group_width + 4 * token_total * text * group_width,
            bytes_accessed=4 * model_width * group_width + 4 * text * group_width
            + 4 * token_total * model_width,
            transcendentals=token_total * text * (group_width // HEAD_DIM),
        ),
    )(length, owner_cross, cross_wq, cross_q_gain.reshape(1, group_width), keys_own, values_own, cross_wo)


def _qkv_kernel(x_ref, wq_ref, wk_ref, wv_ref, cos_ref, sin_ref, gain_ref, o_ref):
    block_in = x_ref[...]
    cosine = cos_ref[...]
    sine_signed = sin_ref[...]
    group_width = wq_ref.shape[1]
    for section, w_ref in enumerate((wq_ref, wk_ref, wv_ref)):
        projected = jnp.dot(block_in, w_ref[...], preferred_element_type=jnp.float32)
        if section < 2:
            gains = gain_ref[section : section + 1, :]
            parts = []
            for head in range(group_width // HEAD_DIM):
                lanes = slice(head * HEAD_DIM, (head + 1) * HEAD_DIM)
                piece = projected[:, lanes]
                mean_square = jnp.mean(piece * piece, axis=-1, keepdims=True)
                normed = piece * lax.rsqrt(mean_square + EPSILON) * gains[:, lanes]
                swapped = pltpu.roll(normed, HEAD_DIM // 2, 1)
                parts.append(normed * cosine + swapped * sine_signed)
            projected = jnp.concatenate(parts, axis=-1)
        o_ref[0, :, section * group_width : (section + 1) * group_width] = projected.astype(
            o_ref.dtype
        )


def pack_projected(block_in, cell_map, w_qkv, self_q_gain, self_k_gain, head_count):
    videos, per_video, model_width = block_in.shape
    rows = block_in.reshape(-1, model_width)
    token_total = rows.shape[0]
    group_width = model_width // head_count
    angles = rope_angles(cell_map).reshape(token_total, HEAD_DIM // 2)
    cosine = jnp.cos(angles)
    sine = jnp.sin(angles)
    cos_full = jnp.concatenate([cosine, cosine], axis=-1)
    sin_signed = jnp.concatenate([-sine, sine], axis=-1)
    gains = jnp.stack([self_q_gain, self_k_gain])
    whole = lambda g: (0, 0)
    packed = pl.pallas_call(
        _qkv_kernel,
        grid=(head_count,),
        in_specs=[
            pl.BlockSpec((token_total, model_width), whole),
            pl.BlockSpec((model_width, group_width), lambda g: (0, g)),
            pl.BlockSpec((model_width, group_width), lambda g: (0, head_count + g)),
            pl.BlockSpec((model_width, group_width), lambda g: (0, 2 * head_count + g)),
            pl.BlockSpec((token_total, HEAD_DIM), whole),
            pl.BlockSpec((token_total, HEAD_DIM), whole),
            pl.BlockSpec((2, group_width), lambda g: (0, g)),
        ],
        out_specs=pl.BlockSpec((1, token_total, 3 * group_width), lambda g: (g, 0, 0)),
        out_shape=jax.ShapeDtypeStruct((head_count, token_total, 3 * group_width), jnp.bfloat16),
        cost_estimate=pl.CostEstimate(
            flops=2 * token_total * model_width * 3 * model_width,
            bytes_accessed=2 * model_width * 3 * model_width + 4 * token_total * 3 * model_width,
            transcendentals=0,
        ),
    )(rows, w_qkv, w_qkv, w_qkv, cos_full, sin_signed, gains)
    return packed.reshape(head_count, videos, per_video, 3 * group_width)


def local(
    hidden,
    latent,
    cell_map,
    text_lengths,
    block_modulation,
    head_modulation,
    step_sizes,
    w_qkv,
    self_q_gain,
    self_k_gain,
    w_out,
    cross_gain,
    cross_wq,
    cross_q_gain,
    text_keys,
    text_values,
    cross_wo,
    head_w,
):
    head_count = lax.axis_size("head")
    tile_count = lax.axis_size("tile")
    videos, per_video, model_width = hidden.shape
    group_heads = HEADS // head_count
    group_width = group_heads * HEAD_DIM
    stream = hidden.astype(jnp.float32)
    block_shift = block_modulation[:, 0][:, None, :]
    block_scale = block_modulation[:, 1][:, None, :]
    block_gate = block_modulation[:, 2][:, None, :]
    block_in = (layer_norm(stream) * (1.0 + block_scale) + block_shift).astype(jnp.bfloat16)
    packed = pack_projected(block_in, cell_map, w_qkv, self_q_gain, self_k_gain, head_count)
    arrived = lax.all_to_all(
        packed.reshape(head_count * videos, 2, per_video * 3 * group_width // 2),
        ("head", "tile"),
        split_axis=0,
        concat_axis=0,
        tiled=True,
    )
    own_mixture = attend_self(arrived.reshape(-1, 3 * group_width), group_width)
    returned = lax.all_to_all(
        own_mixture.reshape(head_count * tile_count, 2, per_video * group_width // 2),
        ("head", "tile"),
        split_axis=0,
        concat_axis=0,
        tiled=True,
    )
    attended = (
        returned.reshape(head_count, videos, per_video, group_width)
        .transpose(1, 2, 0, 3)
        .reshape(videos * per_video, model_width)
    )
    self_update = jnp.dot(attended, w_out, preferred_element_type=jnp.float32).reshape(
        videos, per_video, model_width
    )
    after_self = stream + block_gate * self_update
    cross_in = (layer_norm(after_self) * cross_gain).astype(jnp.bfloat16)
    copies = jnp.broadcast_to(cross_in[None], (head_count,) + cross_in.shape).reshape(
        head_count * videos, 2, per_video * model_width // 2
    )
    owner_cross = lax.all_to_all(copies, ("head", "tile"), split_axis=0, concat_axis=0, tiled=True)
    owner_cross = owner_cross.reshape(-1, model_width)
    partial = cross_partial(
        owner_cross, cross_wq, cross_q_gain, text_keys[0], text_values[0], text_lengths, cross_wo
    )
    returned_partials = lax.all_to_all(
        partial.reshape(head_count * tile_count, 2, per_video * model_width // 2),
        ("head", "tile"),
        split_axis=0,
        concat_axis=0,
        tiled=True,
    ).reshape(head_count, videos, 2, per_video * model_width // 2)
    returned_cross = (
        jnp.sum(returned_partials.astype(jnp.float32), axis=0)
        .astype(jnp.bfloat16)
        .reshape(videos, per_video, model_width)
    )
    after_cross = after_self + returned_cross.astype(jnp.float32)
    hidden_next = after_cross.astype(jnp.bfloat16)
    head_shift = head_modulation[:, 0][:, None, :]
    head_scale = head_modulation[:, 1][:, None, :]
    head_in = (layer_norm(after_cross) * (1.0 + head_scale) + head_shift).astype(jnp.bfloat16)
    velocity = jnp.dot(
        head_in.reshape(-1, model_width), head_w, preferred_element_type=jnp.float32
    ).reshape(videos, per_video, -1)
    latent_next = latent + step_sizes[:, None, None] * velocity
    return (hidden_next, latent_next)


def solution(mesh):
    return jax.shard_map(
        local,
        mesh=mesh,
        in_specs=(
            P(None, ("head", "tile"), None),
            P(None, ("head", "tile"), None),
            P(None, ("head", "tile")),
            P("tile"),
            P(),
            P(),
            P(),
            P(),
            P(),
            P(),
            P(),
            P(),
            P(None, "head"),
            P("head"),
            P("tile", None, "head"),
            P("tile", None, "head"),
            P("head", None),
            P(),
        ),
        out_specs=(P(None, ("head", "tile"), None), P(None, ("head", "tile"), None)),
        check_vma=False,
    )
```

```python
import math

import jax
import jax.numpy as jnp
from jax import lax
from jax.experimental import pallas as pl
from jax.experimental.pallas import tpu as pltpu
from jax.sharding import PartitionSpec as P

HEADS = 12
HEAD_DIM = 128
GRID_H = 24
GRID_W = 8


EPSILON = 1e-06


def layer_norm(inputs):
    average = jnp.mean(inputs, axis=-1, keepdims=True)
    centred = inputs - average
    variance = jnp.mean(centred * centred, axis=-1, keepdims=True)
    return centred * lax.rsqrt(variance + EPSILON)


def head_norm(inputs, gain_table):
    mean_square = jnp.mean(inputs * inputs, axis=-1, keepdims=True)
    return inputs * lax.rsqrt(mean_square + EPSILON) * gain_table


def frequencies(pair_count):
    return jnp.power(10000.0, -jnp.arange(pair_count, dtype=jnp.float32) / pair_count)


def rope_angles(cell_ids):
    sixth_part = HEAD_DIM // 6
    time_pairs = HEAD_DIM // 2 - 2 * sixth_part
    plane_cells = GRID_H * GRID_W
    frame_index = (cell_ids // plane_cells).astype(jnp.float32)
    row_index = (cell_ids // GRID_W % GRID_H).astype(jnp.float32)
    column = (cell_ids % GRID_W).astype(jnp.float32)
    return jnp.concatenate(
        [
            frame_index[..., None] * frequencies(time_pairs),
            row_index[..., None] * frequencies(sixth_part),
            column[..., None] * frequencies(sixth_part),
        ],
        axis=-1,
    )


def rotate(inputs, angles):
    half_dim = inputs.shape[-1] // 2
    cosine = jnp.cos(angles)[..., None, :]
    sine_part = jnp.sin(angles)[..., None, :]
    lower_half = inputs[..., :half_dim]
    upper_half = inputs[..., half_dim:]
    return jnp.concatenate(
        [
            lower_half * cosine - upper_half * sine_part,
            lower_half * sine_part + upper_half * cosine,
        ],
        axis=-1,
    )


def _self_attention_kernel(x_ref, o_ref):
    group_width = o_ref.shape[1]
    factor = 1.0 / math.sqrt(HEAD_DIM)
    for head in range(group_width // HEAD_DIM):
        lanes = slice(head * HEAD_DIM, (head + 1) * HEAD_DIM)
        queries = x_ref[:, head * HEAD_DIM : (head + 1) * HEAD_DIM]
        keys = x_ref[:, group_width + head * HEAD_DIM : group_width + (head + 1) * HEAD_DIM]
        values = x_ref[:, 2 * group_width + head * HEAD_DIM : 2 * group_width + (head + 1) * HEAD_DIM]
        scores = (
            lax.dot_general(
                queries, keys, (((1,), (1,)), ((), ())), preferred_element_type=jnp.float32
            )
            * factor
        )
        weights = jnp.exp(scores)
        totals = jnp.sum(weights, axis=-1, keepdims=True)
        mixture = jnp.dot(
            weights.astype(jnp.bfloat16), values, preferred_element_type=jnp.float32
        )
        o_ref[:, lanes] = (mixture / totals).astype(o_ref.dtype)


def attend_self(arrived, group_width):
    token_total = arrived.shape[0]
    return pl.pallas_call(
        _self_attention_kernel,
        out_shape=jax.ShapeDtypeStruct((token_total, group_width), jnp.bfloat16),
        cost_estimate=pl.CostEstimate(
            flops=4 * token_total * token_total * group_width,
            bytes_accessed=2 * token_total * 4 * group_width,
            transcendentals=token_total * token_total * (group_width // HEAD_DIM),
        ),
    )(arrived)


def _cross_kernel(length_ref, x_ref, wq_ref, gain_ref, keys_ref, values_ref, wo_ref, o_ref, mixed_ref):
    factor = 1.0 / math.sqrt(HEAD_DIM)
    group_width = wq_ref.shape[1]
    text = keys_ref.shape[0]
    projected = jnp.dot(x_ref[...], wq_ref[...], preferred_element_type=jnp.float32)
    gains = gain_ref[...]
    live = (lax.broadcasted_iota(jnp.int32, (1, text), 1) < length_ref[0]).astype(jnp.float32)
    for head in range(group_width // HEAD_DIM):
        lanes = slice(head * HEAD_DIM, (head + 1) * HEAD_DIM)
        piece = projected[:, lanes]
        mean_square = jnp.mean(piece * piece, axis=-1, keepdims=True)
        queries = (piece * lax.rsqrt(mean_square + EPSILON) * gains[:, lanes]).astype(jnp.bfloat16)
        scores = (
            lax.dot_general(
                queries, keys_ref[:, lanes], (((1,), (1,)), ((), ())),
                preferred_element_type=jnp.float32,
            )
            * factor
        )
        weights = jnp.exp(scores) * live
        totals = jnp.sum(weights, axis=-1, keepdims=True)
        mixture = jnp.dot(
            weights.astype(jnp.bfloat16), values_ref[:, lanes], preferred_element_type=jnp.float32
        )
        mixed_ref[:, lanes] = (mixture / totals).astype(mixed_ref.dtype)
    o_ref[...] = jnp.dot(mixed_ref[...], wo_ref[...], preferred_element_type=jnp.float32).astype(
        o_ref.dtype
    )


def cross_partial(owner_cross, cross_wq, cross_q_gain, keys_own, values_own, length, cross_wo):
    token_total, model_width = owner_cross.shape
    group_width = cross_wq.shape[1]
    text = keys_own.shape[0]
    vmem = pl.BlockSpec(memory_space=pltpu.VMEM)
    return pl.pallas_call(
        _cross_kernel,
        in_specs=[pl.BlockSpec(memory_space=pltpu.SMEM)] + [vmem] * 6,
        out_specs=vmem,
        out_shape=jax.ShapeDtypeStruct((token_total, model_width), jnp.bfloat16),
        scratch_shapes=[pltpu.VMEM((token_total, group_width), jnp.bfloat16)],
        cost_estimate=pl.CostEstimate(
            flops=4 * token_total * model_width * group_width + 4 * token_total * text * group_width,
            bytes_accessed=4 * model_width * group_width + 4 * text * group_width
            + 4 * token_total * model_width,
            transcendentals=token_total * text * (group_width // HEAD_DIM),
        ),
    )(length, owner_cross, cross_wq, cross_q_gain.reshape(1, group_width), keys_own, values_own, cross_wo)


def _qkv_kernel(x_ref, wq_ref, wk_ref, wv_ref, cos_ref, sin_ref, gain_ref, o_ref):
    block_in = x_ref[...]
    cosine = cos_ref[...]
    sine_signed = sin_ref[...]
    group_width = wq_ref.shape[1]
    for section, w_ref in enumerate((wq_ref, wk_ref, wv_ref)):
        projected = jnp.dot(block_in, w_ref[...], preferred_element_type=jnp.float32)
        if section < 2:
            gains = gain_ref[section : section + 1, :]
            parts = []
            for head in range(group_width // HEAD_DIM):
                lanes = slice(head * HEAD_DIM, (head + 1) * HEAD_DIM)
                piece = projected[:, lanes]
                mean_square = jnp.mean(piece * piece, axis=-1, keepdims=True)
                normed = piece * lax.rsqrt(mean_square + EPSILON) * gains[:, lanes]
                swapped = pltpu.roll(normed, HEAD_DIM // 2, 1)
                parts.append(normed * cosine + swapped * sine_signed)
            projected = jnp.concatenate(parts, axis=-1)
        o_ref[0, :, section * group_width : (section + 1) * group_width] = projected.astype(
            o_ref.dtype
        )


def pack_projected(block_in, cell_map, w_qkv, self_q_gain, self_k_gain, head_count):
    videos, per_video, model_width = block_in.shape
    rows = block_in.reshape(-1, model_width)
    token_total = rows.shape[0]
    group_width = model_width // head_count
    angles = rope_angles(cell_map).reshape(token_total, HEAD_DIM // 2)
    cosine = jnp.cos(angles)
    sine = jnp.sin(angles)
    cos_full = jnp.concatenate([cosine, cosine], axis=-1)
    sin_signed = jnp.concatenate([-sine, sine], axis=-1)
    gains = jnp.stack([self_q_gain, self_k_gain])
    whole = lambda g: (0, 0)
    packed = pl.pallas_call(
        _qkv_kernel,
        grid=(head_count,),
        in_specs=[
            pl.BlockSpec((token_total, model_width), whole),
            pl.BlockSpec((model_width, group_width), lambda g: (0, g)),
            pl.BlockSpec((model_width, group_width), lambda g: (0, head_count + g)),
            pl.BlockSpec((model_width, group_width), lambda g: (0, 2 * head_count + g)),
            pl.BlockSpec((token_total, HEAD_DIM), whole),
            pl.BlockSpec((token_total, HEAD_DIM), whole),
            pl.BlockSpec((2, group_width), lambda g: (0, g)),
        ],
        out_specs=pl.BlockSpec((1, token_total, 3 * group_width), lambda g: (g, 0, 0)),
        out_shape=jax.ShapeDtypeStruct((head_count, token_total, 3 * group_width), jnp.bfloat16),
        cost_estimate=pl.CostEstimate(
            flops=2 * token_total * model_width * 3 * model_width,
            bytes_accessed=2 * model_width * 3 * model_width + 4 * token_total * 3 * model_width,
            transcendentals=0,
        ),
    )(rows, w_qkv, w_qkv, w_qkv, cos_full, sin_signed, gains)
    return packed.reshape(head_count, videos, per_video, 3 * group_width)


def local(
    hidden,
    latent,
    cell_map,
    text_lengths,
    block_modulation,
    head_modulation,
    step_sizes,
    w_qkv,
    self_q_gain,
    self_k_gain,
    w_out,
    cross_gain,
    cross_wq,
    cross_q_gain,
    text_keys,
    text_values,
    cross_wo,
    head_w,
):
    head_count = lax.axis_size("head")
    tile_count = lax.axis_size("tile")
    videos, per_video, model_width = hidden.shape
    group_heads = HEADS // head_count
    group_width = group_heads * HEAD_DIM
    stream = hidden.astype(jnp.float32)
    block_shift = block_modulation[:, 0][:, None, :]
    block_scale = block_modulation[:, 1][:, None, :]
    block_gate = block_modulation[:, 2][:, None, :]
    block_in = (layer_norm(stream) * (1.0 + block_scale) + block_shift).astype(jnp.bfloat16)
    packed = pack_projected(block_in, cell_map, w_qkv, self_q_gain, self_k_gain, head_count)
    arrived = lax.all_to_all(
        packed.reshape(head_count * videos, 2, per_video * 3 * group_width // 2),
        ("head", "tile"),
        split_axis=0,
        concat_axis=0,
        tiled=True,
    )
    own_mixture = attend_self(arrived.reshape(-1, 3 * group_width), group_width)
    returned = lax.all_to_all(
        own_mixture.reshape(head_count * tile_count, 2, per_video * group_width // 2),
        ("head", "tile"),
        split_axis=0,
        concat_axis=0,
        tiled=True,
    )
    attended = (
        returned.reshape(head_count, videos, per_video, group_width)
        .transpose(1, 2, 0, 3)
        .reshape(videos * per_video, model_width)
    )
    self_update = jnp.dot(attended, w_out, preferred_element_type=jnp.float32).reshape(
        videos, per_video, model_width
    )
    after_self = stream + block_gate * self_update
    cross_in = (layer_norm(after_self) * cross_gain).astype(jnp.bfloat16)
    cross_rows = cross_in.reshape(videos, 2, per_video * model_width // 2)
    copies = jnp.broadcast_to(cross_rows[None], (head_count,) + cross_rows.shape).reshape(
        head_count * videos, 2, per_video * model_width // 2
    )
    owner_cross = lax.all_to_all(copies, ("head", "tile"), split_axis=0, concat_axis=0, tiled=True)
    owner_cross = owner_cross.reshape(-1, model_width)
    partial = cross_partial(
        owner_cross, cross_wq, cross_q_gain, text_keys[0], text_values[0], text_lengths, cross_wo
    )
    returned_partials = lax.all_to_all(
        partial.reshape(head_count * tile_count, 2, per_video * model_width // 2),
        ("head", "tile"),
        split_axis=0,
        concat_axis=0,
        tiled=True,
    ).reshape(head_count, videos, 2, per_video * model_width // 2)
    returned_cross = (
        jnp.sum(returned_partials.astype(jnp.float32), axis=0)
        .astype(jnp.bfloat16)
        .reshape(videos, per_video, model_width)
    )
    after_cross = after_self + returned_cross.astype(jnp.float32)
    hidden_next = after_cross.astype(jnp.bfloat16)
    head_shift = head_modulation[:, 0][:, None, :]
    head_scale = head_modulation[:, 1][:, None, :]
    head_in = (layer_norm(after_cross) * (1.0 + head_scale) + head_shift).astype(jnp.bfloat16)
    velocity = jnp.dot(
        head_in.reshape(-1, model_width), head_w, preferred_element_type=jnp.float32
    ).reshape(videos, per_video, -1)
    latent_next = latent + step_sizes[:, None, None] * velocity
    return (hidden_next, latent_next)


def solution(mesh):
    return jax.shard_map(
        local,
        mesh=mesh,
        in_specs=(
            P(None, ("head", "tile"), None),
            P(None, ("head", "tile"), None),
            P(None, ("head", "tile")),
            P("tile"),
            P(),
            P(),
            P(),
            P(),
            P(),
            P(),
            P(),
            P(),
            P(None, "head"),
            P("head"),
            P("tile", None, "head"),
            P("tile", None, "head"),
            P("head", None),
            P(),
        ),
        out_specs=(P(None, ("head", "tile"), None), P(None, ("head", "tile"), None)),
        check_vma=False,
    )
```

```python
import math

import jax
import jax.numpy as jnp
from jax import lax
from jax.experimental import pallas as pl
from jax.experimental.pallas import tpu as pltpu
from jax.sharding import PartitionSpec as P

HEADS = 12
HEAD_DIM = 128
GRID_H = 24
GRID_W = 8


EPSILON = 1e-06


def layer_norm(inputs):
    average = jnp.mean(inputs, axis=-1, keepdims=True)
    centred = inputs - average
    variance = jnp.mean(centred * centred, axis=-1, keepdims=True)
    return centred * lax.rsqrt(variance + EPSILON)


def head_norm(inputs, gain_table):
    mean_square = jnp.mean(inputs * inputs, axis=-1, keepdims=True)
    return inputs * lax.rsqrt(mean_square + EPSILON) * gain_table


def frequencies(pair_count):
    return jnp.power(10000.0, -jnp.arange(pair_count, dtype=jnp.float32) / pair_count)


def rope_angles(cell_ids):
    sixth_part = HEAD_DIM // 6
    time_pairs = HEAD_DIM // 2 - 2 * sixth_part
    plane_cells = GRID_H * GRID_W
    frame_index = (cell_ids // plane_cells).astype(jnp.float32)
    row_index = (cell_ids // GRID_W % GRID_H).astype(jnp.float32)
    column = (cell_ids % GRID_W).astype(jnp.float32)
    return jnp.concatenate(
        [
            frame_index[..., None] * frequencies(time_pairs),
            row_index[..., None] * frequencies(sixth_part),
            column[..., None] * frequencies(sixth_part),
        ],
        axis=-1,
    )


def rotate(inputs, angles):
    half_dim = inputs.shape[-1] // 2
    cosine = jnp.cos(angles)[..., None, :]
    sine_part = jnp.sin(angles)[..., None, :]
    lower_half = inputs[..., :half_dim]
    upper_half = inputs[..., half_dim:]
    return jnp.concatenate(
        [
            lower_half * cosine - upper_half * sine_part,
            lower_half * sine_part + upper_half * cosine,
        ],
        axis=-1,
    )


def _self_attention_kernel(x_ref, o_ref):
    group_width = o_ref.shape[1]
    factor = 1.0 / math.sqrt(HEAD_DIM)
    for head in range(group_width // HEAD_DIM):
        lanes = slice(head * HEAD_DIM, (head + 1) * HEAD_DIM)
        queries = x_ref[:, head * HEAD_DIM : (head + 1) * HEAD_DIM]
        keys = x_ref[:, group_width + head * HEAD_DIM : group_width + (head + 1) * HEAD_DIM]
        values = x_ref[:, 2 * group_width + head * HEAD_DIM : 2 * group_width + (head + 1) * HEAD_DIM]
        scores = (
            lax.dot_general(
                queries, keys, (((1,), (1,)), ((), ())), preferred_element_type=jnp.float32
            )
            * factor
        )
        weights = jnp.exp(scores)
        totals = jnp.sum(weights, axis=-1, keepdims=True)
        mixture = jnp.dot(
            weights.astype(jnp.bfloat16), values, preferred_element_type=jnp.float32
        )
        o_ref[:, lanes] = (mixture / totals).astype(o_ref.dtype)


def attend_self(arrived, group_width):
    token_total = arrived.shape[0]
    return pl.pallas_call(
        _self_attention_kernel,
        out_shape=jax.ShapeDtypeStruct((token_total, group_width), jnp.bfloat16),
        cost_estimate=pl.CostEstimate(
            flops=4 * token_total * token_total * group_width,
            bytes_accessed=2 * token_total * 4 * group_width,
            transcendentals=token_total * token_total * (group_width // HEAD_DIM),
        ),
    )(arrived)


def _cross_kernel(
    length_ref, x_ref, wq_ref, gain_ref, keys_hbm, values_hbm, wo_hbm, o_ref,
    mixed_ref, keys_ref, values_ref, wo_ref, copy_sems,
):
    factor = 1.0 / math.sqrt(HEAD_DIM)
    group_width = wq_ref.shape[1]
    text = keys_ref.shape[0]
    copies = [
        pltpu.make_async_copy(source, target, copy_sems.at[index])
        for index, (source, target) in enumerate(
            ((keys_hbm, keys_ref), (values_hbm, values_ref), (wo_hbm, wo_ref))
        )
    ]
    for copy in copies:
        copy.start()
    projected = jnp.dot(x_ref[...], wq_ref[...], preferred_element_type=jnp.float32)
    gains = gain_ref[...]
    live = (lax.broadcasted_iota(jnp.int32, (1, text), 1) < length_ref[0]).astype(jnp.float32)
    copies[0].wait()
    copies[1].wait()
    for head in range(group_width // HEAD_DIM):
        lanes = slice(head * HEAD_DIM, (head + 1) * HEAD_DIM)
        piece = projected[:, lanes]
        mean_square = jnp.mean(piece * piece, axis=-1, keepdims=True)
        queries = (piece * lax.rsqrt(mean_square + EPSILON) * gains[:, lanes]).astype(jnp.bfloat16)
        scores = (
            lax.dot_general(
                queries, keys_ref[:, lanes], (((1,), (1,)), ((), ())),
                preferred_element_type=jnp.float32,
            )
            * factor
        )
        weights = jnp.exp(scores) * live
        totals = jnp.sum(weights, axis=-1, keepdims=True)
        mixture = jnp.dot(
            weights.astype(jnp.bfloat16), values_ref[:, lanes], preferred_element_type=jnp.float32
        )
        mixed_ref[:, lanes] = (mixture / totals).astype(mixed_ref.dtype)
    copies[2].wait()
    o_ref[...] = jnp.dot(mixed_ref[...], wo_ref[...], preferred_element_type=jnp.float32).astype(
        o_ref.dtype
    )


def cross_partial(owner_cross, cross_wq, cross_q_gain, keys_own, values_own, length, cross_wo):
    token_total, model_width = owner_cross.shape
    group_width = cross_wq.shape[1]
    text = keys_own.shape[0]
    vmem = pl.BlockSpec(memory_space=pltpu.VMEM)
    hbm = pl.BlockSpec(memory_space=pl.ANY)
    return pl.pallas_call(
        _cross_kernel,
        in_specs=[pl.BlockSpec(memory_space=pltpu.SMEM), vmem, vmem, vmem, hbm, hbm, hbm],
        out_specs=vmem,
        out_shape=jax.ShapeDtypeStruct((token_total, model_width), jnp.bfloat16),
        scratch_shapes=[
            pltpu.VMEM((token_total, group_width), jnp.bfloat16),
            pltpu.VMEM((text, group_width), jnp.bfloat16),
            pltpu.VMEM((text, group_width), jnp.bfloat16),
            pltpu.VMEM((group_width, model_width), jnp.bfloat16),
            pltpu.SemaphoreType.DMA((3,)),
        ],
        cost_estimate=pl.CostEstimate(
            flops=4 * token_total * model_width * group_width + 4 * token_total * text * group_width,
            bytes_accessed=4 * model_width * group_width + 4 * text * group_width
            + 4 * token_total * model_width,
            transcendentals=token_total * text * (group_width // HEAD_DIM),
        ),
    )(length, owner_cross, cross_wq, cross_q_gain.reshape(1, group_width), keys_own, values_own, cross_wo)


def _qkv_kernel(x_ref, wq_ref, wk_ref, wv_ref, cos_ref, sin_ref, gain_ref, o_ref):
    block_in = x_ref[...]
    cosine = cos_ref[...]
    sine_signed = sin_ref[...]
    group_width = wq_ref.shape[1]
    for section, w_ref in enumerate((wq_ref, wk_ref, wv_ref)):
        projected = jnp.dot(block_in, w_ref[...], preferred_element_type=jnp.float32)
        if section < 2:
            gains = gain_ref[section : section + 1, :]
            parts = []
            for head in range(group_width // HEAD_DIM):
                lanes = slice(head * HEAD_DIM, (head + 1) * HEAD_DIM)
                piece = projected[:, lanes]
                mean_square = jnp.mean(piece * piece, axis=-1, keepdims=True)
                normed = piece * lax.rsqrt(mean_square + EPSILON) * gains[:, lanes]
                swapped = pltpu.roll(normed, HEAD_DIM // 2, 1)
                parts.append(normed * cosine + swapped * sine_signed)
            projected = jnp.concatenate(parts, axis=-1)
        o_ref[0, :, section * group_width : (section + 1) * group_width] = projected.astype(
            o_ref.dtype
        )


def pack_projected(block_in, cell_map, w_qkv, self_q_gain, self_k_gain, head_count):
    videos, per_video, model_width = block_in.shape
    rows = block_in.reshape(-1, model_width)
    token_total = rows.shape[0]
    group_width = model_width // head_count
    angles = rope_angles(cell_map).reshape(token_total, HEAD_DIM // 2)
    cosine = jnp.cos(angles)
    sine = jnp.sin(angles)
    cos_full = jnp.concatenate([cosine, cosine], axis=-1)
    sin_signed = jnp.concatenate([-sine, sine], axis=-1)
    gains = jnp.stack([self_q_gain, self_k_gain])
    whole = lambda g: (0, 0)
    packed = pl.pallas_call(
        _qkv_kernel,
        grid=(head_count,),
        in_specs=[
            pl.BlockSpec((token_total, model_width), whole),
            pl.BlockSpec((model_width, group_width), lambda g: (0, g)),
            pl.BlockSpec((model_width, group_width), lambda g: (0, head_count + g)),
            pl.BlockSpec((model_width, group_width), lambda g: (0, 2 * head_count + g)),
            pl.BlockSpec((token_total, HEAD_DIM), whole),
            pl.BlockSpec((token_total, HEAD_DIM), whole),
            pl.BlockSpec((2, group_width), lambda g: (0, g)),
        ],
        out_specs=pl.BlockSpec((1, token_total, 3 * group_width), lambda g: (g, 0, 0)),
        out_shape=jax.ShapeDtypeStruct((head_count, token_total, 3 * group_width), jnp.bfloat16),
        cost_estimate=pl.CostEstimate(
            flops=2 * token_total * model_width * 3 * model_width,
            bytes_accessed=2 * model_width * 3 * model_width + 4 * token_total * 3 * model_width,
            transcendentals=0,
        ),
    )(rows, w_qkv, w_qkv, w_qkv, cos_full, sin_signed, gains)
    return packed.reshape(head_count, videos, per_video, 3 * group_width)


def local(
    hidden,
    latent,
    cell_map,
    text_lengths,
    block_modulation,
    head_modulation,
    step_sizes,
    w_qkv,
    self_q_gain,
    self_k_gain,
    w_out,
    cross_gain,
    cross_wq,
    cross_q_gain,
    text_keys,
    text_values,
    cross_wo,
    head_w,
):
    head_count = lax.axis_size("head")
    tile_count = lax.axis_size("tile")
    videos, per_video, model_width = hidden.shape
    group_heads = HEADS // head_count
    group_width = group_heads * HEAD_DIM
    stream = hidden.astype(jnp.float32)
    block_shift = block_modulation[:, 0][:, None, :]
    block_scale = block_modulation[:, 1][:, None, :]
    block_gate = block_modulation[:, 2][:, None, :]
    block_in = (layer_norm(stream) * (1.0 + block_scale) + block_shift).astype(jnp.bfloat16)
    packed = pack_projected(block_in, cell_map, w_qkv, self_q_gain, self_k_gain, head_count)
    arrived = lax.all_to_all(
        packed.reshape(head_count * videos, 2, per_video * 3 * group_width // 2),
        ("head", "tile"),
        split_axis=0,
        concat_axis=0,
        tiled=True,
    )
    own_mixture = attend_self(arrived.reshape(-1, 3 * group_width), group_width)
    returned = lax.all_to_all(
        own_mixture.reshape(head_count * tile_count, 2, per_video * group_width // 2),
        ("head", "tile"),
        split_axis=0,
        concat_axis=0,
        tiled=True,
    )
    attended = (
        returned.reshape(head_count, videos, per_video, group_width)
        .transpose(1, 2, 0, 3)
        .reshape(videos * per_video, model_width)
    )
    self_update = jnp.dot(attended, w_out, preferred_element_type=jnp.float32).reshape(
        videos, per_video, model_width
    )
    after_self = stream + block_gate * self_update
    cross_in = (layer_norm(after_self) * cross_gain).astype(jnp.bfloat16)
    cross_rows = cross_in.reshape(videos, 2, per_video * model_width // 2)
    copies = jnp.broadcast_to(cross_rows[None], (head_count,) + cross_rows.shape).reshape(
        head_count * videos, 2, per_video * model_width // 2
    )
    owner_cross = lax.all_to_all(copies, ("head", "tile"), split_axis=0, concat_axis=0, tiled=True)
    owner_cross = owner_cross.reshape(-1, model_width)
    partial = cross_partial(
        owner_cross, cross_wq, cross_q_gain, text_keys[0], text_values[0], text_lengths, cross_wo
    )
    returned_partials = lax.all_to_all(
        partial.reshape(head_count * tile_count, 2, per_video * model_width // 2),
        ("head", "tile"),
        split_axis=0,
        concat_axis=0,
        tiled=True,
    ).reshape(head_count, videos, 2, per_video * model_width // 2)
    returned_cross = (
        jnp.sum(returned_partials.astype(jnp.float32), axis=0)
        .astype(jnp.bfloat16)
        .reshape(videos, per_video, model_width)
    )
    after_cross = after_self + returned_cross.astype(jnp.float32)
    hidden_next = after_cross.astype(jnp.bfloat16)
    head_shift = head_modulation[:, 0][:, None, :]
    head_scale = head_modulation[:, 1][:, None, :]
    head_in = (layer_norm(after_cross) * (1.0 + head_scale) + head_shift).astype(jnp.bfloat16)
    velocity = jnp.dot(
        head_in.reshape(-1, model_width), head_w, preferred_element_type=jnp.float32
    ).reshape(videos, per_video, -1)
    latent_next = latent + step_sizes[:, None, None] * velocity
    return (hidden_next, latent_next)


def solution(mesh):
    return jax.shard_map(
        local,
        mesh=mesh,
        in_specs=(
            P(None, ("head", "tile"), None),
            P(None, ("head", "tile"), None),
            P(None, ("head", "tile")),
            P("tile"),
            P(),
            P(),
            P(),
            P(),
            P(),
            P(),
            P(),
            P(),
            P(None, "head"),
            P("head"),
            P("tile", None, "head"),
            P("tile", None, "head"),
            P("head", None),
            P(),
        ),
        out_specs=(P(None, ("head", "tile"), None), P(None, ("head", "tile"), None)),
        check_vma=False,
    )
```

```python
import math

import jax
import jax.numpy as jnp
from jax import lax
from jax.experimental import pallas as pl
from jax.experimental.pallas import tpu as pltpu
from jax.sharding import PartitionSpec as P

HEADS = 12
HEAD_DIM = 128
GRID_H = 24
GRID_W = 8


EPSILON = 1e-06


def layer_norm(inputs):
    average = jnp.mean(inputs, axis=-1, keepdims=True)
    centred = inputs - average
    variance = jnp.mean(centred * centred, axis=-1, keepdims=True)
    return centred * lax.rsqrt(variance + EPSILON)


def head_norm(inputs, gain_table):
    mean_square = jnp.mean(inputs * inputs, axis=-1, keepdims=True)
    return inputs * lax.rsqrt(mean_square + EPSILON) * gain_table


def frequencies(pair_count):
    return jnp.power(10000.0, -jnp.arange(pair_count, dtype=jnp.float32) / pair_count)


def rope_angles(cell_ids):
    sixth_part = HEAD_DIM // 6
    time_pairs = HEAD_DIM // 2 - 2 * sixth_part
    plane_cells = GRID_H * GRID_W
    frame_index = (cell_ids // plane_cells).astype(jnp.float32)
    row_index = (cell_ids // GRID_W % GRID_H).astype(jnp.float32)
    column = (cell_ids % GRID_W).astype(jnp.float32)
    return jnp.concatenate(
        [
            frame_index[..., None] * frequencies(time_pairs),
            row_index[..., None] * frequencies(sixth_part),
            column[..., None] * frequencies(sixth_part),
        ],
        axis=-1,
    )


def rotate(inputs, angles):
    half_dim = inputs.shape[-1] // 2
    cosine = jnp.cos(angles)[..., None, :]
    sine_part = jnp.sin(angles)[..., None, :]
    lower_half = inputs[..., :half_dim]
    upper_half = inputs[..., half_dim:]
    return jnp.concatenate(
        [
            lower_half * cosine - upper_half * sine_part,
            lower_half * sine_part + upper_half * cosine,
        ],
        axis=-1,
    )


def _self_attention_kernel(x_ref, o_ref):
    group_width = o_ref.shape[1]
    factor = 1.0 / math.sqrt(HEAD_DIM)
    for head in range(group_width // HEAD_DIM):
        lanes = slice(head * HEAD_DIM, (head + 1) * HEAD_DIM)
        queries = x_ref[:, head * HEAD_DIM : (head + 1) * HEAD_DIM]
        keys = x_ref[:, group_width + head * HEAD_DIM : group_width + (head + 1) * HEAD_DIM]
        values = x_ref[:, 2 * group_width + head * HEAD_DIM : 2 * group_width + (head + 1) * HEAD_DIM]
        scores = (
            lax.dot_general(
                queries, keys, (((1,), (1,)), ((), ())), preferred_element_type=jnp.float32
            )
            * factor
        )
        weights = jnp.exp(scores)
        totals = jnp.sum(weights, axis=-1, keepdims=True)
        mixture = jnp.dot(
            weights.astype(jnp.bfloat16), values, preferred_element_type=jnp.float32
        )
        o_ref[:, lanes] = (mixture / totals).astype(o_ref.dtype)


def attend_self(arrived, group_width):
    token_total = arrived.shape[0]
    return pl.pallas_call(
        _self_attention_kernel,
        out_shape=jax.ShapeDtypeStruct((token_total, group_width), jnp.bfloat16),
        cost_estimate=pl.CostEstimate(
            flops=4 * token_total * token_total * group_width,
            bytes_accessed=2 * token_total * 4 * group_width,
            transcendentals=token_total * token_total * (group_width // HEAD_DIM),
        ),
    )(arrived)


def _cross_kernel(length_ref, x_ref, wq_ref, gain_ref, keys_ref, values_ref, wo_ref, o_ref, mixed_ref):
    factor = 1.0 / math.sqrt(HEAD_DIM)
    group_width = wq_ref.shape[1]
    text = keys_ref.shape[0]
    projected = jnp.dot(x_ref[...], wq_ref[...], preferred_element_type=jnp.float32)
    gains = gain_ref[...]
    live = (lax.broadcasted_iota(jnp.int32, (1, text), 1) < length_ref[0]).astype(jnp.float32)
    for head in range(group_width // HEAD_DIM):
        lanes = slice(head * HEAD_DIM, (head + 1) * HEAD_DIM)
        piece = projected[:, lanes]
        mean_square = jnp.mean(piece * piece, axis=-1, keepdims=True)
        queries = (piece * lax.rsqrt(mean_square + EPSILON) * gains[:, lanes]).astype(jnp.bfloat16)
        scores = (
            lax.dot_general(
                queries, keys_ref[:, lanes], (((1,), (1,)), ((), ())),
                preferred_element_type=jnp.float32,
            )
            * factor
        )
        weights = jnp.exp(scores) * live
        totals = jnp.sum(weights, axis=-1, keepdims=True)
        mixture = jnp.dot(
            weights.astype(jnp.bfloat16), values_ref[:, lanes], preferred_element_type=jnp.float32
        )
        mixed_ref[:, lanes] = (mixture / totals).astype(mixed_ref.dtype)
    o_ref[...] = jnp.dot(mixed_ref[...], wo_ref[...], preferred_element_type=jnp.float32).astype(
        o_ref.dtype
    )


def cross_partial(owner_cross, cross_wq, cross_q_gain, keys_own, values_own, length, cross_wo):
    token_total, model_width = owner_cross.shape
    group_width = cross_wq.shape[1]
    text = keys_own.shape[0]
    vmem = pl.BlockSpec(memory_space=pltpu.VMEM)
    return pl.pallas_call(
        _cross_kernel,
        in_specs=[pl.BlockSpec(memory_space=pltpu.SMEM)] + [vmem] * 6,
        out_specs=vmem,
        out_shape=jax.ShapeDtypeStruct((token_total, model_width), jnp.bfloat16),
        scratch_shapes=[pltpu.VMEM((token_total, group_width), jnp.bfloat16)],
        cost_estimate=pl.CostEstimate(
            flops=4 * token_total * model_width * group_width + 4 * token_total * text * group_width,
            bytes_accessed=4 * model_width * group_width + 4 * text * group_width
            + 4 * token_total * model_width,
            transcendentals=token_total * text * (group_width // HEAD_DIM),
        ),
    )(length, owner_cross, cross_wq, cross_q_gain.reshape(1, group_width), keys_own, values_own, cross_wo)


def _qkv_kernel(x_ref, wq_ref, wk_ref, wv_ref, angle_ref, qgain_ref, kgain_ref, o_ref):
    block_in = x_ref[...]
    angles = angle_ref[...]
    lane = lax.broadcasted_iota(jnp.int32, angles.shape, 1)
    cosine = jnp.cos(angles)
    sine = jnp.sin(angles)
    sine_signed = jnp.where(lane < HEAD_DIM // 2, -sine, sine)
    group_width = wq_ref.shape[1]
    gain_refs = (qgain_ref, kgain_ref)
    for section, w_ref in enumerate((wq_ref, wk_ref, wv_ref)):
        projected = jnp.dot(block_in, w_ref[...], preferred_element_type=jnp.float32)
        if section < 2:
            gains = gain_refs[section][...]
            parts = []
            for head in range(group_width // HEAD_DIM):
                lanes = slice(head * HEAD_DIM, (head + 1) * HEAD_DIM)
                piece = projected[:, lanes]
                mean_square = jnp.mean(piece * piece, axis=-1, keepdims=True)
                normed = piece * lax.rsqrt(mean_square + EPSILON) * gains[:, lanes]
                swapped = pltpu.roll(normed, HEAD_DIM // 2, 1)
                parts.append(normed * cosine + swapped * sine_signed)
            projected = jnp.concatenate(parts, axis=-1)
        o_ref[0, :, section * group_width : (section + 1) * group_width] = projected.astype(
            o_ref.dtype
        )


def pack_projected(block_in, cell_map, w_qkv, self_q_gain, self_k_gain, head_count):
    videos, per_video, model_width = block_in.shape
    rows = block_in.reshape(-1, model_width)
    token_total = rows.shape[0]
    group_width = model_width // head_count
    angles = rope_angles(cell_map).reshape(token_total, HEAD_DIM // 2)
    angles_full = jnp.concatenate([angles, angles], axis=-1)
    whole = lambda g: (0, 0)
    packed = pl.pallas_call(
        _qkv_kernel,
        grid=(head_count,),
        in_specs=[
            pl.BlockSpec((token_total, model_width), whole),
            pl.BlockSpec((model_width, group_width), lambda g: (0, g)),
            pl.BlockSpec((model_width, group_width), lambda g: (0, head_count + g)),
            pl.BlockSpec((model_width, group_width), lambda g: (0, 2 * head_count + g)),
            pl.BlockSpec((token_total, HEAD_DIM), whole),
            pl.BlockSpec((1, group_width), lambda g: (0, g)),
            pl.BlockSpec((1, group_width), lambda g: (0, g)),
        ],
        out_specs=pl.BlockSpec((1, token_total, 3 * group_width), lambda g: (g, 0, 0)),
        out_shape=jax.ShapeDtypeStruct((head_count, token_total, 3 * group_width), jnp.bfloat16),
        cost_estimate=pl.CostEstimate(
            flops=2 * token_total * model_width * 3 * model_width,
            bytes_accessed=2 * model_width * 3 * model_width + 4 * token_total * 3 * model_width,
            transcendentals=0,
        ),
    )(
        rows, w_qkv, w_qkv, w_qkv, angles_full,
        self_q_gain.reshape(1, model_width), self_k_gain.reshape(1, model_width),
    )
    return packed.reshape(head_count, videos, per_video, 3 * group_width)


def local(
    hidden,
    latent,
    cell_map,
    text_lengths,
    block_modulation,
    head_modulation,
    step_sizes,
    w_qkv,
    self_q_gain,
    self_k_gain,
    w_out,
    cross_gain,
    cross_wq,
    cross_q_gain,
    text_keys,
    text_values,
    cross_wo,
    head_w,
):
    head_count = lax.axis_size("head")
    tile_count = lax.axis_size("tile")
    videos, per_video, model_width = hidden.shape
    group_heads = HEADS // head_count
    group_width = group_heads * HEAD_DIM
    stream = hidden.astype(jnp.float32)
    block_shift = block_modulation[:, 0][:, None, :]
    block_scale = block_modulation[:, 1][:, None, :]
    block_gate = block_modulation[:, 2][:, None, :]
    block_in = (layer_norm(stream) * (1.0 + block_scale) + block_shift).astype(jnp.bfloat16)
    packed = pack_projected(block_in, cell_map, w_qkv, self_q_gain, self_k_gain, head_count)
    arrived = lax.all_to_all(
        packed.reshape(head_count * videos, 2, per_video * 3 * group_width // 2),
        ("head", "tile"),
        split_axis=0,
        concat_axis=0,
        tiled=True,
    )
    own_mixture = attend_self(arrived.reshape(-1, 3 * group_width), group_width)
    returned = lax.all_to_all(
        own_mixture.reshape(head_count * tile_count, 2, per_video * group_width // 2),
        ("head", "tile"),
        split_axis=0,
        concat_axis=0,
        tiled=True,
    )
    attended = (
        returned.reshape(head_count, videos, per_video, group_width)
        .transpose(1, 2, 0, 3)
        .reshape(videos * per_video, model_width)
    )
    self_update = jnp.dot(attended, w_out, preferred_element_type=jnp.float32).reshape(
        videos, per_video, model_width
    )
    after_self = stream + block_gate * self_update
    cross_in = (layer_norm(after_self) * cross_gain).astype(jnp.bfloat16)
    cross_rows = cross_in.reshape(videos, 2, per_video * model_width // 2)
    copies = jnp.broadcast_to(cross_rows[None], (head_count,) + cross_rows.shape).reshape(
        head_count * videos, 2, per_video * model_width // 2
    )
    owner_cross = lax.all_to_all(copies, ("head", "tile"), split_axis=0, concat_axis=0, tiled=True)
    owner_cross = owner_cross.reshape(-1, model_width)
    partial = cross_partial(
        owner_cross, cross_wq, cross_q_gain, text_keys[0], text_values[0], text_lengths, cross_wo
    )
    returned_partials = lax.all_to_all(
        partial.reshape(head_count * tile_count, 2, per_video * model_width // 2),
        ("head", "tile"),
        split_axis=0,
        concat_axis=0,
        tiled=True,
    ).reshape(head_count, videos, 2, per_video * model_width // 2)
    returned_cross = (
        jnp.sum(returned_partials.astype(jnp.float32), axis=0)
        .astype(jnp.bfloat16)
        .reshape(videos, per_video, model_width)
    )
    after_cross = after_self + returned_cross.astype(jnp.float32)
    hidden_next = after_cross.astype(jnp.bfloat16)
    head_shift = head_modulation[:, 0][:, None, :]
    head_scale = head_modulation[:, 1][:, None, :]
    head_in = (layer_norm(after_cross) * (1.0 + head_scale) + head_shift).astype(jnp.bfloat16)
    velocity = jnp.dot(
        head_in.reshape(-1, model_width), head_w, preferred_element_type=jnp.float32
    ).reshape(videos, per_video, -1)
    latent_next = latent + step_sizes[:, None, None] * velocity
    return (hidden_next, latent_next)


def solution(mesh):
    return jax.shard_map(
        local,
        mesh=mesh,
        in_specs=(
            P(None, ("head", "tile"), None),
            P(None, ("head", "tile"), None),
            P(None, ("head", "tile")),
            P("tile"),
            P(),
            P(),
            P(),
            P(),
            P(),
            P(),
            P(),
            P(),
            P(None, "head"),
            P("head"),
            P("tile", None, "head"),
            P("tile", None, "head"),
            P("head", None),
            P(),
        ),
        out_specs=(P(None, ("head", "tile"), None), P(None, ("head", "tile"), None)),
        check_vma=False,
    )
```

```python
import math

import jax
import jax.numpy as jnp
from jax import lax
from jax.experimental import pallas as pl
from jax.experimental.pallas import tpu as pltpu
from jax.sharding import PartitionSpec as P

HEADS = 12
HEAD_DIM = 128
GRID_H = 24
GRID_W = 8


EPSILON = 1e-06


def layer_norm(inputs):
    average = jnp.mean(inputs, axis=-1, keepdims=True)
    centred = inputs - average
    variance = jnp.mean(centred * centred, axis=-1, keepdims=True)
    return centred * lax.rsqrt(variance + EPSILON)


def head_norm(inputs, gain_table):
    mean_square = jnp.mean(inputs * inputs, axis=-1, keepdims=True)
    return inputs * lax.rsqrt(mean_square + EPSILON) * gain_table


def frequencies(pair_count):
    return jnp.power(10000.0, -jnp.arange(pair_count, dtype=jnp.float32) / pair_count)


def rope_angles(cell_ids):
    sixth_part = HEAD_DIM // 6
    time_pairs = HEAD_DIM // 2 - 2 * sixth_part
    plane_cells = GRID_H * GRID_W
    frame_index = (cell_ids // plane_cells).astype(jnp.float32)
    row_index = (cell_ids // GRID_W % GRID_H).astype(jnp.float32)
    column = (cell_ids % GRID_W).astype(jnp.float32)
    return jnp.concatenate(
        [
            frame_index[..., None] * frequencies(time_pairs),
            row_index[..., None] * frequencies(sixth_part),
            column[..., None] * frequencies(sixth_part),
        ],
        axis=-1,
    )


def rotate(inputs, angles):
    half_dim = inputs.shape[-1] // 2
    cosine = jnp.cos(angles)[..., None, :]
    sine_part = jnp.sin(angles)[..., None, :]
    lower_half = inputs[..., :half_dim]
    upper_half = inputs[..., half_dim:]
    return jnp.concatenate(
        [
            lower_half * cosine - upper_half * sine_part,
            lower_half * sine_part + upper_half * cosine,
        ],
        axis=-1,
    )


def _self_attention_kernel(x_ref, o_ref):
    group_width = o_ref.shape[1]
    factor = 1.0 / math.sqrt(HEAD_DIM)
    for head in range(group_width // HEAD_DIM):
        lanes = slice(head * HEAD_DIM, (head + 1) * HEAD_DIM)
        queries = x_ref[:, head * HEAD_DIM : (head + 1) * HEAD_DIM]
        keys = x_ref[:, group_width + head * HEAD_DIM : group_width + (head + 1) * HEAD_DIM]
        values = x_ref[:, 2 * group_width + head * HEAD_DIM : 2 * group_width + (head + 1) * HEAD_DIM]
        scores = (
            lax.dot_general(
                queries, keys, (((1,), (1,)), ((), ())), preferred_element_type=jnp.float32
            )
            * factor
        )
        weights = jnp.exp(scores)
        totals = jnp.sum(weights, axis=-1, keepdims=True)
        mixture = jnp.dot(
            weights.astype(jnp.bfloat16), values, preferred_element_type=jnp.float32
        )
        o_ref[:, lanes] = (mixture / totals).astype(o_ref.dtype)


def attend_self(arrived, group_width):
    token_total = arrived.shape[0]
    return pl.pallas_call(
        _self_attention_kernel,
        out_shape=jax.ShapeDtypeStruct((token_total, group_width), jnp.bfloat16),
        cost_estimate=pl.CostEstimate(
            flops=4 * token_total * token_total * group_width,
            bytes_accessed=2 * token_total * 4 * group_width,
            transcendentals=token_total * token_total * (group_width // HEAD_DIM),
        ),
    )(arrived)


def _cross_kernel(length_ref, x_ref, wq_ref, gain_ref, keys_ref, values_ref, wo_ref, o_ref, mixed_ref):
    factor = 1.0 / math.sqrt(HEAD_DIM)
    group_width = wq_ref.shape[1]
    text = keys_ref.shape[0]
    projected = jnp.dot(x_ref[...], wq_ref[...], preferred_element_type=jnp.float32)
    gains = gain_ref[...]
    live = (lax.broadcasted_iota(jnp.int32, (1, text), 1) < length_ref[0]).astype(jnp.float32)
    block_rows = 128
    for start in range(0, x_ref.shape[0], block_rows):
        rows = slice(start, start + block_rows)
        for head in range(group_width // HEAD_DIM):
            lanes = slice(head * HEAD_DIM, (head + 1) * HEAD_DIM)
            piece = projected[rows, lanes]
            mean_square = jnp.mean(piece * piece, axis=-1, keepdims=True)
            queries = (piece * lax.rsqrt(mean_square + EPSILON) * gains[:, lanes]).astype(
                jnp.bfloat16
            )
            scores = (
                lax.dot_general(
                    queries, keys_ref[:, lanes], (((1,), (1,)), ((), ())),
                    preferred_element_type=jnp.float32,
                )
                * factor
            )
            weights = jnp.exp(scores) * live
            totals = jnp.sum(weights, axis=-1, keepdims=True)
            mixture = jnp.dot(
                weights.astype(jnp.bfloat16), values_ref[:, lanes],
                preferred_element_type=jnp.float32,
            )
            mixed_ref[rows, lanes] = (mixture / totals).astype(mixed_ref.dtype)
    o_ref[...] = jnp.dot(mixed_ref[...], wo_ref[...], preferred_element_type=jnp.float32).astype(
        o_ref.dtype
    )


def cross_partial(owner_cross, cross_wq, cross_q_gain, keys_own, values_own, length, cross_wo):
    token_total, model_width = owner_cross.shape
    group_width = cross_wq.shape[1]
    text = keys_own.shape[0]
    vmem = pl.BlockSpec(memory_space=pltpu.VMEM)
    return pl.pallas_call(
        _cross_kernel,
        in_specs=[pl.BlockSpec(memory_space=pltpu.SMEM)] + [vmem] * 6,
        out_specs=vmem,
        out_shape=jax.ShapeDtypeStruct((token_total, model_width), jnp.bfloat16),
        scratch_shapes=[pltpu.VMEM((token_total, group_width), jnp.bfloat16)],
        cost_estimate=pl.CostEstimate(
            flops=4 * token_total * model_width * group_width + 4 * token_total * text * group_width,
            bytes_accessed=4 * model_width * group_width + 4 * text * group_width
            + 4 * token_total * model_width,
            transcendentals=token_total * text * (group_width // HEAD_DIM),
        ),
    )(length, owner_cross, cross_wq, cross_q_gain.reshape(1, group_width), keys_own, values_own, cross_wo)


def _qkv_kernel(x_ref, wq_ref, wk_ref, wv_ref, cos_ref, sin_ref, gain_ref, o_ref):
    block_in = x_ref[...]
    cosine = cos_ref[...]
    sine_signed = sin_ref[...]
    group_width = wq_ref.shape[1]
    for section, w_ref in enumerate((wq_ref, wk_ref, wv_ref)):
        projected = jnp.dot(block_in, w_ref[...], preferred_element_type=jnp.float32)
        if section < 2:
            gains = gain_ref[section : section + 1, :]
            parts = []
            for head in range(group_width // HEAD_DIM):
                lanes = slice(head * HEAD_DIM, (head + 1) * HEAD_DIM)
                piece = projected[:, lanes]
                mean_square = jnp.mean(piece * piece, axis=-1, keepdims=True)
                normed = piece * lax.rsqrt(mean_square + EPSILON) * gains[:, lanes]
                swapped = pltpu.roll(normed, HEAD_DIM // 2, 1)
                parts.append(normed * cosine + swapped * sine_signed)
            projected = jnp.concatenate(parts, axis=-1)
        o_ref[0, :, section * group_width : (section + 1) * group_width] = projected.astype(
            o_ref.dtype
        )


def pack_projected(block_in, cell_map, w_qkv, self_q_gain, self_k_gain, head_count):
    videos, per_video, model_width = block_in.shape
    rows = block_in.reshape(-1, model_width)
    token_total = rows.shape[0]
    group_width = model_width // head_count
    angles = rope_angles(cell_map).reshape(token_total, HEAD_DIM // 2)
    cosine = jnp.cos(angles)
    sine = jnp.sin(angles)
    cos_full = jnp.concatenate([cosine, cosine], axis=-1)
    sin_signed = jnp.concatenate([-sine, sine], axis=-1)
    gains = jnp.stack([self_q_gain, self_k_gain])
    whole = lambda g: (0, 0)
    packed = pl.pallas_call(
        _qkv_kernel,
        grid=(head_count,),
        in_specs=[
            pl.BlockSpec((token_total, model_width), whole),
            pl.BlockSpec((model_width, group_width), lambda g: (0, g)),
            pl.BlockSpec((model_width, group_width), lambda g: (0, head_count + g)),
            pl.BlockSpec((model_width, group_width), lambda g: (0, 2 * head_count + g)),
            pl.BlockSpec((token_total, HEAD_DIM), whole),
            pl.BlockSpec((token_total, HEAD_DIM), whole),
            pl.BlockSpec((2, group_width), lambda g: (0, g)),
        ],
        out_specs=pl.BlockSpec((1, token_total, 3 * group_width), lambda g: (g, 0, 0)),
        out_shape=jax.ShapeDtypeStruct((head_count, token_total, 3 * group_width), jnp.bfloat16),
        cost_estimate=pl.CostEstimate(
            flops=2 * token_total * model_width * 3 * model_width,
            bytes_accessed=2 * model_width * 3 * model_width + 4 * token_total * 3 * model_width,
            transcendentals=0,
        ),
    )(rows, w_qkv, w_qkv, w_qkv, cos_full, sin_signed, gains)
    return packed.reshape(head_count, videos, per_video, 3 * group_width)


def local(
    hidden,
    latent,
    cell_map,
    text_lengths,
    block_modulation,
    head_modulation,
    step_sizes,
    w_qkv,
    self_q_gain,
    self_k_gain,
    w_out,
    cross_gain,
    cross_wq,
    cross_q_gain,
    text_keys,
    text_values,
    cross_wo,
    head_w,
):
    head_count = lax.axis_size("head")
    tile_count = lax.axis_size("tile")
    videos, per_video, model_width = hidden.shape
    group_heads = HEADS // head_count
    group_width = group_heads * HEAD_DIM
    stream = hidden.astype(jnp.float32)
    block_shift = block_modulation[:, 0][:, None, :]
    block_scale = block_modulation[:, 1][:, None, :]
    block_gate = block_modulation[:, 2][:, None, :]
    block_in = (layer_norm(stream) * (1.0 + block_scale) + block_shift).astype(jnp.bfloat16)
    packed = pack_projected(block_in, cell_map, w_qkv, self_q_gain, self_k_gain, head_count)
    arrived = lax.all_to_all(
        packed.reshape(head_count * videos, 2, per_video * 3 * group_width // 2),
        ("head", "tile"),
        split_axis=0,
        concat_axis=0,
        tiled=True,
    )
    own_mixture = attend_self(arrived.reshape(-1, 3 * group_width), group_width)
    returned = lax.all_to_all(
        own_mixture.reshape(head_count * tile_count, 2, per_video * group_width // 2),
        ("head", "tile"),
        split_axis=0,
        concat_axis=0,
        tiled=True,
    )
    attended = (
        returned.reshape(head_count, videos, per_video, group_width)
        .transpose(1, 2, 0, 3)
        .reshape(videos * per_video, model_width)
    )
    self_update = jnp.dot(attended, w_out, preferred_element_type=jnp.float32).reshape(
        videos, per_video, model_width
    )
    after_self = stream + block_gate * self_update
    cross_in = (layer_norm(after_self) * cross_gain).astype(jnp.bfloat16)
    cross_rows = cross_in.reshape(videos, 2, per_video * model_width // 2)
    copies = jnp.broadcast_to(cross_rows[None], (head_count,) + cross_rows.shape).reshape(
        head_count * videos, 2, per_video * model_width // 2
    )
    owner_cross = lax.all_to_all(copies, ("head", "tile"), split_axis=0, concat_axis=0, tiled=True)
    owner_cross = owner_cross.reshape(-1, model_width)
    partial = cross_partial(
        owner_cross, cross_wq, cross_q_gain, text_keys[0], text_values[0], text_lengths, cross_wo
    )
    returned_partials = lax.all_to_all(
        partial.reshape(head_count * tile_count, 2, per_video * model_width // 2),
        ("head", "tile"),
        split_axis=0,
        concat_axis=0,
        tiled=True,
    ).reshape(head_count, videos, 2, per_video * model_width // 2)
    returned_cross = (
        jnp.sum(returned_partials.astype(jnp.float32), axis=0)
        .astype(jnp.bfloat16)
        .reshape(videos, per_video, model_width)
    )
    after_cross = after_self + returned_cross.astype(jnp.float32)
    hidden_next = after_cross.astype(jnp.bfloat16)
    head_shift = head_modulation[:, 0][:, None, :]
    head_scale = head_modulation[:, 1][:, None, :]
    head_in = (layer_norm(after_cross) * (1.0 + head_scale) + head_shift).astype(jnp.bfloat16)
    velocity = jnp.dot(
        head_in.reshape(-1, model_width), head_w, preferred_element_type=jnp.float32
    ).reshape(videos, per_video, -1)
    latent_next = latent + step_sizes[:, None, None] * velocity
    return (hidden_next, latent_next)


def solution(mesh):
    return jax.shard_map(
        local,
        mesh=mesh,
        in_specs=(
            P(None, ("head", "tile"), None),
            P(None, ("head", "tile"), None),
            P(None, ("head", "tile")),
            P("tile"),
            P(),
            P(),
            P(),
            P(),
            P(),
            P(),
            P(),
            P(),
            P(None, "head"),
            P("head"),
            P("tile", None, "head"),
            P("tile", None, "head"),
            P("head", None),
            P(),
        ),
        out_specs=(P(None, ("head", "tile"), None), P(None, ("head", "tile"), None)),
        check_vma=False,
    )
```

```python
import math

import jax
import jax.numpy as jnp
from jax import lax
from jax.experimental import pallas as pl
from jax.experimental.pallas import tpu as pltpu
from jax.sharding import PartitionSpec as P

HEADS = 12
HEAD_DIM = 128
GRID_H = 24
GRID_W = 8


EPSILON = 1e-06


def layer_norm(inputs):
    average = jnp.mean(inputs, axis=-1, keepdims=True)
    centred = inputs - average
    variance = jnp.mean(centred * centred, axis=-1, keepdims=True)
    return centred * lax.rsqrt(variance + EPSILON)


def head_norm(inputs, gain_table):
    mean_square = jnp.mean(inputs * inputs, axis=-1, keepdims=True)
    return inputs * lax.rsqrt(mean_square + EPSILON) * gain_table


def frequencies(pair_count):
    return jnp.power(10000.0, -jnp.arange(pair_count, dtype=jnp.float32) / pair_count)


def rope_angles(cell_ids):
    sixth_part = HEAD_DIM // 6
    time_pairs = HEAD_DIM // 2 - 2 * sixth_part
    plane_cells = GRID_H * GRID_W
    frame_index = (cell_ids // plane_cells).astype(jnp.float32)
    row_index = (cell_ids // GRID_W % GRID_H).astype(jnp.float32)
    column = (cell_ids % GRID_W).astype(jnp.float32)
    return jnp.concatenate(
        [
            frame_index[..., None] * frequencies(time_pairs),
            row_index[..., None] * frequencies(sixth_part),
            column[..., None] * frequencies(sixth_part),
        ],
        axis=-1,
    )


def rotate(inputs, angles):
    half_dim = inputs.shape[-1] // 2
    cosine = jnp.cos(angles)[..., None, :]
    sine_part = jnp.sin(angles)[..., None, :]
    lower_half = inputs[..., :half_dim]
    upper_half = inputs[..., half_dim:]
    return jnp.concatenate(
        [
            lower_half * cosine - upper_half * sine_part,
            lower_half * sine_part + upper_half * cosine,
        ],
        axis=-1,
    )


def _self_attention_kernel(x_ref, o_ref):
    group_width = o_ref.shape[1]
    factor = 1.0 / math.sqrt(HEAD_DIM)
    for head in range(group_width // HEAD_DIM):
        lanes = slice(head * HEAD_DIM, (head + 1) * HEAD_DIM)
        queries = x_ref[:, head * HEAD_DIM : (head + 1) * HEAD_DIM]
        keys = x_ref[:, group_width + head * HEAD_DIM : group_width + (head + 1) * HEAD_DIM]
        values = x_ref[:, 2 * group_width + head * HEAD_DIM : 2 * group_width + (head + 1) * HEAD_DIM]
        scores = (
            lax.dot_general(
                queries, keys, (((1,), (1,)), ((), ())), preferred_element_type=jnp.float32
            )
            * factor
        )
        weights = jnp.exp(scores)
        totals = jnp.sum(weights, axis=-1, keepdims=True)
        mixture = jnp.dot(
            weights.astype(jnp.bfloat16), values, preferred_element_type=jnp.float32
        )
        o_ref[:, lanes] = (mixture / totals).astype(o_ref.dtype)


def attend_self(arrived, group_width):
    token_total = arrived.shape[0]
    return pl.pallas_call(
        _self_attention_kernel,
        out_shape=jax.ShapeDtypeStruct((token_total, group_width), jnp.bfloat16),
        cost_estimate=pl.CostEstimate(
            flops=4 * token_total * token_total * group_width,
            bytes_accessed=2 * token_total * 4 * group_width,
            transcendentals=token_total * token_total * (group_width // HEAD_DIM),
        ),
    )(arrived)


def _cross_kernel(length_ref, x_ref, wq_ref, gain_ref, keys_ref, values_ref, wo_ref, o_ref, mixed_ref):
    factor = 1.0 / math.sqrt(HEAD_DIM)
    group_width = wq_ref.shape[1]
    text = keys_ref.shape[0]
    projected = jnp.dot(x_ref[...], wq_ref[...], preferred_element_type=jnp.float32)
    gains = gain_ref[...]
    live = (lax.broadcasted_iota(jnp.int32, (1, text), 1) < length_ref[0]).astype(jnp.float32)
    for head in range(group_width // HEAD_DIM):
        lanes = slice(head * HEAD_DIM, (head + 1) * HEAD_DIM)
        piece = projected[:, lanes]
        mean_square = jnp.mean(piece * piece, axis=-1, keepdims=True)
        queries = (piece * lax.rsqrt(mean_square + EPSILON) * gains[:, lanes]).astype(jnp.bfloat16)
        scores = (
            lax.dot_general(
                queries, keys_ref[:, lanes], (((1,), (1,)), ((), ())),
                preferred_element_type=jnp.float32,
            )
            * factor
        )
        weights = jnp.exp(scores) * live
        totals = jnp.sum(weights, axis=-1, keepdims=True)
        mixture = jnp.dot(
            weights.astype(jnp.bfloat16), values_ref[:, lanes], preferred_element_type=jnp.float32
        )
        mixed_ref[:, lanes] = (mixture / totals).astype(mixed_ref.dtype)
    o_ref[...] = jnp.dot(mixed_ref[...], wo_ref[...], preferred_element_type=jnp.float32).astype(
        o_ref.dtype
    )


def cross_partial(owner_cross, cross_wq, cross_q_gain, keys_own, values_own, length, cross_wo):
    token_total, model_width = owner_cross.shape
    group_width = cross_wq.shape[1]
    text = keys_own.shape[0]
    vmem = pl.BlockSpec(memory_space=pltpu.VMEM)
    return pl.pallas_call(
        _cross_kernel,
        in_specs=[pl.BlockSpec(memory_space=pltpu.SMEM)] + [vmem] * 6,
        out_specs=vmem,
        out_shape=jax.ShapeDtypeStruct((token_total, model_width), jnp.bfloat16),
        scratch_shapes=[pltpu.VMEM((token_total, group_width), jnp.bfloat16)],
        cost_estimate=pl.CostEstimate(
            flops=4 * token_total * model_width * group_width + 4 * token_total * text * group_width,
            bytes_accessed=4 * model_width * group_width + 4 * text * group_width
            + 4 * token_total * model_width,
            transcendentals=token_total * text * (group_width // HEAD_DIM),
        ),
    )(
        length,
        owner_cross,
        pltpu.with_memory_space_constraint(cross_wq, pltpu.VMEM),
        cross_q_gain.reshape(1, group_width),
        pltpu.with_memory_space_constraint(keys_own, pltpu.VMEM),
        pltpu.with_memory_space_constraint(values_own, pltpu.VMEM),
        pltpu.with_memory_space_constraint(cross_wo, pltpu.VMEM),
    )


def _qkv_kernel(x_ref, wq_ref, wk_ref, wv_ref, cos_ref, sin_ref, gain_ref, o_ref):
    block_in = x_ref[...]
    cosine = cos_ref[...]
    sine_signed = sin_ref[...]
    group_width = wq_ref.shape[1]
    for section, w_ref in enumerate((wq_ref, wk_ref, wv_ref)):
        projected = jnp.dot(block_in, w_ref[...], preferred_element_type=jnp.float32)
        if section < 2:
            gains = gain_ref[section : section + 1, :]
            parts = []
            for head in range(group_width // HEAD_DIM):
                lanes = slice(head * HEAD_DIM, (head + 1) * HEAD_DIM)
                piece = projected[:, lanes]
                mean_square = jnp.mean(piece * piece, axis=-1, keepdims=True)
                normed = piece * lax.rsqrt(mean_square + EPSILON) * gains[:, lanes]
                swapped = pltpu.roll(normed, HEAD_DIM // 2, 1)
                parts.append(normed * cosine + swapped * sine_signed)
            projected = jnp.concatenate(parts, axis=-1)
        o_ref[0, :, section * group_width : (section + 1) * group_width] = projected.astype(
            o_ref.dtype
        )


def pack_projected(block_in, cell_map, w_qkv, self_q_gain, self_k_gain, head_count):
    videos, per_video, model_width = block_in.shape
    rows = block_in.reshape(-1, model_width)
    token_total = rows.shape[0]
    group_width = model_width // head_count
    angles = rope_angles(cell_map).reshape(token_total, HEAD_DIM // 2)
    cosine = jnp.cos(angles)
    sine = jnp.sin(angles)
    cos_full = jnp.concatenate([cosine, cosine], axis=-1)
    sin_signed = jnp.concatenate([-sine, sine], axis=-1)
    gains = jnp.stack([self_q_gain, self_k_gain])
    whole = lambda g: (0, 0)
    packed = pl.pallas_call(
        _qkv_kernel,
        grid=(head_count,),
        in_specs=[
            pl.BlockSpec((token_total, model_width), whole),
            pl.BlockSpec((model_width, group_width), lambda g: (0, g)),
            pl.BlockSpec((model_width, group_width), lambda g: (0, head_count + g)),
            pl.BlockSpec((model_width, group_width), lambda g: (0, 2 * head_count + g)),
            pl.BlockSpec((token_total, HEAD_DIM), whole),
            pl.BlockSpec((token_total, HEAD_DIM), whole),
            pl.BlockSpec((2, group_width), lambda g: (0, g)),
        ],
        out_specs=pl.BlockSpec((1, token_total, 3 * group_width), lambda g: (g, 0, 0)),
        out_shape=jax.ShapeDtypeStruct((head_count, token_total, 3 * group_width), jnp.bfloat16),
        cost_estimate=pl.CostEstimate(
            flops=2 * token_total * model_width * 3 * model_width,
            bytes_accessed=2 * model_width * 3 * model_width + 4 * token_total * 3 * model_width,
            transcendentals=0,
        ),
    )(rows, w_qkv, w_qkv, w_qkv, cos_full, sin_signed, gains)
    return packed.reshape(head_count, videos, per_video, 3 * group_width)


def local(
    hidden,
    latent,
    cell_map,
    text_lengths,
    block_modulation,
    head_modulation,
    step_sizes,
    w_qkv,
    self_q_gain,
    self_k_gain,
    w_out,
    cross_gain,
    cross_wq,
    cross_q_gain,
    text_keys,
    text_values,
    cross_wo,
    head_w,
):
    head_count = lax.axis_size("head")
    tile_count = lax.axis_size("tile")
    videos, per_video, model_width = hidden.shape
    group_heads = HEADS // head_count
    group_width = group_heads * HEAD_DIM
    stream = hidden.astype(jnp.float32)
    block_shift = block_modulation[:, 0][:, None, :]
    block_scale = block_modulation[:, 1][:, None, :]
    block_gate = block_modulation[:, 2][:, None, :]
    block_in = (layer_norm(stream) * (1.0 + block_scale) + block_shift).astype(jnp.bfloat16)
    packed = pack_projected(block_in, cell_map, w_qkv, self_q_gain, self_k_gain, head_count)
    arrived = lax.all_to_all(
        packed.reshape(head_count * videos, 2, per_video * 3 * group_width // 2),
        ("head", "tile"),
        split_axis=0,
        concat_axis=0,
        tiled=True,
    )
    own_mixture = attend_self(arrived.reshape(-1, 3 * group_width), group_width)
    returned = lax.all_to_all(
        own_mixture.reshape(head_count * tile_count, 2, per_video * group_width // 2),
        ("head", "tile"),
        split_axis=0,
        concat_axis=0,
        tiled=True,
    )
    attended = (
        returned.reshape(head_count, videos, per_video, group_width)
        .transpose(1, 2, 0, 3)
        .reshape(videos * per_video, model_width)
    )
    self_update = jnp.dot(attended, w_out, preferred_element_type=jnp.float32).reshape(
        videos, per_video, model_width
    )
    after_self = stream + block_gate * self_update
    cross_in = (layer_norm(after_self) * cross_gain).astype(jnp.bfloat16)
    cross_rows = cross_in.reshape(videos, 2, per_video * model_width // 2)
    copies = jnp.broadcast_to(cross_rows[None], (head_count,) + cross_rows.shape).reshape(
        head_count * videos, 2, per_video * model_width // 2
    )
    owner_cross = lax.all_to_all(copies, ("head", "tile"), split_axis=0, concat_axis=0, tiled=True)
    owner_cross = owner_cross.reshape(-1, model_width)
    partial = cross_partial(
        owner_cross, cross_wq, cross_q_gain, text_keys[0], text_values[0], text_lengths, cross_wo
    )
    returned_partials = lax.all_to_all(
        partial.reshape(head_count * tile_count, 2, per_video * model_width // 2),
        ("head", "tile"),
        split_axis=0,
        concat_axis=0,
        tiled=True,
    ).reshape(head_count, videos, 2, per_video * model_width // 2)
    returned_cross = (
        jnp.sum(returned_partials.astype(jnp.float32), axis=0)
        .astype(jnp.bfloat16)
        .reshape(videos, per_video, model_width)
    )
    after_cross = after_self + returned_cross.astype(jnp.float32)
    hidden_next = after_cross.astype(jnp.bfloat16)
    head_shift = head_modulation[:, 0][:, None, :]
    head_scale = head_modulation[:, 1][:, None, :]
    head_in = (layer_norm(after_cross) * (1.0 + head_scale) + head_shift).astype(jnp.bfloat16)
    velocity = jnp.dot(
        head_in.reshape(-1, model_width), head_w, preferred_element_type=jnp.float32
    ).reshape(videos, per_video, -1)
    latent_next = latent + step_sizes[:, None, None] * velocity
    return (hidden_next, latent_next)


def solution(mesh):
    return jax.shard_map(
        local,
        mesh=mesh,
        in_specs=(
            P(None, ("head", "tile"), None),
            P(None, ("head", "tile"), None),
            P(None, ("head", "tile")),
            P("tile"),
            P(),
            P(),
            P(),
            P(),
            P(),
            P(),
            P(),
            P(),
            P(None, "head"),
            P("head"),
            P("tile", None, "head"),
            P("tile", None, "head"),
            P("head", None),
            P(),
        ),
        out_specs=(P(None, ("head", "tile"), None), P(None, ("head", "tile"), None)),
        check_vma=False,
    )
```

```python
import math

import jax
import jax.numpy as jnp
from jax import lax
from jax.experimental import pallas as pl
from jax.experimental.pallas import tpu as pltpu
from jax.sharding import PartitionSpec as P

HEADS = 12
HEAD_DIM = 128
GRID_H = 24
GRID_W = 8


EPSILON = 1e-06


def layer_norm(inputs):
    average = jnp.mean(inputs, axis=-1, keepdims=True)
    centred = inputs - average
    variance = jnp.mean(centred * centred, axis=-1, keepdims=True)
    return centred * lax.rsqrt(variance + EPSILON)


def head_norm(inputs, gain_table):
    mean_square = jnp.mean(inputs * inputs, axis=-1, keepdims=True)
    return inputs * lax.rsqrt(mean_square + EPSILON) * gain_table


def frequencies(pair_count):
    return jnp.power(10000.0, -jnp.arange(pair_count, dtype=jnp.float32) / pair_count)


def rope_angles(cell_ids):
    sixth_part = HEAD_DIM // 6
    time_pairs = HEAD_DIM // 2 - 2 * sixth_part
    plane_cells = GRID_H * GRID_W
    frame_index = (cell_ids // plane_cells).astype(jnp.float32)
    row_index = (cell_ids // GRID_W % GRID_H).astype(jnp.float32)
    column = (cell_ids % GRID_W).astype(jnp.float32)
    return jnp.concatenate(
        [
            frame_index[..., None] * frequencies(time_pairs),
            row_index[..., None] * frequencies(sixth_part),
            column[..., None] * frequencies(sixth_part),
        ],
        axis=-1,
    )


def rotate(inputs, angles):
    half_dim = inputs.shape[-1] // 2
    cosine = jnp.cos(angles)[..., None, :]
    sine_part = jnp.sin(angles)[..., None, :]
    lower_half = inputs[..., :half_dim]
    upper_half = inputs[..., half_dim:]
    return jnp.concatenate(
        [
            lower_half * cosine - upper_half * sine_part,
            lower_half * sine_part + upper_half * cosine,
        ],
        axis=-1,
    )


def _self_attention_kernel(x_ref, o_ref):
    group_width = o_ref.shape[1]
    factor = 1.0 / math.sqrt(HEAD_DIM)
    for head in range(group_width // HEAD_DIM):
        lanes = slice(head * HEAD_DIM, (head + 1) * HEAD_DIM)
        queries = x_ref[:, head * HEAD_DIM : (head + 1) * HEAD_DIM]
        keys = x_ref[:, group_width + head * HEAD_DIM : group_width + (head + 1) * HEAD_DIM]
        values = x_ref[:, 2 * group_width + head * HEAD_DIM : 2 * group_width + (head + 1) * HEAD_DIM]
        scores = (
            lax.dot_general(
                queries, keys, (((1,), (1,)), ((), ())), preferred_element_type=jnp.float32
            )
            * factor
        )
        weights = jnp.exp(scores)
        totals = jnp.sum(weights, axis=-1, keepdims=True)
        mixture = jnp.dot(
            weights.astype(jnp.bfloat16), values, preferred_element_type=jnp.float32
        )
        o_ref[:, lanes] = (mixture / totals).astype(o_ref.dtype)


def attend_self(arrived, group_width):
    token_total = arrived.shape[0]
    return pl.pallas_call(
        _self_attention_kernel,
        out_shape=jax.ShapeDtypeStruct((token_total, group_width), jnp.bfloat16),
        cost_estimate=pl.CostEstimate(
            flops=4 * token_total * token_total * group_width,
            bytes_accessed=2 * token_total * 4 * group_width,
            transcendentals=token_total * token_total * (group_width // HEAD_DIM),
        ),
    )(arrived)


def _cross_kernel(length_ref, x_ref, wq_ref, gain_ref, keys_ref, values_ref, wo_ref, o_ref, mixed_ref):
    factor = 1.0 / math.sqrt(HEAD_DIM)
    group_width = wq_ref.shape[1]
    text = keys_ref.shape[0]
    projected = jnp.dot(x_ref[...], wq_ref[...], preferred_element_type=jnp.float32)
    gains = gain_ref[...]
    live = (lax.broadcasted_iota(jnp.int32, (1, text), 1) < length_ref[0]).astype(jnp.float32)
    for head in range(group_width // HEAD_DIM):
        lanes = slice(head * HEAD_DIM, (head + 1) * HEAD_DIM)
        piece = projected[:, lanes]
        mean_square = jnp.mean(piece * piece, axis=-1, keepdims=True)
        queries = (piece * lax.rsqrt(mean_square + EPSILON) * gains[:, lanes]).astype(jnp.bfloat16)
        scores = (
            lax.dot_general(
                queries, keys_ref[:, lanes], (((1,), (1,)), ((), ())),
                preferred_element_type=jnp.float32,
            )
            * factor
        )
        weights = jnp.exp(scores) * live
        totals = jnp.sum(weights, axis=-1, keepdims=True)
        mixture = jnp.dot(
            weights.astype(jnp.bfloat16), values_ref[:, lanes], preferred_element_type=jnp.float32
        )
        mixed_ref[:, lanes] = (mixture / totals).astype(mixed_ref.dtype)
    o_ref[...] = jnp.dot(mixed_ref[...], wo_ref[...], preferred_element_type=jnp.float32).astype(
        o_ref.dtype
    )


def cross_partial(owner_cross, cross_wq, cross_q_gain, keys_own, values_own, length, cross_wo):
    token_total, model_width = owner_cross.shape
    group_width = cross_wq.shape[1]
    text = keys_own.shape[0]
    vmem = pl.BlockSpec(memory_space=pltpu.VMEM)
    return pl.pallas_call(
        _cross_kernel,
        in_specs=[pl.BlockSpec(memory_space=pltpu.SMEM)] + [vmem] * 6,
        out_specs=vmem,
        out_shape=jax.ShapeDtypeStruct((token_total, model_width), jnp.bfloat16),
        scratch_shapes=[pltpu.VMEM((token_total, group_width), jnp.bfloat16)],
        cost_estimate=pl.CostEstimate(
            flops=4 * token_total * model_width * group_width + 4 * token_total * text * group_width,
            bytes_accessed=4 * model_width * group_width + 4 * text * group_width
            + 4 * token_total * model_width,
            transcendentals=token_total * text * (group_width // HEAD_DIM),
        ),
    )(
        length,
        owner_cross,
        cross_wq,
        cross_q_gain.reshape(1, group_width),
        pltpu.with_memory_space_constraint(keys_own, pltpu.VMEM),
        pltpu.with_memory_space_constraint(values_own, pltpu.VMEM),
        cross_wo,
    )


def _qkv_kernel(x_ref, wq_ref, wk_ref, wv_ref, cos_ref, sin_ref, gain_ref, o_ref):
    block_in = x_ref[...]
    cosine = cos_ref[...]
    sine_signed = sin_ref[...]
    group_width = wq_ref.shape[1]
    for section, w_ref in enumerate((wq_ref, wk_ref, wv_ref)):
        projected = jnp.dot(block_in, w_ref[...], preferred_element_type=jnp.float32)
        if section < 2:
            gains = gain_ref[section : section + 1, :]
            parts = []
            for head in range(group_width // HEAD_DIM):
                lanes = slice(head * HEAD_DIM, (head + 1) * HEAD_DIM)
                piece = projected[:, lanes]
                mean_square = jnp.mean(piece * piece, axis=-1, keepdims=True)
                normed = piece * lax.rsqrt(mean_square + EPSILON) * gains[:, lanes]
                swapped = pltpu.roll(normed, HEAD_DIM // 2, 1)
                parts.append(normed * cosine + swapped * sine_signed)
            projected = jnp.concatenate(parts, axis=-1)
        o_ref[0, :, section * group_width : (section + 1) * group_width] = projected.astype(
            o_ref.dtype
        )


def pack_projected(block_in, cell_map, w_qkv, self_q_gain, self_k_gain, head_count):
    videos, per_video, model_width = block_in.shape
    rows = block_in.reshape(-1, model_width)
    token_total = rows.shape[0]
    group_width = model_width // head_count
    angles = rope_angles(cell_map).reshape(token_total, HEAD_DIM // 2)
    cosine = jnp.cos(angles)
    sine = jnp.sin(angles)
    cos_full = jnp.concatenate([cosine, cosine], axis=-1)
    sin_signed = jnp.concatenate([-sine, sine], axis=-1)
    gains = jnp.stack([self_q_gain, self_k_gain])
    whole = lambda g: (0, 0)
    packed = pl.pallas_call(
        _qkv_kernel,
        grid=(head_count,),
        in_specs=[
            pl.BlockSpec((token_total, model_width), whole),
            pl.BlockSpec((model_width, group_width), lambda g: (0, g)),
            pl.BlockSpec((model_width, group_width), lambda g: (0, head_count + g)),
            pl.BlockSpec((model_width, group_width), lambda g: (0, 2 * head_count + g)),
            pl.BlockSpec((token_total, HEAD_DIM), whole),
            pl.BlockSpec((token_total, HEAD_DIM), whole),
            pl.BlockSpec((2, group_width), lambda g: (0, g)),
        ],
        out_specs=pl.BlockSpec((1, token_total, 3 * group_width), lambda g: (g, 0, 0)),
        out_shape=jax.ShapeDtypeStruct((head_count, token_total, 3 * group_width), jnp.bfloat16),
        cost_estimate=pl.CostEstimate(
            flops=2 * token_total * model_width * 3 * model_width,
            bytes_accessed=2 * model_width * 3 * model_width + 4 * token_total * 3 * model_width,
            transcendentals=0,
        ),
    )(rows, w_qkv, w_qkv, w_qkv, cos_full, sin_signed, gains)
    return packed.reshape(head_count, videos, per_video, 3 * group_width)


def local(
    hidden,
    latent,
    cell_map,
    text_lengths,
    block_modulation,
    head_modulation,
    step_sizes,
    w_qkv,
    self_q_gain,
    self_k_gain,
    w_out,
    cross_gain,
    cross_wq,
    cross_q_gain,
    text_keys,
    text_values,
    cross_wo,
    head_w,
):
    head_count = lax.axis_size("head")
    tile_count = lax.axis_size("tile")
    videos, per_video, model_width = hidden.shape
    group_heads = HEADS // head_count
    group_width = group_heads * HEAD_DIM
    stream = hidden.astype(jnp.float32)
    block_shift = block_modulation[:, 0][:, None, :]
    block_scale = block_modulation[:, 1][:, None, :]
    block_gate = block_modulation[:, 2][:, None, :]
    block_in = (layer_norm(stream) * (1.0 + block_scale) + block_shift).astype(jnp.bfloat16)
    packed = pack_projected(block_in, cell_map, w_qkv, self_q_gain, self_k_gain, head_count)
    arrived = lax.all_to_all(
        packed.reshape(head_count * videos, 2, per_video * 3 * group_width // 2),
        ("head", "tile"),
        split_axis=0,
        concat_axis=0,
        tiled=True,
    )
    own_mixture = attend_self(arrived.reshape(-1, 3 * group_width), group_width)
    returned = lax.all_to_all(
        own_mixture.reshape(head_count * tile_count, 2, per_video * group_width // 2),
        ("head", "tile"),
        split_axis=0,
        concat_axis=0,
        tiled=True,
    )
    attended = (
        returned.reshape(head_count, videos, per_video, group_width)
        .transpose(1, 2, 0, 3)
        .reshape(videos * per_video, model_width)
    )
    self_update = jnp.dot(attended, w_out, preferred_element_type=jnp.float32).reshape(
        videos, per_video, model_width
    )
    after_self = stream + block_gate * self_update
    cross_in = (layer_norm(after_self) * cross_gain).astype(jnp.bfloat16)
    cross_rows = cross_in.reshape(videos, 2, per_video * model_width // 2)
    copies = jnp.broadcast_to(cross_rows[None], (head_count,) + cross_rows.shape).reshape(
        head_count * videos, 2, per_video * model_width // 2
    )
    owner_cross = lax.all_to_all(copies, ("head", "tile"), split_axis=0, concat_axis=0, tiled=True)
    owner_cross = owner_cross.reshape(-1, model_width)
    partial = cross_partial(
        owner_cross, cross_wq, cross_q_gain, text_keys[0], text_values[0], text_lengths, cross_wo
    )
    returned_partials = lax.all_to_all(
        partial.reshape(head_count * tile_count, 2, per_video * model_width // 2),
        ("head", "tile"),
        split_axis=0,
        concat_axis=0,
        tiled=True,
    ).reshape(head_count, videos, 2, per_video * model_width // 2)
    returned_cross = (
        jnp.sum(returned_partials.astype(jnp.float32), axis=0)
        .astype(jnp.bfloat16)
        .reshape(videos, per_video, model_width)
    )
    after_cross = after_self + returned_cross.astype(jnp.float32)
    hidden_next = after_cross.astype(jnp.bfloat16)
    head_shift = head_modulation[:, 0][:, None, :]
    head_scale = head_modulation[:, 1][:, None, :]
    head_in = (layer_norm(after_cross) * (1.0 + head_scale) + head_shift).astype(jnp.bfloat16)
    velocity = jnp.dot(
        head_in.reshape(-1, model_width), head_w, preferred_element_type=jnp.float32
    ).reshape(videos, per_video, -1)
    latent_next = latent + step_sizes[:, None, None] * velocity
    return (hidden_next, latent_next)


def solution(mesh):
    return jax.shard_map(
        local,
        mesh=mesh,
        in_specs=(
            P(None, ("head", "tile"), None),
            P(None, ("head", "tile"), None),
            P(None, ("head", "tile")),
            P("tile"),
            P(),
            P(),
            P(),
            P(),
            P(),
            P(),
            P(),
            P(),
            P(None, "head"),
            P("head"),
            P("tile", None, "head"),
            P("tile", None, "head"),
            P("head", None),
            P(),
        ),
        out_specs=(P(None, ("head", "tile"), None), P(None, ("head", "tile"), None)),
        check_vma=False,
    )
```

```python
import math

import jax
import jax.numpy as jnp
from jax import lax
from jax.experimental import pallas as pl
from jax.experimental.pallas import tpu as pltpu
from jax.sharding import PartitionSpec as P

HEADS = 12
HEAD_DIM = 128
GRID_H = 24
GRID_W = 8


EPSILON = 1e-06


def layer_norm(inputs):
    average = jnp.mean(inputs, axis=-1, keepdims=True)
    centred = inputs - average
    variance = jnp.mean(centred * centred, axis=-1, keepdims=True)
    return centred * lax.rsqrt(variance + EPSILON)


def head_norm(inputs, gain_table):
    mean_square = jnp.mean(inputs * inputs, axis=-1, keepdims=True)
    return inputs * lax.rsqrt(mean_square + EPSILON) * gain_table


def frequencies(pair_count):
    return jnp.power(10000.0, -jnp.arange(pair_count, dtype=jnp.float32) / pair_count)


def rope_angles(cell_ids):
    sixth_part = HEAD_DIM // 6
    time_pairs = HEAD_DIM // 2 - 2 * sixth_part
    plane_cells = GRID_H * GRID_W
    frame_index = (cell_ids // plane_cells).astype(jnp.float32)
    row_index = (cell_ids // GRID_W % GRID_H).astype(jnp.float32)
    column = (cell_ids % GRID_W).astype(jnp.float32)
    return jnp.concatenate(
        [
            frame_index[..., None] * frequencies(time_pairs),
            row_index[..., None] * frequencies(sixth_part),
            column[..., None] * frequencies(sixth_part),
        ],
        axis=-1,
    )


def rotate(inputs, angles):
    half_dim = inputs.shape[-1] // 2
    cosine = jnp.cos(angles)[..., None, :]
    sine_part = jnp.sin(angles)[..., None, :]
    lower_half = inputs[..., :half_dim]
    upper_half = inputs[..., half_dim:]
    return jnp.concatenate(
        [
            lower_half * cosine - upper_half * sine_part,
            lower_half * sine_part + upper_half * cosine,
        ],
        axis=-1,
    )


def _self_attention_kernel(x_ref, o_ref):
    group_width = o_ref.shape[1]
    factor = 1.0 / math.sqrt(HEAD_DIM)
    for head in range(group_width // HEAD_DIM):
        lanes = slice(head * HEAD_DIM, (head + 1) * HEAD_DIM)
        queries = x_ref[:, head * HEAD_DIM : (head + 1) * HEAD_DIM]
        keys = x_ref[:, group_width + head * HEAD_DIM : group_width + (head + 1) * HEAD_DIM]
        values = x_ref[:, 2 * group_width + head * HEAD_DIM : 2 * group_width + (head + 1) * HEAD_DIM]
        scores = (
            lax.dot_general(
                queries, keys, (((1,), (1,)), ((), ())), preferred_element_type=jnp.float32
            )
            * factor
        )
        weights = jnp.exp(scores)
        totals = jnp.sum(weights, axis=-1, keepdims=True)
        mixture = jnp.dot(
            weights.astype(jnp.bfloat16), values, preferred_element_type=jnp.float32
        )
        o_ref[:, lanes] = (mixture / totals).astype(o_ref.dtype)


def attend_self(arrived, group_width):
    token_total = arrived.shape[0]
    return pl.pallas_call(
        _self_attention_kernel,
        out_shape=jax.ShapeDtypeStruct((token_total, group_width), jnp.bfloat16),
        cost_estimate=pl.CostEstimate(
            flops=4 * token_total * token_total * group_width,
            bytes_accessed=2 * token_total * 4 * group_width,
            transcendentals=token_total * token_total * (group_width // HEAD_DIM),
        ),
    )(arrived)


def _cross_kernel(length_ref, x_ref, wq_ref, gain_ref, keys_ref, values_ref, wo_ref, o_ref, mixed_ref):
    factor = 1.0 / math.sqrt(HEAD_DIM)
    group_width = wq_ref.shape[1]
    text = keys_ref.shape[0]
    projected = jnp.dot(x_ref[...], wq_ref[...], preferred_element_type=jnp.float32)
    gains = gain_ref[...]
    live = (lax.broadcasted_iota(jnp.int32, (1, text), 1) < length_ref[0]).astype(jnp.float32)
    for head in range(group_width // HEAD_DIM):
        lanes = slice(head * HEAD_DIM, (head + 1) * HEAD_DIM)
        piece = projected[:, lanes]
        mean_square = jnp.mean(piece * piece, axis=-1, keepdims=True)
        queries = (piece * lax.rsqrt(mean_square + EPSILON) * gains[:, lanes]).astype(jnp.bfloat16)
        scores = (
            lax.dot_general(
                queries, keys_ref[:, lanes], (((1,), (1,)), ((), ())),
                preferred_element_type=jnp.float32,
            )
            * factor
        )
        weights = jnp.exp(scores) * live
        totals = jnp.sum(weights, axis=-1, keepdims=True)
        mixture = jnp.dot(
            weights.astype(jnp.bfloat16), values_ref[:, lanes], preferred_element_type=jnp.float32
        )
        mixed_ref[:, lanes] = (mixture / totals).astype(mixed_ref.dtype)
    o_ref[...] = jnp.dot(mixed_ref[...], wo_ref[...], preferred_element_type=jnp.float32).astype(
        o_ref.dtype
    )


def cross_partial(owner_cross, cross_wq, cross_q_gain, keys_own, values_own, length, cross_wo):
    token_total, model_width = owner_cross.shape
    group_width = cross_wq.shape[1]
    text = keys_own.shape[0]
    vmem = pl.BlockSpec(memory_space=pltpu.VMEM)
    return pl.pallas_call(
        _cross_kernel,
        in_specs=[pl.BlockSpec(memory_space=pltpu.SMEM)] + [vmem] * 6,
        out_specs=vmem,
        out_shape=jax.ShapeDtypeStruct((token_total, model_width), jnp.bfloat16),
        scratch_shapes=[pltpu.VMEM((token_total, group_width), jnp.bfloat16)],
        cost_estimate=pl.CostEstimate(
            flops=4 * token_total * model_width * group_width + 4 * token_total * text * group_width,
            bytes_accessed=4 * model_width * group_width + 4 * text * group_width
            + 4 * token_total * model_width,
            transcendentals=token_total * text * (group_width // HEAD_DIM),
        ),
    )(
        length,
        owner_cross,
        cross_wq,
        cross_q_gain.reshape(1, group_width),
        pltpu.with_memory_space_constraint(keys_own, pltpu.VMEM),
        pltpu.with_memory_space_constraint(values_own, pltpu.VMEM),
        pltpu.with_memory_space_constraint(cross_wo, pltpu.VMEM),
    )


def _qkv_kernel(x_ref, wq_ref, wk_ref, wv_ref, cos_ref, sin_ref, gain_ref, o_ref):
    block_in = x_ref[...]
    cosine = cos_ref[...]
    sine_signed = sin_ref[...]
    group_width = wq_ref.shape[1]
    for section, w_ref in enumerate((wq_ref, wk_ref, wv_ref)):
        projected = jnp.dot(block_in, w_ref[...], preferred_element_type=jnp.float32)
        if section < 2:
            gains = gain_ref[section : section + 1, :]
            parts = []
            for head in range(group_width // HEAD_DIM):
                lanes = slice(head * HEAD_DIM, (head + 1) * HEAD_DIM)
                piece = projected[:, lanes]
                mean_square = jnp.mean(piece * piece, axis=-1, keepdims=True)
                normed = piece * lax.rsqrt(mean_square + EPSILON) * gains[:, lanes]
                swapped = pltpu.roll(normed, HEAD_DIM // 2, 1)
                parts.append(normed * cosine + swapped * sine_signed)
            projected = jnp.concatenate(parts, axis=-1)
        o_ref[0, :, section * group_width : (section + 1) * group_width] = projected.astype(
            o_ref.dtype
        )


def pack_projected(block_in, cell_map, w_qkv, self_q_gain, self_k_gain, head_count):
    videos, per_video, model_width = block_in.shape
    rows = block_in.reshape(-1, model_width)
    token_total = rows.shape[0]
    group_width = model_width // head_count
    angles = rope_angles(cell_map).reshape(token_total, HEAD_DIM // 2)
    cosine = jnp.cos(angles)
    sine = jnp.sin(angles)
    cos_full = jnp.concatenate([cosine, cosine], axis=-1)
    sin_signed = jnp.concatenate([-sine, sine], axis=-1)
    gains = jnp.stack([self_q_gain, self_k_gain])
    whole = lambda g: (0, 0)
    packed = pl.pallas_call(
        _qkv_kernel,
        grid=(head_count,),
        in_specs=[
            pl.BlockSpec((token_total, model_width), whole),
            pl.BlockSpec((model_width, group_width), lambda g: (0, g)),
            pl.BlockSpec((model_width, group_width), lambda g: (0, head_count + g)),
            pl.BlockSpec((model_width, group_width), lambda g: (0, 2 * head_count + g)),
            pl.BlockSpec((token_total, HEAD_DIM), whole),
            pl.BlockSpec((token_total, HEAD_DIM), whole),
            pl.BlockSpec((2, group_width), lambda g: (0, g)),
        ],
        out_specs=pl.BlockSpec((1, token_total, 3 * group_width), lambda g: (g, 0, 0)),
        out_shape=jax.ShapeDtypeStruct((head_count, token_total, 3 * group_width), jnp.bfloat16),
        cost_estimate=pl.CostEstimate(
            flops=2 * token_total * model_width * 3 * model_width,
            bytes_accessed=2 * model_width * 3 * model_width + 4 * token_total * 3 * model_width,
            transcendentals=0,
        ),
    )(rows, w_qkv, w_qkv, w_qkv, cos_full, sin_signed, gains)
    return packed.reshape(head_count, videos, per_video, 3 * group_width)


def local(
    hidden,
    latent,
    cell_map,
    text_lengths,
    block_modulation,
    head_modulation,
    step_sizes,
    w_qkv,
    self_q_gain,
    self_k_gain,
    w_out,
    cross_gain,
    cross_wq,
    cross_q_gain,
    text_keys,
    text_values,
    cross_wo,
    head_w,
):
    head_count = lax.axis_size("head")
    tile_count = lax.axis_size("tile")
    videos, per_video, model_width = hidden.shape
    group_heads = HEADS // head_count
    group_width = group_heads * HEAD_DIM
    stream = hidden.astype(jnp.float32)
    block_shift = block_modulation[:, 0][:, None, :]
    block_scale = block_modulation[:, 1][:, None, :]
    block_gate = block_modulation[:, 2][:, None, :]
    block_in = (layer_norm(stream) * (1.0 + block_scale) + block_shift).astype(jnp.bfloat16)
    packed = pack_projected(block_in, cell_map, w_qkv, self_q_gain, self_k_gain, head_count)
    arrived = lax.all_to_all(
        packed.reshape(head_count * videos, 2, per_video * 3 * group_width // 2),
        ("head", "tile"),
        split_axis=0,
        concat_axis=0,
        tiled=True,
    )
    own_mixture = attend_self(arrived.reshape(-1, 3 * group_width), group_width)
    returned = lax.all_to_all(
        own_mixture.reshape(head_count * tile_count, 2, per_video * group_width // 2),
        ("head", "tile"),
        split_axis=0,
        concat_axis=0,
        tiled=True,
    )
    attended = (
        returned.reshape(head_count, videos, per_video, group_width)
        .transpose(1, 2, 0, 3)
        .reshape(videos * per_video, model_width)
    )
    self_update = jnp.dot(attended, w_out, preferred_element_type=jnp.float32).reshape(
        videos, per_video, model_width
    )
    after_self = stream + block_gate * self_update
    cross_in = (layer_norm(after_self) * cross_gain).astype(jnp.bfloat16)
    cross_rows = cross_in.reshape(videos, 2, per_video * model_width // 2)
    copies = jnp.broadcast_to(cross_rows[None], (head_count,) + cross_rows.shape).reshape(
        head_count * videos, 2, per_video * model_width // 2
    )
    owner_cross = lax.all_to_all(copies, ("head", "tile"), split_axis=0, concat_axis=0, tiled=True)
    owner_cross = owner_cross.reshape(-1, model_width)
    partial = cross_partial(
        owner_cross, cross_wq, cross_q_gain, text_keys[0], text_values[0], text_lengths, cross_wo
    )
    returned_partials = lax.all_to_all(
        partial.reshape(head_count * tile_count, 2, per_video * model_width // 2),
        ("head", "tile"),
        split_axis=0,
        concat_axis=0,
        tiled=True,
    ).reshape(head_count, videos, 2, per_video * model_width // 2)
    returned_cross = (
        jnp.sum(returned_partials.astype(jnp.float32), axis=0)
        .astype(jnp.bfloat16)
        .reshape(videos, per_video, model_width)
    )
    after_cross = after_self + returned_cross.astype(jnp.float32)
    hidden_next = after_cross.astype(jnp.bfloat16)
    head_shift = head_modulation[:, 0][:, None, :]
    head_scale = head_modulation[:, 1][:, None, :]
    head_in = (layer_norm(after_cross) * (1.0 + head_scale) + head_shift).astype(jnp.bfloat16)
    velocity = jnp.dot(
        head_in.reshape(-1, model_width), head_w, preferred_element_type=jnp.float32
    ).reshape(videos, per_video, -1)
    latent_next = latent + step_sizes[:, None, None] * velocity
    return (hidden_next, latent_next)


def solution(mesh):
    return jax.shard_map(
        local,
        mesh=mesh,
        in_specs=(
            P(None, ("head", "tile"), None),
            P(None, ("head", "tile"), None),
            P(None, ("head", "tile")),
            P("tile"),
            P(),
            P(),
            P(),
            P(),
            P(),
            P(),
            P(),
            P(),
            P(None, "head"),
            P("head"),
            P("tile", None, "head"),
            P("tile", None, "head"),
            P("head", None),
            P(),
        ),
        out_specs=(P(None, ("head", "tile"), None), P(None, ("head", "tile"), None)),
        check_vma=False,
    )
```
